768 devices in a mesh: bx: 12 (over x, z_hi), by: 64 (over z_lo, y, core).
Axes of the slice: x: 4, y: 8, z: 12 (z_hi: 3, z_lo: 4; z = z_hi * 4 + z_lo), core: 2. Of those that a mesh axis runs over, the one named last changes fastest.
Arguments:
- cotangent: float32 [36, 384, 384], P('bx', 'by'), may hold values from -45 to 45
- pointwise: bfloat16 [7, 4, 4, 4, 12, 128, 128], P(None, None, None, None, 'bx', 'by'), may hold values from -1.25 to 8, as said below
Outputs:
- adjoint: float32 [36, 384, 384], P('bx', 'by')
- residual: float32 [36, 384, 384], P('bx', 'by')
The draws below stay inside these ranges and needn't reach their ends.
Inputs may be any that keep to these rules, and one draw needn't show every extreme that they name: `pointwise`: entry 0 of every point is positive; entries 1 to 6 form a symmetric positive definite tensor whose off-diagonal entries are at most 0.31 times the geometric mean of the two matching diagonal entries.
All inputs are finite; a program needn't handle non-finite values.
Results may differ from the reference program's by a relative error of at most 0.0003.
Values sent between devices are 32-bit elements; how exact they have to be, the bound alone decides.
No kernel may reach another device: no remote copies, remote signals or barrier semaphores. Data moves between devices by JAX's collectives and lax.ppermute only.
A program may use at most 32 MiB of HBM per device.

```python
import math
import jax
import jax.numpy as jnp
import numpy as np
from jax import lax

EZ = 128
ITERS = 2
NEX = 12
NEY = 128
NX = 36
NY = 384
NZ = 384


def draw_pointwise(key, part):
    extent = (4, 4, 4, NEX, NEY, EZ)
    subkeys = jax.random.split(key, 7)
    reaction = jnp.exp(jax.random.uniform(subkeys[0], extent, jnp.float32, math.log(0.5), math.log(8.0)))
    tensor_xx = jnp.exp(jax.random.uniform(subkeys[1], extent, jnp.float32, math.log(0.25), math.log(4.0)))
    tensor_yy = jnp.exp(jax.random.uniform(subkeys[2], extent, jnp.float32, math.log(0.25), math.log(4.0)))
    tensor_zz = jnp.exp(jax.random.uniform(subkeys[3], extent, jnp.float32, math.log(0.25), math.log(4.0)))
    tensor_xy = 0.3 * jax.random.uniform(subkeys[4], extent, jnp.float32, -1.0, 1.0) * jnp.sqrt(tensor_xx * tensor_yy)
    tensor_xz = 0.3 * jax.random.uniform(subkeys[5], extent, jnp.float32, -1.0, 1.0) * jnp.sqrt(tensor_xx * tensor_zz)
    tensor_yz = 0.3 * jax.random.uniform(subkeys[6], extent, jnp.float32, -1.0, 1.0) * jnp.sqrt(tensor_yy * tensor_zz)
    stacked = jnp.stack([reaction, tensor_xx, tensor_yy, tensor_zz, tensor_xy, tensor_xz, tensor_yz], 0)
    return stacked.astype(jnp.bfloat16)


def draw_cotangent(key, part):
    extent = (NX, NY, NZ)
    across_x = jax.lax.broadcasted_iota(jnp.float32, extent, 0) / NX
    across_y = jax.lax.broadcasted_iota(jnp.float32, extent, 1) / NY
    slope_up = (1.0 + 2.0 * across_x) * (1.0 + 2.0 * across_y)
    noise = jax.random.truncated_normal(key, -4.5, 4.5, extent, jnp.float32)
    return noise * slope_up


def setup_inputs(seed: int = 0) -> dict:
    splits = jax.random.split(jax.random.key(seed), 3)
    return {
        "cotangent": draw_cotangent(jax.random.fold_in(splits[2], 71), 0),
        "pointwise": draw_pointwise(jax.random.fold_in(splits[2], 71), 0),
    }


EINSUM_FORMS = ('pa,abcxyz->pbcxyz', 'pb,abcxyz->apcxyz', 'pc,abcxyz->abpxyz')

def gauss_tables():
    inner_point = math.sqrt(3.0 / 7.0 - 2.0 / 7.0 * math.sqrt(6.0 / 5.0))
    outer_point = math.sqrt(3.0 / 7.0 + 2.0 / 7.0 * math.sqrt(6.0 / 5.0))
    points = [-outer_point, -inner_point, inner_point, outer_point]
    lobatto = [-1.0, -1.0 / math.sqrt(5.0), 1.0 / math.sqrt(5.0), 1.0]
    values = np.zeros((4, 4))
    slopes = np.zeros((4, 4))
    for a in range(4):
        others = [lobatto[k] for k in range(4) if k != a]
        scaling = (lobatto[a] - others[0]) * (lobatto[a] - others[1]) * (lobatto[a] - others[2])
        for q in range(4):
            sample = points[q]
            values[q, a] = (sample - others[0]) * (sample - others[1]) * (sample - others[2]) / scaling
            slopes[q, a] = ((sample - others[1]) * (sample - others[2]) + (sample - others[0]) * (sample - others[2]) + (sample - others[0]) * (sample - others[1])) / scaling
    return (values, slopes)

def apply_table(weights_1d, operand, stack_pos):
    return jnp.einsum(EINSUM_FORMS[stack_pos], weights_1d, operand, precision=lax.Precision.HIGHEST)

def split_axis(dof_field, axis_pos, stack_pos):
    elem_count = (dof_field.shape[axis_pos] - 1) // 3
    widths = [(0, 0)] * dof_field.ndim
    widths[axis_pos] = (0, 2)
    padded = jnp.pad(dof_field, widths)
    shaped = padded.reshape(dof_field.shape[:axis_pos] + (elem_count + 1, 3) + dof_field.shape[axis_pos + 1:])
    lower_rows = lax.slice_in_dim(shaped, 0, elem_count, axis=axis_pos)
    upper_rows = lax.slice_in_dim(shaped, 1, elem_count + 1, axis=axis_pos)
    pieces = [lax.index_in_dim(lower_rows, k, axis_pos + 1, keepdims=False) for k in range(3)]
    pieces.append(lax.index_in_dim(upper_rows, 0, axis_pos + 1, keepdims=False))
    return jnp.stack(pieces, stack_pos)

def merge_axis(parts, axis_pos, stack_pos):
    pieces = [lax.index_in_dim(parts, k, stack_pos, keepdims=False) for k in range(4)]
    target = axis_pos - 1
    extent = pieces[0].shape
    elem_count = extent[target]
    ending = [(0, 0)] * len(extent)
    ending[target] = (0, 1)
    leading = [(0, 0)] * len(extent)
    leading[target] = (1, 0)
    head_piece = jnp.pad(pieces[0], ending) + jnp.pad(pieces[3], leading)
    stacked = jnp.stack([head_piece, jnp.pad(pieces[1], ending), jnp.pad(pieces[2], ending)], target + 1)
    merged = stacked.reshape(extent[:target] + (3 * (elem_count + 1),) + extent[target + 1:])
    return lax.slice_in_dim(merged, 0, 3 * elem_count + 1, axis=target)

def element_action(elements, pointwise):
    table_pair = gauss_tables()
    values = jnp.asarray(table_pair[0], jnp.float32)
    slopes = jnp.asarray(table_pair[1], jnp.float32)
    coeffs = pointwise.astype(jnp.float32)
    x_value = apply_table(values, elements, 0)
    x_slope = apply_table(slopes, elements, 0)
    value_value = apply_table(values, x_value, 1)
    value_slope = apply_table(slopes, x_value, 1)
    slope_value = apply_table(values, x_slope, 1)
    point_value = apply_table(values, value_value, 2)
    grad_z = apply_table(slopes, value_value, 2)
    grad_y = apply_table(values, value_slope, 2)
    grad_x = apply_table(values, slope_value, 2)
    flux_x = coeffs[1] * grad_x + coeffs[4] * grad_y + coeffs[5] * grad_z
    flux_y = coeffs[4] * grad_x + coeffs[2] * grad_y + coeffs[6] * grad_z
    flux_z = coeffs[5] * grad_x + coeffs[6] * grad_y + coeffs[3] * grad_z
    mass_term = coeffs[0] * point_value
    back_plain = apply_table(values.T, mass_term, 2) + apply_table(slopes.T, flux_z, 2)
    back_fluxx = apply_table(values.T, flux_x, 2)
    back_fluxy = apply_table(values.T, flux_y, 2)
    near_sum = apply_table(values.T, back_plain, 1) + apply_table(slopes.T, back_fluxy, 1)
    far_sum = apply_table(values.T, back_fluxx, 1)
    return apply_table(values.T, near_sum, 0) + apply_table(slopes.T, far_sum, 0)

def diagonal_action(pointwise):
    table_pair = gauss_tables()
    values = jnp.asarray(table_pair[0], jnp.float32)
    slopes = jnp.asarray(table_pair[1], jnp.float32)
    coeffs = pointwise.astype(jnp.float32)
    square_v = values * values
    square_s = slopes * slopes
    mixed_vs = values * slopes

    def triple(table_x, table_y, table_z, term):
        return apply_table(table_x.T, apply_table(table_y.T, apply_table(table_z.T, term, 2), 1), 0)
    running_total = triple(square_v, square_v, square_v, coeffs[0])
    running_total = running_total + triple(square_s, square_v, square_v, coeffs[1])
    running_total = running_total + triple(square_v, square_s, square_v, coeffs[2])
    running_total = running_total + triple(square_v, square_v, square_s, coeffs[3])
    running_total = running_total + 2.0 * triple(mixed_vs, mixed_vs, square_v, coeffs[4])
    running_total = running_total + 2.0 * triple(mixed_vs, square_v, mixed_vs, coeffs[5])
    running_total = running_total + 2.0 * triple(square_v, mixed_vs, mixed_vs, coeffs[6])
    return running_total

def to_dofs(parts):
    return merge_axis(merge_axis(merge_axis(parts, 5, 2), 3, 1), 1, 0)

def element_block(dof_block, pointwise):
    elements = split_axis(split_axis(split_axis(dof_block, 0, 0), 2, 1), 4, 2)
    return to_dofs(element_action(elements, pointwise))

def slab_sum(slab_term):
    running_total = jnp.zeros((NX + 1, NY + 1, NZ + 1), jnp.float32)

    def advance(running_total, layer_index):
        start_row = 3 * layer_index
        current = lax.dynamic_slice_in_dim(running_total, start_row, 4, 0)
        return (lax.dynamic_update_slice_in_dim(running_total, current + slab_term(layer_index), start_row, 0), None)
    running_total, unused = lax.scan(advance, running_total, jnp.arange(NEX, dtype=jnp.int32))
    return running_total[:NX, :NY, :NZ]

def apply_global(dof_field, pointwise):
    padded = jnp.pad(dof_field, ((0, 1), (0, 1), (0, 1)))

    def slab_term(layer_index):
        dof_block = lax.dynamic_slice_in_dim(padded, 3 * layer_index, 4, 0)
        local_coeffs = lax.dynamic_slice_in_dim(pointwise, layer_index, 1, 4)
        return element_block(dof_block, local_coeffs)
    return slab_sum(slab_term)

def diagonal_global(pointwise):

    def slab_term(layer_index):
        local_coeffs = lax.dynamic_slice_in_dim(pointwise, layer_index, 1, 4)
        return to_dofs(diagonal_action(local_coeffs))
    return slab_sum(slab_term)

def reference(cotangent, pointwise):
    extent = cotangent.shape
    place_x = lax.broadcasted_iota(jnp.int32, extent, 0)
    place_y = lax.broadcasted_iota(jnp.int32, extent, 1)
    place_z = lax.broadcasted_iota(jnp.int32, extent, 2)
    interior = jnp.where((place_x > 0) & (place_y > 0) & (place_z > 0), 1.0, 0.0).astype(jnp.float32)
    diagonal = diagonal_global(pointwise)
    adjoint = jnp.zeros(extent, jnp.float32)
    residual = cotangent * interior
    precond = residual / diagonal
    direction = precond
    rz_now = jnp.sum(residual * precond)
    for sweep in range(ITERS):
        image = apply_global(direction, pointwise) * interior
        alpha = rz_now / jnp.sum(direction * image)
        adjoint = adjoint + alpha * direction
        residual = residual - alpha * image
        if sweep + 1 < ITERS:
            precond = residual / diagonal
            fresh = jnp.sum(residual * precond)
            direction = precond + fresh / rz_now * direction
            rz_now = fresh
    return (adjoint, residual)
```

```python
import math

import jax
import jax.numpy as jnp
import numpy as np
from jax import lax
from jax.sharding import Mesh
from jax.sharding import PartitionSpec as P

ITERS = 2
BX = ("bx_0", "bx_1")
BY = ("by_0", "by_1", "by_2")
BX_BY = ("bx_0", "bx_1", "by_0", "by_1", "by_2")


EINSUM_FORMS = ("pa,abcxyz->pbcxyz", "pb,abcxyz->apcxyz", "pc,abcxyz->abpxyz")


def shifted(value, axis, steps):
    count = lax.axis_size(axis)
    initial, last = (max(0, -steps), min(count, count - steps))
    return lax.ppermute(value, axis, [(source, source + steps) for source in range(initial, last)])


def over_axes(value, axes):
    for axis in axes:
        value = lax.psum(value, axis)
    return value


def gauss_tables():
    inner_point = math.sqrt(3.0 / 7.0 - 2.0 / 7.0 * math.sqrt(6.0 / 5.0))
    outer_point = math.sqrt(3.0 / 7.0 + 2.0 / 7.0 * math.sqrt(6.0 / 5.0))
    points = [-outer_point, -inner_point, inner_point, outer_point]
    lobatto = [-1.0, -1.0 / math.sqrt(5.0), 1.0 / math.sqrt(5.0), 1.0]
    values = np.zeros((4, 4))
    slopes = np.zeros((4, 4))
    for a in range(4):
        others = [lobatto[k] for k in range(4) if k != a]
        scaling = (lobatto[a] - others[0]) * (lobatto[a] - others[1]) * (lobatto[a] - others[2])
        for q in range(4):
            sample = points[q]
            values[q, a] = (
                (sample - others[0]) * (sample - others[1]) * (sample - others[2]) / scaling
            )
            slopes[q, a] = (
                (sample - others[1]) * (sample - others[2])
                + (sample - others[0]) * (sample - others[2])
                + (sample - others[0]) * (sample - others[1])
            ) / scaling
    return (values, slopes)


def apply_table(weights_1d, operand, stack_pos):
    return jnp.einsum(EINSUM_FORMS[stack_pos], weights_1d, operand, precision=lax.Precision.HIGHEST)


def split_axis(dof_field, axis_pos, stack_pos):
    elem_count = (dof_field.shape[axis_pos] - 1) // 3
    widths = [(0, 0)] * dof_field.ndim
    widths[axis_pos] = (0, 2)
    padded = jnp.pad(dof_field, widths)
    shaped = padded.reshape(
        dof_field.shape[:axis_pos] + (elem_count + 1, 3) + dof_field.shape[axis_pos + 1 :]
    )
    lower_rows = lax.slice_in_dim(shaped, 0, elem_count, axis=axis_pos)
    upper_rows = lax.slice_in_dim(shaped, 1, elem_count + 1, axis=axis_pos)
    pieces = [lax.index_in_dim(lower_rows, k, axis_pos + 1, keepdims=False) for k in range(3)]
    pieces.append(lax.index_in_dim(upper_rows, 0, axis_pos + 1, keepdims=False))
    return jnp.stack(pieces, stack_pos)


def merge_axis(parts, axis_pos, stack_pos):
    pieces = [lax.index_in_dim(parts, k, stack_pos, keepdims=False) for k in range(4)]
    target = axis_pos - 1
    extent = pieces[0].shape
    elem_count = extent[target]
    ending = [(0, 0)] * len(extent)
    ending[target] = (0, 1)
    leading = [(0, 0)] * len(extent)
    leading[target] = (1, 0)
    head_piece = jnp.pad(pieces[0], ending) + jnp.pad(pieces[3], leading)
    stacked = jnp.stack(
        [head_piece, jnp.pad(pieces[1], ending), jnp.pad(pieces[2], ending)], target + 1
    )
    merged = stacked.reshape(extent[:target] + (3 * (elem_count + 1),) + extent[target + 1 :])
    return lax.slice_in_dim(merged, 0, 3 * elem_count + 1, axis=target)


def element_action(elements, pointwise):
    table_pair = gauss_tables()
    values = jnp.asarray(table_pair[0], jnp.float32)
    slopes = jnp.asarray(table_pair[1], jnp.float32)
    coeffs = pointwise.astype(jnp.float32)
    x_value = apply_table(values, elements, 0)
    x_slope = apply_table(slopes, elements, 0)
    value_value = apply_table(values, x_value, 1)
    value_slope = apply_table(slopes, x_value, 1)
    slope_value = apply_table(values, x_slope, 1)
    point_value = apply_table(values, value_value, 2)
    grad_z = apply_table(slopes, value_value, 2)
    grad_y = apply_table(values, value_slope, 2)
    grad_x = apply_table(values, slope_value, 2)
    flux_x = coeffs[1] * grad_x + coeffs[4] * grad_y + coeffs[5] * grad_z
    flux_y = coeffs[4] * grad_x + coeffs[2] * grad_y + coeffs[6] * grad_z
    flux_z = coeffs[5] * grad_x + coeffs[6] * grad_y + coeffs[3] * grad_z
    mass_term = coeffs[0] * point_value
    back_plain = apply_table(values.T, mass_term, 2) + apply_table(slopes.T, flux_z, 2)
    back_fluxx = apply_table(values.T, flux_x, 2)
    back_fluxy = apply_table(values.T, flux_y, 2)
    near_sum = apply_table(values.T, back_plain, 1) + apply_table(slopes.T, back_fluxy, 1)
    far_sum = apply_table(values.T, back_fluxx, 1)
    return apply_table(values.T, near_sum, 0) + apply_table(slopes.T, far_sum, 0)


def diagonal_action(pointwise):
    table_pair = gauss_tables()
    values = jnp.asarray(table_pair[0], jnp.float32)
    slopes = jnp.asarray(table_pair[1], jnp.float32)
    coeffs = pointwise.astype(jnp.float32)
    square_v = values * values
    square_s = slopes * slopes
    mixed_vs = values * slopes

    def triple(table_x, table_y, table_z, term):
        return apply_table(table_x.T, apply_table(table_y.T, apply_table(table_z.T, term, 2), 1), 0)

    running_total = triple(square_v, square_v, square_v, coeffs[0])
    running_total = running_total + triple(square_s, square_v, square_v, coeffs[1])
    running_total = running_total + triple(square_v, square_s, square_v, coeffs[2])
    running_total = running_total + triple(square_v, square_v, square_s, coeffs[3])
    running_total = running_total + 2.0 * triple(mixed_vs, mixed_vs, square_v, coeffs[4])
    running_total = running_total + 2.0 * triple(mixed_vs, square_v, mixed_vs, coeffs[5])
    running_total = running_total + 2.0 * triple(square_v, mixed_vs, mixed_vs, coeffs[6])
    return running_total


def to_dofs(parts):
    return merge_axis(merge_axis(merge_axis(parts, 5, 2), 3, 1), 1, 0)


def element_block(dof_block, pointwise):
    elements = split_axis(split_axis(split_axis(dof_block, 0, 0), 2, 1), 4, 2)
    return to_dofs(element_action(elements, pointwise))


def upper_x(plane):
    return shifted(plane, BX, -1)


def upper_y(plane):
    return shifted(plane, BY, -1)


def lower_x(plane):
    return shifted(plane, BX, 1)


def lower_y(plane):
    return shifted(plane, BY, 1)


def global_sums(terms):
    summed = lax.psum(jnp.stack(terms), BX_BY)
    return (summed[0], summed[1])


def widen(dof_field):
    widened = jnp.concatenate([dof_field, upper_x(dof_field[0:1])], 0)
    widened = jnp.concatenate([widened, upper_y(widened[:, 0:1])], 1)
    return widened


def pad_top(dof_field):
    return jnp.pad(dof_field, ((0, 0), (0, 0), (0, 1)))


def collect(contributions, rows_x, rows_y, rows_z):
    summed = contributions[:, :, :rows_z]
    arrived = lower_y(summed[:, rows_y:])
    summed = jnp.concatenate([summed[:, 0:1] + arrived, summed[:, 1:rows_y]], 1)
    arrived = lower_x(summed[rows_x:])
    summed = jnp.concatenate([summed[0:1] + arrived, summed[1:rows_x]], 0)
    return summed


def shards(cotangent, pointwise):
    rows_x, rows_y, rows_z = cotangent.shape
    total_x = rows_x * lax.axis_size(BX)
    total_y = rows_y * lax.axis_size(BY)
    extent = cotangent.shape
    place_x = lax.broadcasted_iota(jnp.int32, extent, 0) + lax.axis_index(BX) * rows_x
    place_y = lax.broadcasted_iota(jnp.int32, extent, 1) + lax.axis_index(BY) * rows_y
    place_z = lax.broadcasted_iota(jnp.int32, extent, 2)
    inside = (
        (place_x > 0) & (place_y > 0) & (place_z > 0) & (place_x < total_x) & (place_y < total_y)
    )
    interior = jnp.where(inside, 1.0, 0.0).astype(jnp.float32)
    diagonal = collect(to_dofs(diagonal_action(pointwise)), rows_x, rows_y, rows_z)

    def operator(dof_field):
        return (
            collect(element_block(pad_top(widen(dof_field)), pointwise), rows_x, rows_y, rows_z)
            * interior
        )

    def local_dot(left, right):
        return jnp.sum(left * right)

    adjoint = jnp.zeros(cotangent.shape, jnp.float32)
    residual = cotangent * interior
    precond = residual / diagonal
    image = operator(precond)
    rz_now, curvature = global_sums((local_dot(residual, precond), local_dot(precond, image)))
    alpha = rz_now / curvature
    direction = precond
    direction_image = image
    for sweep in range(ITERS):
        adjoint = adjoint + alpha * direction
        residual = residual - alpha * direction_image
        if sweep + 1 < ITERS:
            precond = residual / diagonal
            image = operator(precond)
            fresh, curvature = global_sums(
                (local_dot(residual, precond), local_dot(precond, image))
            )
            ratio = fresh / rz_now
            alpha = fresh / (curvature - ratio * fresh / alpha)
            direction = precond + ratio * direction
            direction_image = image + ratio * direction_image
            rz_now = fresh
    return (adjoint, residual)


def solution(mesh):
    split = Mesh(mesh.devices.reshape(4, 3, 4, 8, 2), ("bx_0", "bx_1", "by_0", "by_1", "by_2"))
    in_specs = (P(BX, BY, None), P(None, None, None, None, BX, BY, None))
    out_specs = (P(BX, BY, None), P(BX, BY, None))
    return jax.shard_map(
        shards, mesh=split, in_specs=in_specs, out_specs=out_specs, check_vma=False
    )
```

```python
import math

import jax
import jax.numpy as jnp
import numpy as np
from jax import lax
from jax.sharding import Mesh
from jax.sharding import PartitionSpec as P

ITERS = 2
BX = ("bx_0", "bx_1")
BY = ("by_0", "by_1", "by_2")
BX_BY = ("bx_0", "bx_1", "by_0", "by_1", "by_2")


EINSUM_FORMS = ("pa,abcxyz->pbcxyz", "pb,abcxyz->apcxyz", "pc,abcxyz->abpxyz")


def shifted(value, axis, steps):
    count = lax.axis_size(axis)
    initial, last = (max(0, -steps), min(count, count - steps))
    return lax.ppermute(value, axis, [(source, source + steps) for source in range(initial, last)])


def over_axes(value, axes):
    for axis in axes:
        value = lax.psum(value, axis)
    return value


def gauss_tables():
    inner_point = math.sqrt(3.0 / 7.0 - 2.0 / 7.0 * math.sqrt(6.0 / 5.0))
    outer_point = math.sqrt(3.0 / 7.0 + 2.0 / 7.0 * math.sqrt(6.0 / 5.0))
    points = [-outer_point, -inner_point, inner_point, outer_point]
    lobatto = [-1.0, -1.0 / math.sqrt(5.0), 1.0 / math.sqrt(5.0), 1.0]
    values = np.zeros((4, 4))
    slopes = np.zeros((4, 4))
    for a in range(4):
        others = [lobatto[k] for k in range(4) if k != a]
        scaling = (lobatto[a] - others[0]) * (lobatto[a] - others[1]) * (lobatto[a] - others[2])
        for q in range(4):
            sample = points[q]
            values[q, a] = (
                (sample - others[0]) * (sample - others[1]) * (sample - others[2]) / scaling
            )
            slopes[q, a] = (
                (sample - others[1]) * (sample - others[2])
                + (sample - others[0]) * (sample - others[2])
                + (sample - others[0]) * (sample - others[1])
            ) / scaling
    return (values, slopes)


def apply_table(weights_1d, operand, stack_pos):
    return jnp.einsum(EINSUM_FORMS[stack_pos], weights_1d, operand, precision=lax.Precision.HIGHEST)


def split_axis(dof_field, axis_pos, stack_pos):
    elem_count = (dof_field.shape[axis_pos] - 1) // 3
    widths = [(0, 0)] * dof_field.ndim
    widths[axis_pos] = (0, 2)
    padded = jnp.pad(dof_field, widths)
    shaped = padded.reshape(
        dof_field.shape[:axis_pos] + (elem_count + 1, 3) + dof_field.shape[axis_pos + 1 :]
    )
    lower_rows = lax.slice_in_dim(shaped, 0, elem_count, axis=axis_pos)
    upper_rows = lax.slice_in_dim(shaped, 1, elem_count + 1, axis=axis_pos)
    pieces = [lax.index_in_dim(lower_rows, k, axis_pos + 1, keepdims=False) for k in range(3)]
    pieces.append(lax.index_in_dim(upper_rows, 0, axis_pos + 1, keepdims=False))
    return jnp.stack(pieces, stack_pos)


def merge_axis(parts, axis_pos, stack_pos):
    pieces = [lax.index_in_dim(parts, k, stack_pos, keepdims=False) for k in range(4)]
    target = axis_pos - 1
    extent = pieces[0].shape
    elem_count = extent[target]
    ending = [(0, 0)] * len(extent)
    ending[target] = (0, 1)
    leading = [(0, 0)] * len(extent)
    leading[target] = (1, 0)
    head_piece = jnp.pad(pieces[0], ending) + jnp.pad(pieces[3], leading)
    stacked = jnp.stack(
        [head_piece, jnp.pad(pieces[1], ending), jnp.pad(pieces[2], ending)], target + 1
    )
    merged = stacked.reshape(extent[:target] + (3 * (elem_count + 1),) + extent[target + 1 :])
    return lax.slice_in_dim(merged, 0, 3 * elem_count + 1, axis=target)


def element_action(elements, pointwise):
    table_pair = gauss_tables()
    values = jnp.asarray(table_pair[0], jnp.float32)
    slopes = jnp.asarray(table_pair[1], jnp.float32)
    coeffs = pointwise.astype(jnp.float32)
    x_value = apply_table(values, elements, 0)
    x_slope = apply_table(slopes, elements, 0)
    value_value = apply_table(values, x_value, 1)
    value_slope = apply_table(slopes, x_value, 1)
    slope_value = apply_table(values, x_slope, 1)
    point_value = apply_table(values, value_value, 2)
    grad_z = apply_table(slopes, value_value, 2)
    grad_y = apply_table(values, value_slope, 2)
    grad_x = apply_table(values, slope_value, 2)
    flux_x = coeffs[1] * grad_x + coeffs[4] * grad_y + coeffs[5] * grad_z
    flux_y = coeffs[4] * grad_x + coeffs[2] * grad_y + coeffs[6] * grad_z
    flux_z = coeffs[5] * grad_x + coeffs[6] * grad_y + coeffs[3] * grad_z
    mass_term = coeffs[0] * point_value
    back_plain = apply_table(values.T, mass_term, 2) + apply_table(slopes.T, flux_z, 2)
    back_fluxx = apply_table(values.T, flux_x, 2)
    back_fluxy = apply_table(values.T, flux_y, 2)
    near_sum = apply_table(values.T, back_plain, 1) + apply_table(slopes.T, back_fluxy, 1)
    far_sum = apply_table(values.T, back_fluxx, 1)
    return apply_table(values.T, near_sum, 0) + apply_table(slopes.T, far_sum, 0)


def diagonal_action(pointwise):
    table_pair = gauss_tables()
    values = jnp.asarray(table_pair[0], jnp.float32)
    slopes = jnp.asarray(table_pair[1], jnp.float32)
    coeffs = pointwise.astype(jnp.float32)
    square_v = values * values
    square_s = slopes * slopes
    mixed_vs = values * slopes

    def triple(table_x, table_y, table_z, term):
        return apply_table(table_x.T, apply_table(table_y.T, apply_table(table_z.T, term, 2), 1), 0)

    running_total = triple(square_v, square_v, square_v, coeffs[0])
    running_total = running_total + triple(square_s, square_v, square_v, coeffs[1])
    running_total = running_total + triple(square_v, square_s, square_v, coeffs[2])
    running_total = running_total + triple(square_v, square_v, square_s, coeffs[3])
    running_total = running_total + 2.0 * triple(mixed_vs, mixed_vs, square_v, coeffs[4])
    running_total = running_total + 2.0 * triple(mixed_vs, square_v, mixed_vs, coeffs[5])
    running_total = running_total + 2.0 * triple(square_v, mixed_vs, mixed_vs, coeffs[6])
    return running_total


def to_dofs(parts):
    return merge_axis(merge_axis(merge_axis(parts, 5, 2), 3, 1), 1, 0)


def element_block(dof_block, pointwise):
    elements = split_axis(split_axis(split_axis(dof_block, 0, 0), 2, 1), 4, 2)
    return to_dofs(element_action(elements, pointwise))


def upper_x(plane):
    return shifted(plane, BX, -1)


def upper_y(plane):
    return shifted(plane, BY, -1)


def lower_x(plane):
    return shifted(plane, BX, 1)


def lower_y(plane):
    return shifted(plane, BY, 1)


def global_sums(terms):
    return (over_axes(terms[0], BX_BY), over_axes(terms[1], BX_BY))


def widen(dof_field):
    widened = jnp.concatenate([dof_field, upper_x(dof_field[0:1])], 0)
    widened = jnp.concatenate([widened, upper_y(widened[:, 0:1])], 1)
    return widened


def pad_top(dof_field):
    return jnp.pad(dof_field, ((0, 0), (0, 0), (0, 1)))


def collect(contributions, rows_x, rows_y, rows_z):
    summed = contributions[:, :, :rows_z]
    arrived = lower_y(summed[:, rows_y:])
    summed = jnp.concatenate([summed[:, 0:1] + arrived, summed[:, 1:rows_y]], 1)
    arrived = lower_x(summed[rows_x:])
    summed = jnp.concatenate([summed[0:1] + arrived, summed[1:rows_x]], 0)
    return summed


def shards(cotangent, pointwise):
    rows_x, rows_y, rows_z = cotangent.shape
    total_x = rows_x * lax.axis_size(BX)
    total_y = rows_y * lax.axis_size(BY)
    extent = cotangent.shape
    place_x = lax.broadcasted_iota(jnp.int32, extent, 0) + lax.axis_index(BX) * rows_x
    place_y = lax.broadcasted_iota(jnp.int32, extent, 1) + lax.axis_index(BY) * rows_y
    place_z = lax.broadcasted_iota(jnp.int32, extent, 2)
    inside = (
        (place_x > 0) & (place_y > 0) & (place_z > 0) & (place_x < total_x) & (place_y < total_y)
    )
    interior = jnp.where(inside, 1.0, 0.0).astype(jnp.float32)
    diagonal = collect(to_dofs(diagonal_action(pointwise)), rows_x, rows_y, rows_z)

    def operator(dof_field):
        return (
            collect(element_block(pad_top(widen(dof_field)), pointwise), rows_x, rows_y, rows_z)
            * interior
        )

    def local_dot(left, right):
        return jnp.sum(left * right)

    residual = cotangent * interior
    precond = residual / diagonal
    image = operator(precond)
    scaled = image / diagonal
    second = operator(scaled)
    terms = [
        local_dot(residual, precond),
        local_dot(precond, image),
        local_dot(residual, scaled),
        local_dot(image, scaled),
        local_dot(precond, second),
        local_dot(scaled, second),
    ]
    summed = over_axes(jnp.stack(terms), BX_BY)
    rz_now, curvature, cross_r, cross_q, cross_z, curvature_w = [summed[k] for k in range(6)]
    alpha = rz_now / curvature
    fresh = rz_now - alpha * cross_r - alpha * curvature + alpha * alpha * cross_q
    ratio = fresh / rz_now
    grow = 1.0 + ratio
    next_curvature = (
        grow * grow * curvature - alpha * grow * (cross_z + cross_q) + alpha * alpha * curvature_w
    )
    next_alpha = fresh / next_curvature
    residual = residual - alpha * image
    direction = residual / diagonal + ratio * precond
    direction_image = image - alpha * second + ratio * image
    adjoint = alpha * precond + next_alpha * direction
    residual = residual - next_alpha * direction_image
    return (adjoint, residual)


def solution(mesh):
    split = Mesh(mesh.devices.reshape(4, 3, 4, 8, 2), ("bx_0", "bx_1", "by_0", "by_1", "by_2"))
    in_specs = (P(BX, BY, None), P(None, None, None, None, BX, BY, None))
    out_specs = (P(BX, BY, None), P(BX, BY, None))
    return jax.shard_map(
        shards, mesh=split, in_specs=in_specs, out_specs=out_specs, check_vma=False
    )
```

```python
import math

import jax
import jax.numpy as jnp
import numpy as np
from jax import lax
from jax.sharding import Mesh
from jax.sharding import PartitionSpec as P

ITERS = 2
BX = ("bx_0", "bx_1")
BY = ("by_0", "by_1", "by_2")
BX_BY = ("bx_0", "bx_1", "by_0", "by_1", "by_2")


EINSUM_FORMS = ("pa,abcxyz->pbcxyz", "pb,abcxyz->apcxyz", "pc,abcxyz->abpxyz")


def shifted(value, axis, steps):
    count = lax.axis_size(axis)
    initial, last = (max(0, -steps), min(count, count - steps))
    return lax.ppermute(value, axis, [(source, source + steps) for source in range(initial, last)])


def over_axes(value, axes):
    for axis in axes:
        value = lax.psum(value, axis)
    return value


def gauss_tables():
    inner_point = math.sqrt(3.0 / 7.0 - 2.0 / 7.0 * math.sqrt(6.0 / 5.0))
    outer_point = math.sqrt(3.0 / 7.0 + 2.0 / 7.0 * math.sqrt(6.0 / 5.0))
    points = [-outer_point, -inner_point, inner_point, outer_point]
    lobatto = [-1.0, -1.0 / math.sqrt(5.0), 1.0 / math.sqrt(5.0), 1.0]
    values = np.zeros((4, 4))
    slopes = np.zeros((4, 4))
    for a in range(4):
        others = [lobatto[k] for k in range(4) if k != a]
        scaling = (lobatto[a] - others[0]) * (lobatto[a] - others[1]) * (lobatto[a] - others[2])
        for q in range(4):
            sample = points[q]
            values[q, a] = (
                (sample - others[0]) * (sample - others[1]) * (sample - others[2]) / scaling
            )
            slopes[q, a] = (
                (sample - others[1]) * (sample - others[2])
                + (sample - others[0]) * (sample - others[2])
                + (sample - others[0]) * (sample - others[1])
            ) / scaling
    return (values, slopes)


def apply_table(weights_1d, operand, stack_pos):
    return jnp.einsum(EINSUM_FORMS[stack_pos], weights_1d, operand, precision=lax.Precision.HIGHEST)


def split_axis(dof_field, axis_pos, stack_pos):
    elem_count = (dof_field.shape[axis_pos] - 1) // 3
    widths = [(0, 0)] * dof_field.ndim
    widths[axis_pos] = (0, 2)
    padded = jnp.pad(dof_field, widths)
    shaped = padded.reshape(
        dof_field.shape[:axis_pos] + (elem_count + 1, 3) + dof_field.shape[axis_pos + 1 :]
    )
    lower_rows = lax.slice_in_dim(shaped, 0, elem_count, axis=axis_pos)
    upper_rows = lax.slice_in_dim(shaped, 1, elem_count + 1, axis=axis_pos)
    pieces = [lax.index_in_dim(lower_rows, k, axis_pos + 1, keepdims=False) for k in range(3)]
    pieces.append(lax.index_in_dim(upper_rows, 0, axis_pos + 1, keepdims=False))
    return jnp.stack(pieces, stack_pos)


def merge_axis(parts, axis_pos, stack_pos):
    pieces = [lax.index_in_dim(parts, k, stack_pos, keepdims=False) for k in range(4)]
    target = axis_pos - 1
    extent = pieces[0].shape
    elem_count = extent[target]
    ending = [(0, 0)] * len(extent)
    ending[target] = (0, 1)
    leading = [(0, 0)] * len(extent)
    leading[target] = (1, 0)
    head_piece = jnp.pad(pieces[0], ending) + jnp.pad(pieces[3], leading)
    stacked = jnp.stack(
        [head_piece, jnp.pad(pieces[1], ending), jnp.pad(pieces[2], ending)], target + 1
    )
    merged = stacked.reshape(extent[:target] + (3 * (elem_count + 1),) + extent[target + 1 :])
    return lax.slice_in_dim(merged, 0, 3 * elem_count + 1, axis=target)


def element_action(elements, pointwise):
    table_pair = gauss_tables()
    values = jnp.asarray(table_pair[0], jnp.float32)
    slopes = jnp.asarray(table_pair[1], jnp.float32)
    coeffs = pointwise.astype(jnp.float32)
    x_value = apply_table(values, elements, 0)
    x_slope = apply_table(slopes, elements, 0)
    value_value = apply_table(values, x_value, 1)
    value_slope = apply_table(slopes, x_value, 1)
    slope_value = apply_table(values, x_slope, 1)
    point_value = apply_table(values, value_value, 2)
    grad_z = apply_table(slopes, value_value, 2)
    grad_y = apply_table(values, value_slope, 2)
    grad_x = apply_table(values, slope_value, 2)
    flux_x = coeffs[1] * grad_x + coeffs[4] * grad_y + coeffs[5] * grad_z
    flux_y = coeffs[4] * grad_x + coeffs[2] * grad_y + coeffs[6] * grad_z
    flux_z = coeffs[5] * grad_x + coeffs[6] * grad_y + coeffs[3] * grad_z
    mass_term = coeffs[0] * point_value
    back_plain = apply_table(values.T, mass_term, 2) + apply_table(slopes.T, flux_z, 2)
    back_fluxx = apply_table(values.T, flux_x, 2)
    back_fluxy = apply_table(values.T, flux_y, 2)
    near_sum = apply_table(values.T, back_plain, 1) + apply_table(slopes.T, back_fluxy, 1)
    far_sum = apply_table(values.T, back_fluxx, 1)
    return apply_table(values.T, near_sum, 0) + apply_table(slopes.T, far_sum, 0)


def diagonal_action(pointwise):
    table_pair = gauss_tables()
    values = jnp.asarray(table_pair[0], jnp.float32)
    slopes = jnp.asarray(table_pair[1], jnp.float32)
    coeffs = pointwise.astype(jnp.float32)
    square_v = values * values
    square_s = slopes * slopes
    mixed_vs = values * slopes

    def triple(table_x, table_y, table_z, term):
        return apply_table(table_x.T, apply_table(table_y.T, apply_table(table_z.T, term, 2), 1), 0)

    running_total = triple(square_v, square_v, square_v, coeffs[0])
    running_total = running_total + triple(square_s, square_v, square_v, coeffs[1])
    running_total = running_total + triple(square_v, square_s, square_v, coeffs[2])
    running_total = running_total + triple(square_v, square_v, square_s, coeffs[3])
    running_total = running_total + 2.0 * triple(mixed_vs, mixed_vs, square_v, coeffs[4])
    running_total = running_total + 2.0 * triple(mixed_vs, square_v, mixed_vs, coeffs[5])
    running_total = running_total + 2.0 * triple(square_v, mixed_vs, mixed_vs, coeffs[6])
    return running_total


def to_dofs(parts):
    return merge_axis(merge_axis(merge_axis(parts, 5, 2), 3, 1), 1, 0)


def element_block(dof_block, pointwise):
    elements = split_axis(split_axis(split_axis(dof_block, 0, 0), 2, 1), 4, 2)
    return to_dofs(element_action(elements, pointwise))


def banded(table, count):
    band = np.zeros((3 * count + 1, 4, count))
    for index in range(count):
        band[3 * index : 3 * index + 4, :, index] = table.T
    return band


def planar(table_x, table_y, count_x, count_y):
    kron = np.einsum("xpi,yqj->piqjxy", banded(table_x, count_x), banded(table_y, count_y))
    return jnp.asarray(kron.reshape(16 * count_x * count_y, -1), jnp.float32)


def long_axis(table, count):
    place = lax.broadcasted_iota(jnp.int32, (3 * count + 1, 4, count), 0)
    first = lax.broadcasted_iota(jnp.int32, (3 * count + 1, 4, count), 2) * 3
    point = lax.broadcasted_iota(jnp.int32, (3 * count + 1, 4, count), 1)
    place, first, point = lax.optimization_barrier((place, first, point))
    offset = place - first
    band = jnp.zeros(place.shape, jnp.float32)
    for node in range(4):
        column = jnp.asarray(table[:, node], jnp.float32)[point]
        band = band + jnp.where(offset == node, column, 0.0)
    return band.reshape(3 * count + 1, 4 * count)


def mat(left, right):
    return jnp.matmul(left, right, precision=lax.Precision.HIGHEST)


def point_layout(pointwise):
    count_x, count_y, count_z = pointwise.shape[4:]
    coeffs = pointwise.astype(jnp.float32).transpose(0, 1, 4, 2, 5, 3, 6)
    return coeffs.reshape(7, 16 * count_x * count_y, 4 * count_z)


def band_operator(field, coeffs, counts):
    count_x, count_y, count_z = counts
    values, slopes = gauss_tables()
    plain = planar(values, values, count_x, count_y)
    along_x = planar(slopes, values, count_x, count_y)
    along_y = planar(values, slopes, count_x, count_y)
    z_tables = jnp.concatenate([long_axis(values, count_z), long_axis(slopes, count_z)], 1)
    rows = field.shape[0] * field.shape[1]
    width = 4 * count_z
    through_z = mat(field.reshape(rows, field.shape[2]), z_tables)
    z_value = through_z[:, :width]
    point_value = mat(plain, z_value)
    grad_x = mat(along_x, z_value)
    grad_y = mat(along_y, z_value)
    grad_z = mat(plain, through_z[:, width:])
    flux_x = coeffs[1] * grad_x + coeffs[4] * grad_y + coeffs[5] * grad_z
    flux_y = coeffs[4] * grad_x + coeffs[2] * grad_y + coeffs[6] * grad_z
    flux_z = coeffs[5] * grad_x + coeffs[6] * grad_y + coeffs[3] * grad_z
    mass_term = coeffs[0] * point_value
    backward = jnp.concatenate([plain, along_x, along_y], 0).T
    near = mat(backward, jnp.concatenate([mass_term, flux_x, flux_y], 0))
    far = mat(plain.T, flux_z)
    merged = mat(jnp.concatenate([near, far], 1), z_tables.T)
    return merged.reshape(field.shape)


def band_diagonal(coeffs, counts):
    count_x, count_y, count_z = counts
    values, slopes = gauss_tables()
    square_v = values * values
    square_s = slopes * slopes
    mixed = values * slopes
    groups = [
        (square_v, [(square_v, square_v, 0, 1.0), (square_s, square_v, 1, 1.0),
                    (square_v, square_s, 2, 1.0), (mixed, mixed, 4, 2.0)]),
        (square_s, [(square_v, square_v, 3, 1.0)]),
        (mixed, [(mixed, square_v, 5, 2.0), (square_v, mixed, 6, 2.0)]),
    ]
    total = 0.0
    for z_table, members in groups:
        inner = 0.0
        for table_x, table_y, entry, factor in members:
            inner = inner + mat(factor * planar(table_x, table_y, count_x, count_y).T, coeffs[entry])
        total = total + mat(inner, long_axis(z_table, count_z).T)
    return total.reshape(3 * count_x + 1, 3 * count_y + 1, 3 * count_z + 1)


def upper_x(plane):
    return shifted(plane, BX, -1)


def upper_y(plane):
    return shifted(plane, BY, -1)


def lower_x(plane):
    return shifted(plane, BX, 1)


def lower_y(plane):
    return shifted(plane, BY, 1)


def global_sums(terms):
    return (over_axes(terms[0], BX_BY), over_axes(terms[1], BX_BY))


def widen(dof_field):
    widened = jnp.concatenate([dof_field, upper_x(dof_field[0:1])], 0)
    widened = jnp.concatenate([widened, upper_y(widened[:, 0:1])], 1)
    return widened


def pad_top(dof_field):
    return jnp.pad(dof_field, ((0, 0), (0, 0), (0, 1)))


def collect(contributions, rows_x, rows_y, rows_z):
    summed = contributions[:, :, :rows_z]
    arrived = lower_y(summed[:, rows_y:])
    summed = jnp.concatenate([summed[:, 0:1] + arrived, summed[:, 1:rows_y]], 1)
    arrived = lower_x(summed[rows_x:])
    summed = jnp.concatenate([summed[0:1] + arrived, summed[1:rows_x]], 0)
    return summed


def shards(cotangent, pointwise):
    rows_x, rows_y, rows_z = cotangent.shape
    total_x = rows_x * lax.axis_size(BX)
    total_y = rows_y * lax.axis_size(BY)
    extent = cotangent.shape
    place_x = lax.broadcasted_iota(jnp.int32, extent, 0) + lax.axis_index(BX) * rows_x
    place_y = lax.broadcasted_iota(jnp.int32, extent, 1) + lax.axis_index(BY) * rows_y
    place_z = lax.broadcasted_iota(jnp.int32, extent, 2)
    inside = (
        (place_x > 0) & (place_y > 0) & (place_z > 0) & (place_x < total_x) & (place_y < total_y)
    )
    interior = jnp.where(inside, 1.0, 0.0).astype(jnp.float32)
    counts = pointwise.shape[4:]
    coeffs = point_layout(pointwise)
    diagonal = collect(band_diagonal(coeffs, counts), rows_x, rows_y, rows_z)

    def operator(dof_field):
        return (
            collect(band_operator(pad_top(widen(dof_field)), coeffs, counts), rows_x, rows_y, rows_z)
            * interior
        )

    def local_dot(left, right):
        return jnp.sum(left * right)

    residual = cotangent * interior
    precond = residual / diagonal
    image = operator(precond)
    scaled = image / diagonal
    second = operator(scaled)
    terms = [
        local_dot(residual, precond),
        local_dot(precond, image),
        local_dot(residual, scaled),
        local_dot(image, scaled),
        local_dot(precond, second),
        local_dot(scaled, second),
    ]
    summed = over_axes(jnp.stack(terms), BX_BY)
    rz_now, curvature, cross_r, cross_q, cross_z, curvature_w = [summed[k] for k in range(6)]
    alpha = rz_now / curvature
    fresh = rz_now - alpha * cross_r - alpha * curvature + alpha * alpha * cross_q
    ratio = fresh / rz_now
    grow = 1.0 + ratio
    next_curvature = (
        grow * grow * curvature - alpha * grow * (cross_z + cross_q) + alpha * alpha * curvature_w
    )
    next_alpha = fresh / next_curvature
    residual = residual - alpha * image
    direction = residual / diagonal + ratio * precond
    direction_image = image - alpha * second + ratio * image
    adjoint = alpha * precond + next_alpha * direction
    residual = residual - next_alpha * direction_image
    return (adjoint, residual)


def solution(mesh):
    split = Mesh(mesh.devices.reshape(4, 3, 4, 8, 2), ("bx_0", "bx_1", "by_0", "by_1", "by_2"))
    in_specs = (P(BX, BY, None), P(None, None, None, None, BX, BY, None))
    out_specs = (P(BX, BY, None), P(BX, BY, None))
    return jax.shard_map(
        shards, mesh=split, in_specs=in_specs, out_specs=out_specs, check_vma=False
    )
```

```python
import math

import jax
import jax.numpy as jnp
import numpy as np
from jax import lax
from jax.sharding import Mesh
from jax.sharding import PartitionSpec as P

ITERS = 2
BX = ("bx_0", "bx_1")
BY = ("by_0", "by_1", "by_2")
BX_BY = ("bx_0", "bx_1", "by_0", "by_1", "by_2")


EINSUM_FORMS = ("pa,abcxyz->pbcxyz", "pb,abcxyz->apcxyz", "pc,abcxyz->abpxyz")


def shifted(value, axis, steps):
    count = lax.axis_size(axis)
    initial, last = (max(0, -steps), min(count, count - steps))
    return lax.ppermute(value, axis, [(source, source + steps) for source in range(initial, last)])


def over_axes(value, axes):
    for axis in axes:
        value = lax.psum(value, axis)
    return value


def gauss_tables():
    inner_point = math.sqrt(3.0 / 7.0 - 2.0 / 7.0 * math.sqrt(6.0 / 5.0))
    outer_point = math.sqrt(3.0 / 7.0 + 2.0 / 7.0 * math.sqrt(6.0 / 5.0))
    points = [-outer_point, -inner_point, inner_point, outer_point]
    lobatto = [-1.0, -1.0 / math.sqrt(5.0), 1.0 / math.sqrt(5.0), 1.0]
    values = np.zeros((4, 4))
    slopes = np.zeros((4, 4))
    for a in range(4):
        others = [lobatto[k] for k in range(4) if k != a]
        scaling = (lobatto[a] - others[0]) * (lobatto[a] - others[1]) * (lobatto[a] - others[2])
        for q in range(4):
            sample = points[q]
            values[q, a] = (
                (sample - others[0]) * (sample - others[1]) * (sample - others[2]) / scaling
            )
            slopes[q, a] = (
                (sample - others[1]) * (sample - others[2])
                + (sample - others[0]) * (sample - others[2])
                + (sample - others[0]) * (sample - others[1])
            ) / scaling
    return (values, slopes)


def apply_table(weights_1d, operand, stack_pos):
    return jnp.einsum(EINSUM_FORMS[stack_pos], weights_1d, operand, precision=lax.Precision.HIGHEST)


def split_axis(dof_field, axis_pos, stack_pos):
    elem_count = (dof_field.shape[axis_pos] - 1) // 3
    widths = [(0, 0)] * dof_field.ndim
    widths[axis_pos] = (0, 2)
    padded = jnp.pad(dof_field, widths)
    shaped = padded.reshape(
        dof_field.shape[:axis_pos] + (elem_count + 1, 3) + dof_field.shape[axis_pos + 1 :]
    )
    lower_rows = lax.slice_in_dim(shaped, 0, elem_count, axis=axis_pos)
    upper_rows = lax.slice_in_dim(shaped, 1, elem_count + 1, axis=axis_pos)
    pieces = [lax.index_in_dim(lower_rows, k, axis_pos + 1, keepdims=False) for k in range(3)]
    pieces.append(lax.index_in_dim(upper_rows, 0, axis_pos + 1, keepdims=False))
    return jnp.stack(pieces, stack_pos)


def merge_axis(parts, axis_pos, stack_pos):
    pieces = [lax.index_in_dim(parts, k, stack_pos, keepdims=False) for k in range(4)]
    target = axis_pos - 1
    extent = pieces[0].shape
    elem_count = extent[target]
    ending = [(0, 0)] * len(extent)
    ending[target] = (0, 1)
    leading = [(0, 0)] * len(extent)
    leading[target] = (1, 0)
    head_piece = jnp.pad(pieces[0], ending) + jnp.pad(pieces[3], leading)
    stacked = jnp.stack(
        [head_piece, jnp.pad(pieces[1], ending), jnp.pad(pieces[2], ending)], target + 1
    )
    merged = stacked.reshape(extent[:target] + (3 * (elem_count + 1),) + extent[target + 1 :])
    return lax.slice_in_dim(merged, 0, 3 * elem_count + 1, axis=target)


def element_action(elements, pointwise):
    table_pair = gauss_tables()
    values = jnp.asarray(table_pair[0], jnp.float32)
    slopes = jnp.asarray(table_pair[1], jnp.float32)
    coeffs = pointwise.astype(jnp.float32)
    x_value = apply_table(values, elements, 0)
    x_slope = apply_table(slopes, elements, 0)
    value_value = apply_table(values, x_value, 1)
    value_slope = apply_table(slopes, x_value, 1)
    slope_value = apply_table(values, x_slope, 1)
    point_value = apply_table(values, value_value, 2)
    grad_z = apply_table(slopes, value_value, 2)
    grad_y = apply_table(values, value_slope, 2)
    grad_x = apply_table(values, slope_value, 2)
    flux_x = coeffs[1] * grad_x + coeffs[4] * grad_y + coeffs[5] * grad_z
    flux_y = coeffs[4] * grad_x + coeffs[2] * grad_y + coeffs[6] * grad_z
    flux_z = coeffs[5] * grad_x + coeffs[6] * grad_y + coeffs[3] * grad_z
    mass_term = coeffs[0] * point_value
    back_plain = apply_table(values.T, mass_term, 2) + apply_table(slopes.T, flux_z, 2)
    back_fluxx = apply_table(values.T, flux_x, 2)
    back_fluxy = apply_table(values.T, flux_y, 2)
    near_sum = apply_table(values.T, back_plain, 1) + apply_table(slopes.T, back_fluxy, 1)
    far_sum = apply_table(values.T, back_fluxx, 1)
    return apply_table(values.T, near_sum, 0) + apply_table(slopes.T, far_sum, 0)


def diagonal_action(pointwise):
    table_pair = gauss_tables()
    values = jnp.asarray(table_pair[0], jnp.float32)
    slopes = jnp.asarray(table_pair[1], jnp.float32)
    coeffs = pointwise.astype(jnp.float32)
    square_v = values * values
    square_s = slopes * slopes
    mixed_vs = values * slopes

    def triple(table_x, table_y, table_z, term):
        return apply_table(table_x.T, apply_table(table_y.T, apply_table(table_z.T, term, 2), 1), 0)

    running_total = triple(square_v, square_v, square_v, coeffs[0])
    running_total = running_total + triple(square_s, square_v, square_v, coeffs[1])
    running_total = running_total + triple(square_v, square_s, square_v, coeffs[2])
    running_total = running_total + triple(square_v, square_v, square_s, coeffs[3])
    running_total = running_total + 2.0 * triple(mixed_vs, mixed_vs, square_v, coeffs[4])
    running_total = running_total + 2.0 * triple(mixed_vs, square_v, mixed_vs, coeffs[5])
    running_total = running_total + 2.0 * triple(square_v, mixed_vs, mixed_vs, coeffs[6])
    return running_total


def to_dofs(parts):
    return merge_axis(merge_axis(merge_axis(parts, 5, 2), 3, 1), 1, 0)


def element_block(dof_block, pointwise):
    elements = split_axis(split_axis(split_axis(dof_block, 0, 0), 2, 1), 4, 2)
    return to_dofs(element_action(elements, pointwise))


def banded(table, count):
    band = np.zeros((3 * count + 1, 4, count))
    for index in range(count):
        band[3 * index : 3 * index + 4, :, index] = table.T
    return band


def planar(table_x, table_y, count_x, count_y):
    kron = np.einsum("xpi,yqj->piqjxy", banded(table_x, count_x), banded(table_y, count_y))
    return jnp.asarray(kron.reshape(16 * count_x * count_y, -1), jnp.float32)


def long_axis(table, count):
    place = lax.broadcasted_iota(jnp.int32, (3 * count + 1, 4, count), 0)
    first = lax.broadcasted_iota(jnp.int32, (3 * count + 1, 4, count), 2) * 3
    point = lax.broadcasted_iota(jnp.int32, (3 * count + 1, 4, count), 1)
    place, first, point = lax.optimization_barrier((place, first, point))
    offset = place - first
    band = jnp.zeros(place.shape, jnp.float32)
    for node in range(4):
        column = jnp.asarray(table[:, node], jnp.float32)[point]
        band = band + jnp.where(offset == node, column, 0.0)
    return band.reshape(3 * count + 1, 4 * count)


def mat(left, right):
    return jnp.matmul(left, right, precision=lax.Precision.HIGHEST)


def point_layout(pointwise):
    count_x, count_y, count_z = pointwise.shape[4:]
    coeffs = pointwise.astype(jnp.float32).transpose(0, 1, 4, 2, 5, 3, 6)
    return coeffs.reshape(7, 16 * count_x * count_y, 4 * count_z)


def band_operator(field, coeffs, counts):
    count_x, count_y, count_z = counts
    values, slopes = gauss_tables()
    plain = planar(values, values, count_x, count_y)
    along_x = planar(slopes, values, count_x, count_y)
    along_y = planar(values, slopes, count_x, count_y)
    z_tables = jnp.concatenate([long_axis(values, count_z), long_axis(slopes, count_z)], 1)
    rows = field.shape[0] * field.shape[1]
    width = 4 * count_z
    through_z = mat(field.reshape(rows, field.shape[2]), z_tables)
    z_value = through_z[:, :width]
    point_value = mat(plain, z_value)
    grad_x = mat(along_x, z_value)
    grad_y = mat(along_y, z_value)
    grad_z = mat(plain, through_z[:, width:])
    flux_x = coeffs[1] * grad_x + coeffs[4] * grad_y + coeffs[5] * grad_z
    flux_y = coeffs[4] * grad_x + coeffs[2] * grad_y + coeffs[6] * grad_z
    flux_z = coeffs[5] * grad_x + coeffs[6] * grad_y + coeffs[3] * grad_z
    mass_term = coeffs[0] * point_value
    backward = jnp.concatenate([plain, along_x, along_y], 0).T
    near = mat(backward, jnp.concatenate([mass_term, flux_x, flux_y], 0))
    far = mat(plain.T, flux_z)
    merged = mat(jnp.concatenate([near, far], 1), z_tables.T)
    return merged.reshape(field.shape)


def band_diagonal(coeffs, counts):
    count_x, count_y, count_z = counts
    values, slopes = gauss_tables()
    square_v = values * values
    square_s = slopes * slopes
    mixed = values * slopes
    groups = [
        (square_v, [(square_v, square_v, 0, 1.0), (square_s, square_v, 1, 1.0),
                    (square_v, square_s, 2, 1.0), (mixed, mixed, 4, 2.0)]),
        (square_s, [(square_v, square_v, 3, 1.0)]),
        (mixed, [(mixed, square_v, 5, 2.0), (square_v, mixed, 6, 2.0)]),
    ]
    total = 0.0
    for z_table, members in groups:
        inner = 0.0
        for table_x, table_y, entry, factor in members:
            inner = inner + mat(factor * planar(table_x, table_y, count_x, count_y).T, coeffs[entry])
        total = total + mat(inner, long_axis(z_table, count_z).T)
    return total.reshape(3 * count_x + 1, 3 * count_y + 1, 3 * count_z + 1)


def moved(value, steps_x, steps_y):
    count_x = lax.axis_size(BX)
    count_y = lax.axis_size(BY)
    pairs = []
    for source_x in range(count_x):
        for source_y in range(count_y):
            target_x, target_y = source_x + steps_x, source_y + steps_y
            if 0 <= target_x < count_x and 0 <= target_y < count_y:
                pairs.append((source_x * count_y + source_y, target_x * count_y + target_y))
    return lax.ppermute(value, BX_BY, pairs)


def surround(dof_field):
    rows_x, rows_y = dof_field.shape[:2]
    top_x, top_y = rows_x - 3, rows_y - 3
    lower_row = jnp.concatenate(
        [
            moved(dof_field[top_x:, top_y:], 1, 1),
            moved(dof_field[top_x:], 1, 0),
            moved(dof_field[top_x:, 0:1], 1, -1),
        ],
        1,
    )
    own_row = jnp.concatenate(
        [moved(dof_field[:, top_y:], 0, 1), dof_field, moved(dof_field[:, 0:1], 0, -1)], 1
    )
    upper_row = jnp.concatenate(
        [
            moved(dof_field[0:1, top_y:], -1, 1),
            moved(dof_field[0:1], -1, 0),
            moved(dof_field[0:1, 0:1], -1, -1),
        ],
        1,
    )
    return jnp.concatenate([lower_row, own_row, upper_row], 0)


def ghost_points(pointwise):
    points = pointwise.astype(jnp.float32)
    corner = moved(points[:, :, :, :, -1:, -1:], 1, 1)
    below_x = moved(points[:, :, :, :, -1:], 1, 0)
    below_y = moved(points[:, :, :, :, :, -1:], 0, 1)
    lower_row = jnp.concatenate([corner, below_x], 5)
    own_row = jnp.concatenate([below_y, points], 5)
    return jnp.concatenate([lower_row, own_row], 4)


def gather_contributions(contributions, rows_x, rows_y, rows_z):
    own = contributions[:rows_x, :rows_y, :rows_z]
    from_x = moved(contributions[rows_x:, :rows_y, :rows_z], 1, 0)
    from_y = moved(contributions[:rows_x, rows_y:, :rows_z], 0, 1)
    from_corner = moved(contributions[rows_x:, rows_y:, :rows_z], 1, 1)
    head = own[0:1] + from_x
    head = jnp.concatenate([head[:, 0:1] + from_corner, head[:, 1:]], 1)
    own = jnp.concatenate([head, own[1:]], 0)
    return jnp.concatenate([own[:, 0:1] + from_y, own[:, 1:]], 1)


def upper_x(plane):
    return shifted(plane, BX, -1)


def upper_y(plane):
    return shifted(plane, BY, -1)


def lower_x(plane):
    return shifted(plane, BX, 1)


def lower_y(plane):
    return shifted(plane, BY, 1)


def global_sums(terms):
    return (over_axes(terms[0], BX_BY), over_axes(terms[1], BX_BY))


def widen(dof_field):
    widened = jnp.concatenate([dof_field, upper_x(dof_field[0:1])], 0)
    widened = jnp.concatenate([widened, upper_y(widened[:, 0:1])], 1)
    return widened


def pad_top(dof_field):
    return jnp.pad(dof_field, ((0, 0), (0, 0), (0, 1)))


def collect(contributions, rows_x, rows_y, rows_z):
    summed = contributions[:, :, :rows_z]
    arrived = lower_y(summed[:, rows_y:])
    summed = jnp.concatenate([summed[:, 0:1] + arrived, summed[:, 1:rows_y]], 1)
    arrived = lower_x(summed[rows_x:])
    summed = jnp.concatenate([summed[0:1] + arrived, summed[1:rows_x]], 0)
    return summed


def shards(cotangent, pointwise):
    rows_x, rows_y, rows_z = cotangent.shape
    total_x = rows_x * lax.axis_size(BX)
    total_y = rows_y * lax.axis_size(BY)
    extent = cotangent.shape
    place_x = lax.broadcasted_iota(jnp.int32, extent, 0) + lax.axis_index(BX) * rows_x
    place_y = lax.broadcasted_iota(jnp.int32, extent, 1) + lax.axis_index(BY) * rows_y
    place_z = lax.broadcasted_iota(jnp.int32, extent, 2)
    inside = (
        (place_x > 0) & (place_y > 0) & (place_z > 0) & (place_x < total_x) & (place_y < total_y)
    )
    interior = jnp.where(inside, 1.0, 0.0).astype(jnp.float32)
    counts = pointwise.shape[4:]
    coeffs = point_layout(pointwise)
    diagonal = gather_contributions(band_diagonal(coeffs, counts), rows_x, rows_y, rows_z)
    wide_counts = (counts[0] + 1, counts[1] + 1, counts[2])
    wide_coeffs = point_layout(ghost_points(pointwise))

    def operator(dof_field):
        wide = band_operator(pad_top(surround(dof_field)), wide_coeffs, wide_counts)
        return wide[3 : 3 + rows_x, 3 : 3 + rows_y, :rows_z] * interior

    def local_dot(left, right):
        return jnp.sum(left * right)

    residual = cotangent * interior
    precond = residual / diagonal
    image = operator(precond)
    scaled = image / diagonal
    second = operator(scaled)
    terms = [
        local_dot(residual, precond),
        local_dot(precond, image),
        local_dot(residual, scaled),
        local_dot(image, scaled),
        local_dot(precond, second),
        local_dot(scaled, second),
    ]
    summed = over_axes(jnp.stack(terms), BX_BY)
    rz_now, curvature, cross_r, cross_q, cross_z, curvature_w = [summed[k] for k in range(6)]
    alpha = rz_now / curvature
    fresh = rz_now - alpha * cross_r - alpha * curvature + alpha * alpha * cross_q
    ratio = fresh / rz_now
    grow = 1.0 + ratio
    next_curvature = (
        grow * grow * curvature - alpha * grow * (cross_z + cross_q) + alpha * alpha * curvature_w
    )
    next_alpha = fresh / next_curvature
    residual = residual - alpha * image
    direction = residual / diagonal + ratio * precond
    direction_image = image - alpha * second + ratio * image
    adjoint = alpha * precond + next_alpha * direction
    residual = residual - next_alpha * direction_image
    return (adjoint, residual)


def solution(mesh):
    split = Mesh(mesh.devices.reshape(4, 3, 4, 8, 2), ("bx_0", "bx_1", "by_0", "by_1", "by_2"))
    in_specs = (P(BX, BY, None), P(None, None, None, None, BX, BY, None))
    out_specs = (P(BX, BY, None), P(BX, BY, None))
    return jax.shard_map(
        shards, mesh=split, in_specs=in_specs, out_specs=out_specs, check_vma=False
    )
```

```python
import math

import jax
import jax.numpy as jnp
import numpy as np
from jax import lax
from jax.sharding import Mesh
from jax.sharding import PartitionSpec as P

ITERS = 2
BX = ("bx_0", "bx_1")
BY = ("by_0", "by_1", "by_2")
BX_BY = ("bx_0", "bx_1", "by_0", "by_1", "by_2")


EINSUM_FORMS = ("pa,abcxyz->pbcxyz", "pb,abcxyz->apcxyz", "pc,abcxyz->abpxyz")


def shifted(value, axis, steps):
    count = lax.axis_size(axis)
    initial, last = (max(0, -steps), min(count, count - steps))
    return lax.ppermute(value, axis, [(source, source + steps) for source in range(initial, last)])


def over_axes(value, axes):
    for axis in axes:
        value = lax.psum(value, axis)
    return value


def gauss_tables():
    inner_point = math.sqrt(3.0 / 7.0 - 2.0 / 7.0 * math.sqrt(6.0 / 5.0))
    outer_point = math.sqrt(3.0 / 7.0 + 2.0 / 7.0 * math.sqrt(6.0 / 5.0))
    points = [-outer_point, -inner_point, inner_point, outer_point]
    lobatto = [-1.0, -1.0 / math.sqrt(5.0), 1.0 / math.sqrt(5.0), 1.0]
    values = np.zeros((4, 4))
    slopes = np.zeros((4, 4))
    for a in range(4):
        others = [lobatto[k] for k in range(4) if k != a]
        scaling = (lobatto[a] - others[0]) * (lobatto[a] - others[1]) * (lobatto[a] - others[2])
        for q in range(4):
            sample = points[q]
            values[q, a] = (
                (sample - others[0]) * (sample - others[1]) * (sample - others[2]) / scaling
            )
            slopes[q, a] = (
                (sample - others[1]) * (sample - others[2])
                + (sample - others[0]) * (sample - others[2])
                + (sample - others[0]) * (sample - others[1])
            ) / scaling
    return (values, slopes)


def apply_table(weights_1d, operand, stack_pos):
    return jnp.einsum(EINSUM_FORMS[stack_pos], weights_1d, operand, precision=lax.Precision.HIGHEST)


def split_axis(dof_field, axis_pos, stack_pos):
    elem_count = (dof_field.shape[axis_pos] - 1) // 3
    widths = [(0, 0)] * dof_field.ndim
    widths[axis_pos] = (0, 2)
    padded = jnp.pad(dof_field, widths)
    shaped = padded.reshape(
        dof_field.shape[:axis_pos] + (elem_count + 1, 3) + dof_field.shape[axis_pos + 1 :]
    )
    lower_rows = lax.slice_in_dim(shaped, 0, elem_count, axis=axis_pos)
    upper_rows = lax.slice_in_dim(shaped, 1, elem_count + 1, axis=axis_pos)
    pieces = [lax.index_in_dim(lower_rows, k, axis_pos + 1, keepdims=False) for k in range(3)]
    pieces.append(lax.index_in_dim(upper_rows, 0, axis_pos + 1, keepdims=False))
    return jnp.stack(pieces, stack_pos)


def merge_axis(parts, axis_pos, stack_pos):
    pieces = [lax.index_in_dim(parts, k, stack_pos, keepdims=False) for k in range(4)]
    target = axis_pos - 1
    extent = pieces[0].shape
    elem_count = extent[target]
    ending = [(0, 0)] * len(extent)
    ending[target] = (0, 1)
    leading = [(0, 0)] * len(extent)
    leading[target] = (1, 0)
    head_piece = jnp.pad(pieces[0], ending) + jnp.pad(pieces[3], leading)
    stacked = jnp.stack(
        [head_piece, jnp.pad(pieces[1], ending), jnp.pad(pieces[2], ending)], target + 1
    )
    merged = stacked.reshape(extent[:target] + (3 * (elem_count + 1),) + extent[target + 1 :])
    return lax.slice_in_dim(merged, 0, 3 * elem_count + 1, axis=target)


def element_action(elements, pointwise):
    table_pair = gauss_tables()
    values = jnp.asarray(table_pair[0], jnp.float32)
    slopes = jnp.asarray(table_pair[1], jnp.float32)
    coeffs = pointwise.astype(jnp.float32)
    x_value = apply_table(values, elements, 0)
    x_slope = apply_table(slopes, elements, 0)
    value_value = apply_table(values, x_value, 1)
    value_slope = apply_table(slopes, x_value, 1)
    slope_value = apply_table(values, x_slope, 1)
    point_value = apply_table(values, value_value, 2)
    grad_z = apply_table(slopes, value_value, 2)
    grad_y = apply_table(values, value_slope, 2)
    grad_x = apply_table(values, slope_value, 2)
    flux_x = coeffs[1] * grad_x + coeffs[4] * grad_y + coeffs[5] * grad_z
    flux_y = coeffs[4] * grad_x + coeffs[2] * grad_y + coeffs[6] * grad_z
    flux_z = coeffs[5] * grad_x + coeffs[6] * grad_y + coeffs[3] * grad_z
    mass_term = coeffs[0] * point_value
    back_plain = apply_table(values.T, mass_term, 2) + apply_table(slopes.T, flux_z, 2)
    back_fluxx = apply_table(values.T, flux_x, 2)
    back_fluxy = apply_table(values.T, flux_y, 2)
    near_sum = apply_table(values.T, back_plain, 1) + apply_table(slopes.T, back_fluxy, 1)
    far_sum = apply_table(values.T, back_fluxx, 1)
    return apply_table(values.T, near_sum, 0) + apply_table(slopes.T, far_sum, 0)


def diagonal_action(pointwise):
    table_pair = gauss_tables()
    values = jnp.asarray(table_pair[0], jnp.float32)
    slopes = jnp.asarray(table_pair[1], jnp.float32)
    coeffs = pointwise.astype(jnp.float32)
    square_v = values * values
    square_s = slopes * slopes
    mixed_vs = values * slopes

    def triple(table_x, table_y, table_z, term):
        return apply_table(table_x.T, apply_table(table_y.T, apply_table(table_z.T, term, 2), 1), 0)

    running_total = triple(square_v, square_v, square_v, coeffs[0])
    running_total = running_total + triple(square_s, square_v, square_v, coeffs[1])
    running_total = running_total + triple(square_v, square_s, square_v, coeffs[2])
    running_total = running_total + triple(square_v, square_v, square_s, coeffs[3])
    running_total = running_total + 2.0 * triple(mixed_vs, mixed_vs, square_v, coeffs[4])
    running_total = running_total + 2.0 * triple(mixed_vs, square_v, mixed_vs, coeffs[5])
    running_total = running_total + 2.0 * triple(square_v, mixed_vs, mixed_vs, coeffs[6])
    return running_total


def to_dofs(parts):
    return merge_axis(merge_axis(merge_axis(parts, 5, 2), 3, 1), 1, 0)


def element_block(dof_block, pointwise):
    elements = split_axis(split_axis(split_axis(dof_block, 0, 0), 2, 1), 4, 2)
    return to_dofs(element_action(elements, pointwise))


def banded(table, count):
    band = np.zeros((3 * count + 1, 4, count))
    for index in range(count):
        band[3 * index : 3 * index + 4, :, index] = table.T
    return band


def planar(table_x, table_y, count_x, count_y):
    kron = np.einsum("xpi,yqj->piqjxy", banded(table_x, count_x), banded(table_y, count_y))
    return jnp.asarray(kron.reshape(16 * count_x * count_y, -1), jnp.float32)


def long_axis(table, count):
    place = lax.broadcasted_iota(jnp.int32, (3 * count + 1, 4, count), 0)
    first = lax.broadcasted_iota(jnp.int32, (3 * count + 1, 4, count), 2) * 3
    point = lax.broadcasted_iota(jnp.int32, (3 * count + 1, 4, count), 1)
    place, first, point = lax.optimization_barrier((place, first, point))
    offset = place - first
    band = jnp.zeros(place.shape, jnp.float32)
    for node in range(4):
        column = jnp.asarray(table[:, node], jnp.float32)[point]
        band = band + jnp.where(offset == node, column, 0.0)
    return band.reshape(3 * count + 1, 4 * count)


def mat(left, right):
    return jnp.matmul(left, right, precision=lax.Precision.HIGHEST)


def point_layout(pointwise):
    count_x, count_y, count_z = pointwise.shape[4:]
    coeffs = pointwise.astype(jnp.float32).transpose(0, 1, 4, 2, 5, 3, 6)
    return coeffs.reshape(7, 16 * count_x * count_y, 4 * count_z)


def band_operator(field, coeffs, counts):
    count_x, count_y, count_z = counts
    values, slopes = gauss_tables()
    plain = planar(values, values, count_x, count_y)
    along_x = planar(slopes, values, count_x, count_y)
    along_y = planar(values, slopes, count_x, count_y)
    z_tables = jnp.concatenate([long_axis(values, count_z), long_axis(slopes, count_z)], 1)
    rows = field.shape[0] * field.shape[1]
    width = 4 * count_z
    through_z = mat(field.reshape(rows, field.shape[2]), z_tables)
    z_value = through_z[:, :width]
    point_value = mat(plain, z_value)
    grad_x = mat(along_x, z_value)
    grad_y = mat(along_y, z_value)
    grad_z = mat(plain, through_z[:, width:])
    flux_x = coeffs[1] * grad_x + coeffs[4] * grad_y + coeffs[5] * grad_z
    flux_y = coeffs[4] * grad_x + coeffs[2] * grad_y + coeffs[6] * grad_z
    flux_z = coeffs[5] * grad_x + coeffs[6] * grad_y + coeffs[3] * grad_z
    mass_term = coeffs[0] * point_value
    backward = jnp.concatenate([plain, along_x, along_y], 0).T
    near = mat(backward, jnp.concatenate([mass_term, flux_x, flux_y], 0))
    far = mat(plain.T, flux_z)
    merged = mat(jnp.concatenate([near, far], 1), z_tables.T)
    return merged.reshape(field.shape)


def band_diagonal(coeffs, counts):
    count_x, count_y, count_z = counts
    values, slopes = gauss_tables()
    square_v = values * values
    square_s = slopes * slopes
    mixed = values * slopes
    groups = [
        (square_v, [(square_v, square_v, 0, 1.0), (square_s, square_v, 1, 1.0),
                    (square_v, square_s, 2, 1.0), (mixed, mixed, 4, 2.0)]),
        (square_s, [(square_v, square_v, 3, 1.0)]),
        (mixed, [(mixed, square_v, 5, 2.0), (square_v, mixed, 6, 2.0)]),
    ]
    total = 0.0
    for z_table, members in groups:
        inner = 0.0
        for table_x, table_y, entry, factor in members:
            inner = inner + mat(factor * planar(table_x, table_y, count_x, count_y).T, coeffs[entry])
        total = total + mat(inner, long_axis(z_table, count_z).T)
    return total.reshape(3 * count_x + 1, 3 * count_y + 1, 3 * count_z + 1)


def surround(dof_field):
    rows_x, rows_y = dof_field.shape[:2]
    wide = jnp.concatenate(
        [lower_x(dof_field[rows_x - 3 :]), dof_field, upper_x(dof_field[0:1])], 0
    )
    return jnp.concatenate([lower_y(wide[:, rows_y - 3 :]), wide, upper_y(wide[:, 0:1])], 1)


def ghost_points(pointwise):
    points = pointwise.astype(jnp.float32)
    points = jnp.concatenate([lower_x(points[:, :, :, :, -1:]), points], 4)
    return jnp.concatenate([lower_y(points[:, :, :, :, :, -1:]), points], 5)


def upper_x(plane):
    return shifted(plane, BX, -1)


def upper_y(plane):
    return shifted(plane, BY, -1)


def lower_x(plane):
    return shifted(plane, BX, 1)


def lower_y(plane):
    return shifted(plane, BY, 1)


def global_sums(terms):
    return (over_axes(terms[0], BX_BY), over_axes(terms[1], BX_BY))


def widen(dof_field):
    widened = jnp.concatenate([dof_field, upper_x(dof_field[0:1])], 0)
    widened = jnp.concatenate([widened, upper_y(widened[:, 0:1])], 1)
    return widened


def pad_top(dof_field):
    return jnp.pad(dof_field, ((0, 0), (0, 0), (0, 1)))


def collect(contributions, rows_x, rows_y, rows_z):
    summed = contributions[:, :, :rows_z]
    arrived = lower_y(summed[:, rows_y:])
    summed = jnp.concatenate([summed[:, 0:1] + arrived, summed[:, 1:rows_y]], 1)
    arrived = lower_x(summed[rows_x:])
    summed = jnp.concatenate([summed[0:1] + arrived, summed[1:rows_x]], 0)
    return summed


def shards(cotangent, pointwise):
    rows_x, rows_y, rows_z = cotangent.shape
    total_x = rows_x * lax.axis_size(BX)
    total_y = rows_y * lax.axis_size(BY)
    extent = cotangent.shape
    place_x = lax.broadcasted_iota(jnp.int32, extent, 0) + lax.axis_index(BX) * rows_x
    place_y = lax.broadcasted_iota(jnp.int32, extent, 1) + lax.axis_index(BY) * rows_y
    place_z = lax.broadcasted_iota(jnp.int32, extent, 2)
    inside = (
        (place_x > 0) & (place_y > 0) & (place_z > 0) & (place_x < total_x) & (place_y < total_y)
    )
    interior = jnp.where(inside, 1.0, 0.0).astype(jnp.float32)
    counts = pointwise.shape[4:]
    coeffs = point_layout(pointwise)
    diagonal = collect(band_diagonal(coeffs, counts), rows_x, rows_y, rows_z)
    wide_counts = (counts[0] + 1, counts[1] + 1, counts[2])
    wide_coeffs = point_layout(ghost_points(pointwise))

    def operator(dof_field):
        wide = band_operator(pad_top(surround(dof_field)), wide_coeffs, wide_counts)
        return wide[3 : 3 + rows_x, 3 : 3 + rows_y, :rows_z] * interior

    def local_dot(left, right):
        return jnp.sum(left * right)

    residual = cotangent * interior
    precond = residual / diagonal
    image = operator(precond)
    scaled = image / diagonal
    second = operator(scaled)
    terms = [
        local_dot(residual, precond),
        local_dot(precond, image),
        local_dot(residual, scaled),
        local_dot(image, scaled),
        local_dot(precond, second),
        local_dot(scaled, second),
    ]
    summed = over_axes(jnp.stack(terms), BX_BY)
    rz_now, curvature, cross_r, cross_q, cross_z, curvature_w = [summed[k] for k in range(6)]
    alpha = rz_now / curvature
    fresh = rz_now - alpha * cross_r - alpha * curvature + alpha * alpha * cross_q
    ratio = fresh / rz_now
    grow = 1.0 + ratio
    next_curvature = (
        grow * grow * curvature - alpha * grow * (cross_z + cross_q) + alpha * alpha * curvature_w
    )
    next_alpha = fresh / next_curvature
    residual = residual - alpha * image
    direction = residual / diagonal + ratio * precond
    direction_image = image - alpha * second + ratio * image
    adjoint = alpha * precond + next_alpha * direction
    residual = residual - next_alpha * direction_image
    return (adjoint, residual)


def solution(mesh):
    split = Mesh(mesh.devices.reshape(4, 3, 4, 8, 2), ("bx_0", "bx_1", "by_0", "by_1", "by_2"))
    in_specs = (P(BX, BY, None), P(None, None, None, None, BX, BY, None))
    out_specs = (P(BX, BY, None), P(BX, BY, None))
    return jax.shard_map(
        shards, mesh=split, in_specs=in_specs, out_specs=out_specs, check_vma=False
    )
```

```python
import math

import jax
import jax.numpy as jnp
import numpy as np
from jax import lax
from jax.sharding import Mesh
from jax.sharding import PartitionSpec as P

ITERS = 2
BX = ("bx_0", "bx_1")
BY = ("by_0", "by_1", "by_2")
BX_BY = ("bx_0", "bx_1", "by_0", "by_1", "by_2")


EINSUM_FORMS = ("pa,abcxyz->pbcxyz", "pb,abcxyz->apcxyz", "pc,abcxyz->abpxyz")


def shifted(value, axis, steps):
    count = lax.axis_size(axis)
    initial, last = (max(0, -steps), min(count, count - steps))
    return lax.ppermute(value, axis, [(source, source + steps) for source in range(initial, last)])


def over_axes(value, axes):
    for axis in axes:
        value = lax.psum(value, axis)
    return value


def gauss_tables():
    inner_point = math.sqrt(3.0 / 7.0 - 2.0 / 7.0 * math.sqrt(6.0 / 5.0))
    outer_point = math.sqrt(3.0 / 7.0 + 2.0 / 7.0 * math.sqrt(6.0 / 5.0))
    points = [-outer_point, -inner_point, inner_point, outer_point]
    lobatto = [-1.0, -1.0 / math.sqrt(5.0), 1.0 / math.sqrt(5.0), 1.0]
    values = np.zeros((4, 4))
    slopes = np.zeros((4, 4))
    for a in range(4):
        others = [lobatto[k] for k in range(4) if k != a]
        scaling = (lobatto[a] - others[0]) * (lobatto[a] - others[1]) * (lobatto[a] - others[2])
        for q in range(4):
            sample = points[q]
            values[q, a] = (
                (sample - others[0]) * (sample - others[1]) * (sample - others[2]) / scaling
            )
            slopes[q, a] = (
                (sample - others[1]) * (sample - others[2])
                + (sample - others[0]) * (sample - others[2])
                + (sample - others[0]) * (sample - others[1])
            ) / scaling
    return (values, slopes)


def apply_table(weights_1d, operand, stack_pos):
    return jnp.einsum(EINSUM_FORMS[stack_pos], weights_1d, operand, precision=lax.Precision.HIGHEST)


def split_axis(dof_field, axis_pos, stack_pos):
    elem_count = (dof_field.shape[axis_pos] - 1) // 3
    widths = [(0, 0)] * dof_field.ndim
    widths[axis_pos] = (0, 2)
    padded = jnp.pad(dof_field, widths)
    shaped = padded.reshape(
        dof_field.shape[:axis_pos] + (elem_count + 1, 3) + dof_field.shape[axis_pos + 1 :]
    )
    lower_rows = lax.slice_in_dim(shaped, 0, elem_count, axis=axis_pos)
    upper_rows = lax.slice_in_dim(shaped, 1, elem_count + 1, axis=axis_pos)
    pieces = [lax.index_in_dim(lower_rows, k, axis_pos + 1, keepdims=False) for k in range(3)]
    pieces.append(lax.index_in_dim(upper_rows, 0, axis_pos + 1, keepdims=False))
    return jnp.stack(pieces, stack_pos)


def merge_axis(parts, axis_pos, stack_pos):
    pieces = [lax.index_in_dim(parts, k, stack_pos, keepdims=False) for k in range(4)]
    target = axis_pos - 1
    extent = pieces[0].shape
    elem_count = extent[target]
    ending = [(0, 0)] * len(extent)
    ending[target] = (0, 1)
    leading = [(0, 0)] * len(extent)
    leading[target] = (1, 0)
    head_piece = jnp.pad(pieces[0], ending) + jnp.pad(pieces[3], leading)
    stacked = jnp.stack(
        [head_piece, jnp.pad(pieces[1], ending), jnp.pad(pieces[2], ending)], target + 1
    )
    merged = stacked.reshape(extent[:target] + (3 * (elem_count + 1),) + extent[target + 1 :])
    return lax.slice_in_dim(merged, 0, 3 * elem_count + 1, axis=target)


def element_action(elements, pointwise):
    table_pair = gauss_tables()
    values = jnp.asarray(table_pair[0], jnp.float32)
    slopes = jnp.asarray(table_pair[1], jnp.float32)
    coeffs = pointwise.astype(jnp.float32)
    x_value = apply_table(values, elements, 0)
    x_slope = apply_table(slopes, elements, 0)
    value_value = apply_table(values, x_value, 1)
    value_slope = apply_table(slopes, x_value, 1)
    slope_value = apply_table(values, x_slope, 1)
    point_value = apply_table(values, value_value, 2)
    grad_z = apply_table(slopes, value_value, 2)
    grad_y = apply_table(values, value_slope, 2)
    grad_x = apply_table(values, slope_value, 2)
    flux_x = coeffs[1] * grad_x + coeffs[4] * grad_y + coeffs[5] * grad_z
    flux_y = coeffs[4] * grad_x + coeffs[2] * grad_y + coeffs[6] * grad_z
    flux_z = coeffs[5] * grad_x + coeffs[6] * grad_y + coeffs[3] * grad_z
    mass_term = coeffs[0] * point_value
    back_plain = apply_table(values.T, mass_term, 2) + apply_table(slopes.T, flux_z, 2)
    back_fluxx = apply_table(values.T, flux_x, 2)
    back_fluxy = apply_table(values.T, flux_y, 2)
    near_sum = apply_table(values.T, back_plain, 1) + apply_table(slopes.T, back_fluxy, 1)
    far_sum = apply_table(values.T, back_fluxx, 1)
    return apply_table(values.T, near_sum, 0) + apply_table(slopes.T, far_sum, 0)


def diagonal_action(pointwise):
    table_pair = gauss_tables()
    values = jnp.asarray(table_pair[0], jnp.float32)
    slopes = jnp.asarray(table_pair[1], jnp.float32)
    coeffs = pointwise.astype(jnp.float32)
    square_v = values * values
    square_s = slopes * slopes
    mixed_vs = values * slopes

    def triple(table_x, table_y, table_z, term):
        return apply_table(table_x.T, apply_table(table_y.T, apply_table(table_z.T, term, 2), 1), 0)

    running_total = triple(square_v, square_v, square_v, coeffs[0])
    running_total = running_total + triple(square_s, square_v, square_v, coeffs[1])
    running_total = running_total + triple(square_v, square_s, square_v, coeffs[2])
    running_total = running_total + triple(square_v, square_v, square_s, coeffs[3])
    running_total = running_total + 2.0 * triple(mixed_vs, mixed_vs, square_v, coeffs[4])
    running_total = running_total + 2.0 * triple(mixed_vs, square_v, mixed_vs, coeffs[5])
    running_total = running_total + 2.0 * triple(square_v, mixed_vs, mixed_vs, coeffs[6])
    return running_total


def to_dofs(parts):
    return merge_axis(merge_axis(merge_axis(parts, 5, 2), 3, 1), 1, 0)


def element_block(dof_block, pointwise):
    elements = split_axis(split_axis(split_axis(dof_block, 0, 0), 2, 1), 4, 2)
    return to_dofs(element_action(elements, pointwise))


def banded(table, count):
    band = np.zeros((3 * count + 1, 4, count))
    for index in range(count):
        band[3 * index : 3 * index + 4, :, index] = table.T
    return band


def planar(table_x, table_y, count_x, count_y):
    kron = np.einsum("xpi,yqj->piqjxy", banded(table_x, count_x), banded(table_y, count_y))
    return jnp.asarray(kron.reshape(16 * count_x * count_y, -1), jnp.float32)


def long_axis(table, count):
    length = 3 * count + 1
    rows = jnp.asarray(table, jnp.float32)[:, None, :] + jnp.zeros((4, count, 4), jnp.float32)
    rows = lax.optimization_barrier(rows)
    rows = jnp.pad(rows, ((0, 0), (0, 0), (0, length - 1)))
    band = rows.reshape(4, count * (length + 3))[:, : count * length]
    return band.reshape(4 * count, length)


def mat(left, right):
    return jnp.matmul(left, right, precision=lax.Precision.HIGHEST)


def point_layout(pointwise):
    count_x, count_y, count_z = pointwise.shape[4:]
    coeffs = pointwise.astype(jnp.float32).transpose(0, 1, 4, 2, 5, 3, 6)
    return coeffs.reshape(7, 16 * count_x * count_y, 4 * count_z)


def band_operator(field, coeffs, counts):
    count_x, count_y, count_z = counts
    values, slopes = gauss_tables()
    plain = planar(values, values, count_x, count_y)
    along_x = planar(slopes, values, count_x, count_y)
    along_y = planar(values, slopes, count_x, count_y)
    z_tables = jnp.concatenate([long_axis(values, count_z), long_axis(slopes, count_z)], 0)
    rows = field.shape[0] * field.shape[1]
    width = 4 * count_z
    through_z = mat(field.reshape(rows, field.shape[2]), z_tables.T)
    z_value = through_z[:, :width]
    point_value = mat(plain, z_value)
    grad_x = mat(along_x, z_value)
    grad_y = mat(along_y, z_value)
    grad_z = mat(plain, through_z[:, width:])
    flux_x = coeffs[1] * grad_x + coeffs[4] * grad_y + coeffs[5] * grad_z
    flux_y = coeffs[4] * grad_x + coeffs[2] * grad_y + coeffs[6] * grad_z
    flux_z = coeffs[5] * grad_x + coeffs[6] * grad_y + coeffs[3] * grad_z
    mass_term = coeffs[0] * point_value
    backward = jnp.concatenate([plain, along_x, along_y], 0).T
    near = mat(backward, jnp.concatenate([mass_term, flux_x, flux_y], 0))
    far = mat(plain.T, flux_z)
    merged = mat(jnp.concatenate([near, far], 1), z_tables)
    return merged.reshape(field.shape)


def band_diagonal(coeffs, counts):
    count_x, count_y, count_z = counts
    values, slopes = gauss_tables()
    square_v = values * values
    square_s = slopes * slopes
    mixed = values * slopes
    groups = [
        (square_v, [(square_v, square_v, 0, 1.0), (square_s, square_v, 1, 1.0),
                    (square_v, square_s, 2, 1.0), (mixed, mixed, 4, 2.0)]),
        (square_s, [(square_v, square_v, 3, 1.0)]),
        (mixed, [(mixed, square_v, 5, 2.0), (square_v, mixed, 6, 2.0)]),
    ]
    total = 0.0
    for z_table, members in groups:
        inner = 0.0
        for table_x, table_y, entry, factor in members:
            inner = inner + mat(factor * planar(table_x, table_y, count_x, count_y).T, coeffs[entry])
        total = total + mat(inner, long_axis(z_table, count_z))
    return total.reshape(3 * count_x + 1, 3 * count_y + 1, 3 * count_z + 1)


def upper_x(plane):
    return shifted(plane, BX, -1)


def upper_y(plane):
    return shifted(plane, BY, -1)


def lower_x(plane):
    return shifted(plane, BX, 1)


def lower_y(plane):
    return shifted(plane, BY, 1)


def global_sums(terms):
    return (over_axes(terms[0], BX_BY), over_axes(terms[1], BX_BY))


def widen(dof_field):
    widened = jnp.concatenate([dof_field, upper_x(dof_field[0:1])], 0)
    widened = jnp.concatenate([widened, upper_y(widened[:, 0:1])], 1)
    return widened


def pad_top(dof_field):
    return jnp.pad(dof_field, ((0, 0), (0, 0), (0, 1)))


def collect(contributions, rows_x, rows_y, rows_z):
    summed = contributions[:, :, :rows_z]
    arrived = lower_y(summed[:, rows_y:])
    summed = jnp.concatenate([summed[:, 0:1] + arrived, summed[:, 1:rows_y]], 1)
    arrived = lower_x(summed[rows_x:])
    summed = jnp.concatenate([summed[0:1] + arrived, summed[1:rows_x]], 0)
    return summed


def shards(cotangent, pointwise):
    rows_x, rows_y, rows_z = cotangent.shape
    total_x = rows_x * lax.axis_size(BX)
    total_y = rows_y * lax.axis_size(BY)
    extent = cotangent.shape
    place_x = lax.broadcasted_iota(jnp.int32, extent, 0) + lax.axis_index(BX) * rows_x
    place_y = lax.broadcasted_iota(jnp.int32, extent, 1) + lax.axis_index(BY) * rows_y
    place_z = lax.broadcasted_iota(jnp.int32, extent, 2)
    inside = (
        (place_x > 0) & (place_y > 0) & (place_z > 0) & (place_x < total_x) & (place_y < total_y)
    )
    interior = jnp.where(inside, 1.0, 0.0).astype(jnp.float32)
    counts = pointwise.shape[4:]
    coeffs = point_layout(pointwise)
    diagonal = collect(band_diagonal(coeffs, counts), rows_x, rows_y, rows_z)

    def operator(dof_field):
        return (
            collect(band_operator(pad_top(widen(dof_field)), coeffs, counts), rows_x, rows_y, rows_z)
            * interior
        )

    def local_dot(left, right):
        return jnp.sum(left * right)

    residual = cotangent * interior
    precond = residual / diagonal
    image = operator(precond)
    scaled = image / diagonal
    second = operator(scaled)
    products = jnp.stack(
        [
            residual * precond,
            precond * image,
            residual * scaled,
            image * scaled,
            precond * second,
            scaled * second,
        ]
    )
    terms = jnp.sum(products.reshape(6, -1, products.shape[-1]), axis=(1, 2))
    summed = over_axes(terms, BX_BY)
    rz_now, curvature, cross_r, cross_q, cross_z, curvature_w = [summed[k] for k in range(6)]
    alpha = rz_now / curvature
    fresh = rz_now - alpha * cross_r - alpha * curvature + alpha * alpha * cross_q
    ratio = fresh / rz_now
    grow = 1.0 + ratio
    next_curvature = (
        grow * grow * curvature - alpha * grow * (cross_z + cross_q) + alpha * alpha * curvature_w
    )
    next_alpha = fresh / next_curvature
    residual = residual - alpha * image
    direction = residual / diagonal + ratio * precond
    direction_image = image - alpha * second + ratio * image
    adjoint = alpha * precond + next_alpha * direction
    residual = residual - next_alpha * direction_image
    return (adjoint, residual)


def solution(mesh):
    split = Mesh(mesh.devices.reshape(4, 3, 4, 8, 2), ("bx_0", "bx_1", "by_0", "by_1", "by_2"))
    in_specs = (P(BX, BY, None), P(None, None, None, None, BX, BY, None))
    out_specs = (P(BX, BY, None), P(BX, BY, None))
    return jax.shard_map(
        shards, mesh=split, in_specs=in_specs, out_specs=out_specs, check_vma=False
    )
```

```python
import math

import jax
import jax.numpy as jnp
import numpy as np
from jax import lax
from jax.sharding import Mesh
from jax.sharding import PartitionSpec as P

ITERS = 2
BX = ("bx_0", "bx_1")
BY = ("by_0", "by_1", "by_2")
BX_BY = ("bx_0", "bx_1", "by_0", "by_1", "by_2")


EINSUM_FORMS = ("pa,abcxyz->pbcxyz", "pb,abcxyz->apcxyz", "pc,abcxyz->abpxyz")


def shifted(value, axis, steps):
    count = lax.axis_size(axis)
    initial, last = (max(0, -steps), min(count, count - steps))
    return lax.ppermute(value, axis, [(source, source + steps) for source in range(initial, last)])


def over_axes(value, axes):
    for axis in axes:
        value = lax.psum(value, axis)
    return value


def gauss_tables():
    inner_point = math.sqrt(3.0 / 7.0 - 2.0 / 7.0 * math.sqrt(6.0 / 5.0))
    outer_point = math.sqrt(3.0 / 7.0 + 2.0 / 7.0 * math.sqrt(6.0 / 5.0))
    points = [-outer_point, -inner_point, inner_point, outer_point]
    lobatto = [-1.0, -1.0 / math.sqrt(5.0), 1.0 / math.sqrt(5.0), 1.0]
    values = np.zeros((4, 4))
    slopes = np.zeros((4, 4))
    for a in range(4):
        others = [lobatto[k] for k in range(4) if k != a]
        scaling = (lobatto[a] - others[0]) * (lobatto[a] - others[1]) * (lobatto[a] - others[2])
        for q in range(4):
            sample = points[q]
            values[q, a] = (
                (sample - others[0]) * (sample - others[1]) * (sample - others[2]) / scaling
            )
            slopes[q, a] = (
                (sample - others[1]) * (sample - others[2])
                + (sample - others[0]) * (sample - others[2])
                + (sample - others[0]) * (sample - others[1])
            ) / scaling
    return (values, slopes)


def apply_table(weights_1d, operand, stack_pos):
    return jnp.einsum(EINSUM_FORMS[stack_pos], weights_1d, operand, precision=lax.Precision.HIGHEST)


def split_axis(dof_field, axis_pos, stack_pos):
    elem_count = (dof_field.shape[axis_pos] - 1) // 3
    widths = [(0, 0)] * dof_field.ndim
    widths[axis_pos] = (0, 2)
    padded = jnp.pad(dof_field, widths)
    shaped = padded.reshape(
        dof_field.shape[:axis_pos] + (elem_count + 1, 3) + dof_field.shape[axis_pos + 1 :]
    )
    lower_rows = lax.slice_in_dim(shaped, 0, elem_count, axis=axis_pos)
    upper_rows = lax.slice_in_dim(shaped, 1, elem_count + 1, axis=axis_pos)
    pieces = [lax.index_in_dim(lower_rows, k, axis_pos + 1, keepdims=False) for k in range(3)]
    pieces.append(lax.index_in_dim(upper_rows, 0, axis_pos + 1, keepdims=False))
    return jnp.stack(pieces, stack_pos)


def merge_axis(parts, axis_pos, stack_pos):
    pieces = [lax.index_in_dim(parts, k, stack_pos, keepdims=False) for k in range(4)]
    target = axis_pos - 1
    extent = pieces[0].shape
    elem_count = extent[target]
    ending = [(0, 0)] * len(extent)
    ending[target] = (0, 1)
    leading = [(0, 0)] * len(extent)
    leading[target] = (1, 0)
    head_piece = jnp.pad(pieces[0], ending) + jnp.pad(pieces[3], leading)
    stacked = jnp.stack(
        [head_piece, jnp.pad(pieces[1], ending), jnp.pad(pieces[2], ending)], target + 1
    )
    merged = stacked.reshape(extent[:target] + (3 * (elem_count + 1),) + extent[target + 1 :])
    return lax.slice_in_dim(merged, 0, 3 * elem_count + 1, axis=target)


def element_action(elements, pointwise):
    table_pair = gauss_tables()
    values = jnp.asarray(table_pair[0], jnp.float32)
    slopes = jnp.asarray(table_pair[1], jnp.float32)
    coeffs = pointwise.astype(jnp.float32)
    x_value = apply_table(values, elements, 0)
    x_slope = apply_table(slopes, elements, 0)
    value_value = apply_table(values, x_value, 1)
    value_slope = apply_table(slopes, x_value, 1)
    slope_value = apply_table(values, x_slope, 1)
    point_value = apply_table(values, value_value, 2)
    grad_z = apply_table(slopes, value_value, 2)
    grad_y = apply_table(values, value_slope, 2)
    grad_x = apply_table(values, slope_value, 2)
    flux_x = coeffs[1] * grad_x + coeffs[4] * grad_y + coeffs[5] * grad_z
    flux_y = coeffs[4] * grad_x + coeffs[2] * grad_y + coeffs[6] * grad_z
    flux_z = coeffs[5] * grad_x + coeffs[6] * grad_y + coeffs[3] * grad_z
    mass_term = coeffs[0] * point_value
    back_plain = apply_table(values.T, mass_term, 2) + apply_table(slopes.T, flux_z, 2)
    back_fluxx = apply_table(values.T, flux_x, 2)
    back_fluxy = apply_table(values.T, flux_y, 2)
    near_sum = apply_table(values.T, back_plain, 1) + apply_table(slopes.T, back_fluxy, 1)
    far_sum = apply_table(values.T, back_fluxx, 1)
    return apply_table(values.T, near_sum, 0) + apply_table(slopes.T, far_sum, 0)


def diagonal_action(pointwise):
    table_pair = gauss_tables()
    values = jnp.asarray(table_pair[0], jnp.float32)
    slopes = jnp.asarray(table_pair[1], jnp.float32)
    coeffs = pointwise.astype(jnp.float32)
    square_v = values * values
    square_s = slopes * slopes
    mixed_vs = values * slopes

    def triple(table_x, table_y, table_z, term):
        return apply_table(table_x.T, apply_table(table_y.T, apply_table(table_z.T, term, 2), 1), 0)

    running_total = triple(square_v, square_v, square_v, coeffs[0])
    running_total = running_total + triple(square_s, square_v, square_v, coeffs[1])
    running_total = running_total + triple(square_v, square_s, square_v, coeffs[2])
    running_total = running_total + triple(square_v, square_v, square_s, coeffs[3])
    running_total = running_total + 2.0 * triple(mixed_vs, mixed_vs, square_v, coeffs[4])
    running_total = running_total + 2.0 * triple(mixed_vs, square_v, mixed_vs, coeffs[5])
    running_total = running_total + 2.0 * triple(square_v, mixed_vs, mixed_vs, coeffs[6])
    return running_total


def to_dofs(parts):
    return merge_axis(merge_axis(merge_axis(parts, 5, 2), 3, 1), 1, 0)


def element_block(dof_block, pointwise):
    elements = split_axis(split_axis(split_axis(dof_block, 0, 0), 2, 1), 4, 2)
    return to_dofs(element_action(elements, pointwise))


def banded(table, count):
    band = np.zeros((3 * count + 1, 4, count))
    for index in range(count):
        band[3 * index : 3 * index + 4, :, index] = table.T
    return band


def planar(table_x, table_y, count_x, count_y):
    kron = np.einsum("xpi,yqj->piqjxy", banded(table_x, count_x), banded(table_y, count_y))
    return jnp.asarray(kron.reshape(16 * count_x * count_y, -1), jnp.float32)


def long_axis(table, count, anchor):
    shape = (3 * count + 1, 4, count)
    offset = lax.broadcasted_iota(jnp.int32, shape, 0) - 3 * lax.broadcasted_iota(jnp.int32, shape, 2)
    offset = offset + anchor
    band = jnp.zeros(shape, jnp.float32)
    for node in range(4):
        column = jnp.asarray(table[:, node], jnp.float32)[None, :, None]
        band = band + jnp.where(offset == node, column, 0.0)
    return band.reshape(3 * count + 1, 4 * count)


def mat(left, right):
    return jnp.matmul(left, right, precision=lax.Precision.HIGHEST)


def point_layout(pointwise):
    count_x, count_y, count_z = pointwise.shape[4:]
    coeffs = pointwise.astype(jnp.float32).transpose(0, 1, 4, 2, 5, 3, 6)
    return coeffs.reshape(7, 16 * count_x * count_y, 4 * count_z)


def band_operator(field, coeffs, counts, anchor):
    count_x, count_y, count_z = counts
    values, slopes = gauss_tables()
    plain = planar(values, values, count_x, count_y)
    along_x = planar(slopes, values, count_x, count_y)
    along_y = planar(values, slopes, count_x, count_y)
    z_tables = jnp.concatenate([long_axis(values, count_z, anchor), long_axis(slopes, count_z, anchor)], 1)
    rows = field.shape[0] * field.shape[1]
    width = 4 * count_z
    through_z = mat(field.reshape(rows, field.shape[2]), z_tables)
    z_value = through_z[:, :width]
    point_value = mat(plain, z_value)
    grad_x = mat(along_x, z_value)
    grad_y = mat(along_y, z_value)
    grad_z = mat(plain, through_z[:, width:])
    flux_x = coeffs[1] * grad_x + coeffs[4] * grad_y + coeffs[5] * grad_z
    flux_y = coeffs[4] * grad_x + coeffs[2] * grad_y + coeffs[6] * grad_z
    flux_z = coeffs[5] * grad_x + coeffs[6] * grad_y + coeffs[3] * grad_z
    mass_term = coeffs[0] * point_value
    backward = jnp.concatenate([plain, along_x, along_y], 0).T
    near = mat(backward, jnp.concatenate([mass_term, flux_x, flux_y], 0))
    far = mat(plain.T, flux_z)
    merged = mat(jnp.concatenate([near, far], 1), z_tables.T)
    return merged.reshape(field.shape)


def band_diagonal(coeffs, counts, anchor):
    count_x, count_y, count_z = counts
    values, slopes = gauss_tables()
    square_v = values * values
    square_s = slopes * slopes
    mixed = values * slopes
    groups = [
        (square_v, [(square_v, square_v, 0, 1.0), (square_s, square_v, 1, 1.0),
                    (square_v, square_s, 2, 1.0), (mixed, mixed, 4, 2.0)]),
        (square_s, [(square_v, square_v, 3, 1.0)]),
        (mixed, [(mixed, square_v, 5, 2.0), (square_v, mixed, 6, 2.0)]),
    ]
    total = 0.0
    for z_table, members in groups:
        inner = 0.0
        for table_x, table_y, entry, factor in members:
            inner = inner + mat(factor * planar(table_x, table_y, count_x, count_y).T, coeffs[entry])
        total = total + mat(inner, long_axis(z_table, count_z, anchor).T)
    return total.reshape(3 * count_x + 1, 3 * count_y + 1, 3 * count_z + 1)


def upper_x(plane):
    return shifted(plane, BX, -1)


def upper_y(plane):
    return shifted(plane, BY, -1)


def lower_x(plane):
    return shifted(plane, BX, 1)


def lower_y(plane):
    return shifted(plane, BY, 1)


def global_sums(terms):
    return (over_axes(terms[0], BX_BY), over_axes(terms[1], BX_BY))


def widen(dof_field):
    widened = jnp.concatenate([dof_field, upper_x(dof_field[0:1])], 0)
    widened = jnp.concatenate([widened, upper_y(widened[:, 0:1])], 1)
    return widened


def pad_top(dof_field):
    return jnp.pad(dof_field, ((0, 0), (0, 0), (0, 1)))


def collect(contributions, rows_x, rows_y, rows_z):
    summed = contributions[:, :, :rows_z]
    arrived = lower_y(summed[:, rows_y:])
    summed = jnp.concatenate([summed[:, 0:1] + arrived, summed[:, 1:rows_y]], 1)
    arrived = lower_x(summed[rows_x:])
    summed = jnp.concatenate([summed[0:1] + arrived, summed[1:rows_x]], 0)
    return summed


def shards(cotangent, pointwise):
    rows_x, rows_y, rows_z = cotangent.shape
    total_x = rows_x * lax.axis_size(BX)
    total_y = rows_y * lax.axis_size(BY)
    extent = cotangent.shape
    place_x = lax.broadcasted_iota(jnp.int32, extent, 0) + lax.axis_index(BX) * rows_x
    place_y = lax.broadcasted_iota(jnp.int32, extent, 1) + lax.axis_index(BY) * rows_y
    place_z = lax.broadcasted_iota(jnp.int32, extent, 2)
    inside = (
        (place_x > 0) & (place_y > 0) & (place_z > 0) & (place_x < total_x) & (place_y < total_y)
    )
    interior = jnp.where(inside, 1.0, 0.0).astype(jnp.float32)
    counts = pointwise.shape[4:]
    coeffs = point_layout(pointwise)
    anchor = (cotangent[0, 0, 0] * 0.0).astype(jnp.int32)
    diagonal = collect(band_diagonal(coeffs, counts, anchor), rows_x, rows_y, rows_z)

    def operator(dof_field):
        return (
            collect(band_operator(pad_top(widen(dof_field)), coeffs, counts, anchor), rows_x, rows_y, rows_z)
            * interior
        )

    def local_dot(left, right):
        return jnp.sum(left * right)

    residual = cotangent * interior
    precond = residual / diagonal
    image = operator(precond)
    scaled = image / diagonal
    second = operator(scaled)
    products = jnp.stack(
        [
            residual * precond,
            precond * image,
            residual * scaled,
            image * scaled,
            precond * second,
            scaled * second,
        ]
    )
    terms = jnp.sum(products.reshape(6, -1, products.shape[-1]), axis=(1, 2))
    summed = over_axes(terms, BX_BY)
    rz_now, curvature, cross_r, cross_q, cross_z, curvature_w = [summed[k] for k in range(6)]
    alpha = rz_now / curvature
    fresh = rz_now - alpha * cross_r - alpha * curvature + alpha * alpha * cross_q
    ratio = fresh / rz_now
    grow = 1.0 + ratio
    next_curvature = (
        grow * grow * curvature - alpha * grow * (cross_z + cross_q) + alpha * alpha * curvature_w
    )
    next_alpha = fresh / next_curvature
    residual = residual - alpha * image
    direction = residual / diagonal + ratio * precond
    direction_image = image - alpha * second + ratio * image
    adjoint = alpha * precond + next_alpha * direction
    residual = residual - next_alpha * direction_image
    return (adjoint, residual)


def solution(mesh):
    split = Mesh(mesh.devices.reshape(4, 3, 4, 8, 2), ("bx_0", "bx_1", "by_0", "by_1", "by_2"))
    in_specs = (P(BX, BY, None), P(None, None, None, None, BX, BY, None))
    out_specs = (P(BX, BY, None), P(BX, BY, None))
    return jax.shard_map(
        shards, mesh=split, in_specs=in_specs, out_specs=out_specs, check_vma=False
    )
```

```python
import math

import jax
import jax.numpy as jnp
import numpy as np
from jax import lax
from jax.sharding import Mesh
from jax.sharding import PartitionSpec as P

ITERS = 2
BX = ("bx_0", "bx_1")
BY = ("by_0", "by_1", "by_2")
BX_BY = ("bx_0", "bx_1", "by_0", "by_1", "by_2")


EINSUM_FORMS = ("pa,abcxyz->pbcxyz", "pb,abcxyz->apcxyz", "pc,abcxyz->abpxyz")


def shifted(value, axis, steps):
    count = lax.axis_size(axis)
    initial, last = (max(0, -steps), min(count, count - steps))
    return lax.ppermute(value, axis, [(source, source + steps) for source in range(initial, last)])


def over_axes(value, axes):
    for axis in axes:
        value = lax.psum(value, axis)
    return value


def gauss_tables():
    inner_point = math.sqrt(3.0 / 7.0 - 2.0 / 7.0 * math.sqrt(6.0 / 5.0))
    outer_point = math.sqrt(3.0 / 7.0 + 2.0 / 7.0 * math.sqrt(6.0 / 5.0))
    points = [-outer_point, -inner_point, inner_point, outer_point]
    lobatto = [-1.0, -1.0 / math.sqrt(5.0), 1.0 / math.sqrt(5.0), 1.0]
    values = np.zeros((4, 4))
    slopes = np.zeros((4, 4))
    for a in range(4):
        others = [lobatto[k] for k in range(4) if k != a]
        scaling = (lobatto[a] - others[0]) * (lobatto[a] - others[1]) * (lobatto[a] - others[2])
        for q in range(4):
            sample = points[q]
            values[q, a] = (
                (sample - others[0]) * (sample - others[1]) * (sample - others[2]) / scaling
            )
            slopes[q, a] = (
                (sample - others[1]) * (sample - others[2])
                + (sample - others[0]) * (sample - others[2])
                + (sample - others[0]) * (sample - others[1])
            ) / scaling
    return (values, slopes)


def apply_table(weights_1d, operand, stack_pos):
    return jnp.einsum(EINSUM_FORMS[stack_pos], weights_1d, operand, precision=lax.Precision.HIGHEST)


def split_axis(dof_field, axis_pos, stack_pos):
    elem_count = (dof_field.shape[axis_pos] - 1) // 3
    widths = [(0, 0)] * dof_field.ndim
    widths[axis_pos] = (0, 2)
    padded = jnp.pad(dof_field, widths)
    shaped = padded.reshape(
        dof_field.shape[:axis_pos] + (elem_count + 1, 3) + dof_field.shape[axis_pos + 1 :]
    )
    lower_rows = lax.slice_in_dim(shaped, 0, elem_count, axis=axis_pos)
    upper_rows = lax.slice_in_dim(shaped, 1, elem_count + 1, axis=axis_pos)
    pieces = [lax.index_in_dim(lower_rows, k, axis_pos + 1, keepdims=False) for k in range(3)]
    pieces.append(lax.index_in_dim(upper_rows, 0, axis_pos + 1, keepdims=False))
    return jnp.stack(pieces, stack_pos)


def merge_axis(parts, axis_pos, stack_pos):
    pieces = [lax.index_in_dim(parts, k, stack_pos, keepdims=False) for k in range(4)]
    target = axis_pos - 1
    extent = pieces[0].shape
    elem_count = extent[target]
    ending = [(0, 0)] * len(extent)
    ending[target] = (0, 1)
    leading = [(0, 0)] * len(extent)
    leading[target] = (1, 0)
    head_piece = jnp.pad(pieces[0], ending) + jnp.pad(pieces[3], leading)
    stacked = jnp.stack(
        [head_piece, jnp.pad(pieces[1], ending), jnp.pad(pieces[2], ending)], target + 1
    )
    merged = stacked.reshape(extent[:target] + (3 * (elem_count + 1),) + extent[target + 1 :])
    return lax.slice_in_dim(merged, 0, 3 * elem_count + 1, axis=target)


def element_action(elements, pointwise):
    table_pair = gauss_tables()
    values = jnp.asarray(table_pair[0], jnp.float32)
    slopes = jnp.asarray(table_pair[1], jnp.float32)
    coeffs = pointwise.astype(jnp.float32)
    x_value = apply_table(values, elements, 0)
    x_slope = apply_table(slopes, elements, 0)
    value_value = apply_table(values, x_value, 1)
    value_slope = apply_table(slopes, x_value, 1)
    slope_value = apply_table(values, x_slope, 1)
    point_value = apply_table(values, value_value, 2)
    grad_z = apply_table(slopes, value_value, 2)
    grad_y = apply_table(values, value_slope, 2)
    grad_x = apply_table(values, slope_value, 2)
    flux_x = coeffs[1] * grad_x + coeffs[4] * grad_y + coeffs[5] * grad_z
    flux_y = coeffs[4] * grad_x + coeffs[2] * grad_y + coeffs[6] * grad_z
    flux_z = coeffs[5] * grad_x + coeffs[6] * grad_y + coeffs[3] * grad_z
    mass_term = coeffs[0] * point_value
    back_plain = apply_table(values.T, mass_term, 2) + apply_table(slopes.T, flux_z, 2)
    back_fluxx = apply_table(values.T, flux_x, 2)
    back_fluxy = apply_table(values.T, flux_y, 2)
    near_sum = apply_table(values.T, back_plain, 1) + apply_table(slopes.T, back_fluxy, 1)
    far_sum = apply_table(values.T, back_fluxx, 1)
    return apply_table(values.T, near_sum, 0) + apply_table(slopes.T, far_sum, 0)


def diagonal_action(pointwise):
    table_pair = gauss_tables()
    values = jnp.asarray(table_pair[0], jnp.float32)
    slopes = jnp.asarray(table_pair[1], jnp.float32)
    coeffs = pointwise.astype(jnp.float32)
    square_v = values * values
    square_s = slopes * slopes
    mixed_vs = values * slopes

    def triple(table_x, table_y, table_z, term):
        return apply_table(table_x.T, apply_table(table_y.T, apply_table(table_z.T, term, 2), 1), 0)

    running_total = triple(square_v, square_v, square_v, coeffs[0])
    running_total = running_total + triple(square_s, square_v, square_v, coeffs[1])
    running_total = running_total + triple(square_v, square_s, square_v, coeffs[2])
    running_total = running_total + triple(square_v, square_v, square_s, coeffs[3])
    running_total = running_total + 2.0 * triple(mixed_vs, mixed_vs, square_v, coeffs[4])
    running_total = running_total + 2.0 * triple(mixed_vs, square_v, mixed_vs, coeffs[5])
    running_total = running_total + 2.0 * triple(square_v, mixed_vs, mixed_vs, coeffs[6])
    return running_total


def to_dofs(parts):
    return merge_axis(merge_axis(merge_axis(parts, 5, 2), 3, 1), 1, 0)


def element_block(dof_block, pointwise):
    elements = split_axis(split_axis(split_axis(dof_block, 0, 0), 2, 1), 4, 2)
    return to_dofs(element_action(elements, pointwise))


def banded(table, count):
    band = np.zeros((3 * count + 1, 4, count))
    for index in range(count):
        band[3 * index : 3 * index + 4, :, index] = table.T
    return band


def planar(table_x, table_y, count_x, count_y):
    kron = np.einsum("xpi,yqj->piqjxy", banded(table_x, count_x), banded(table_y, count_y))
    return jnp.asarray(kron.reshape(16 * count_x * count_y, -1), jnp.float32)


def long_axis(table, count, anchor):
    shape = (3 * count + 1, 4, count)
    offset = lax.broadcasted_iota(jnp.int32, shape, 0) - 3 * lax.broadcasted_iota(jnp.int32, shape, 2)
    offset = offset + anchor
    band = jnp.zeros(shape, jnp.float32)
    for node in range(4):
        column = jnp.asarray(table[:, node], jnp.float32)[None, :, None]
        band = band + jnp.where(offset == node, column, 0.0)
    return band.reshape(3 * count + 1, 4 * count)


def mat(left, right):
    return jnp.matmul(left, right, precision=lax.Precision.HIGHEST)


def point_layout(pointwise):
    count_x, count_y, count_z = pointwise.shape[4:]
    coeffs = pointwise.astype(jnp.float32).transpose(0, 1, 4, 2, 5, 3, 6)
    return coeffs.reshape(7, 16 * count_x * count_y, 4 * count_z)


def band_operator(field, coeffs, counts, anchor):
    count_x, count_y, count_z = counts
    values, slopes = gauss_tables()
    plain = planar(values, values, count_x, count_y)
    along_x = planar(slopes, values, count_x, count_y)
    along_y = planar(values, slopes, count_x, count_y)
    z_tables = jnp.concatenate([long_axis(values, count_z, anchor), long_axis(slopes, count_z, anchor)], 1)
    rows = field.shape[0] * field.shape[1]
    width = 4 * count_z
    through_z = mat(field.reshape(rows, field.shape[2]), z_tables)
    z_value = through_z[:, :width]
    point_value = mat(plain, z_value)
    grad_x = mat(along_x, z_value)
    grad_y = mat(along_y, z_value)
    grad_z = mat(plain, through_z[:, width:])
    flux_x = coeffs[1] * grad_x + coeffs[4] * grad_y + coeffs[5] * grad_z
    flux_y = coeffs[4] * grad_x + coeffs[2] * grad_y + coeffs[6] * grad_z
    flux_z = coeffs[5] * grad_x + coeffs[6] * grad_y + coeffs[3] * grad_z
    mass_term = coeffs[0] * point_value
    backward = jnp.concatenate([plain, along_x, along_y], 0).T
    near = mat(backward, jnp.concatenate([mass_term, flux_x, flux_y], 0))
    far = mat(plain.T, flux_z)
    merged = mat(jnp.concatenate([near, far], 1), z_tables.T)
    return merged.reshape(field.shape)


def band_diagonal(coeffs, counts, anchor):
    count_x, count_y, count_z = counts
    values, slopes = gauss_tables()
    square_v = values * values
    square_s = slopes * slopes
    mixed = values * slopes
    groups = [
        (square_v, [(square_v, square_v, 0, 1.0), (square_s, square_v, 1, 1.0),
                    (square_v, square_s, 2, 1.0), (mixed, mixed, 4, 2.0)]),
        (square_s, [(square_v, square_v, 3, 1.0)]),
        (mixed, [(mixed, square_v, 5, 2.0), (square_v, mixed, 6, 2.0)]),
    ]
    total = 0.0
    for z_table, members in groups:
        inner = 0.0
        for table_x, table_y, entry, factor in members:
            inner = inner + mat(factor * planar(table_x, table_y, count_x, count_y).T, coeffs[entry])
        total = total + mat(inner, long_axis(z_table, count_z, anchor).T)
    return total.reshape(3 * count_x + 1, 3 * count_y + 1, 3 * count_z + 1)


def upper_x(plane):
    return shifted(plane, BX, -1)


def upper_y(plane):
    return shifted(plane, BY, -1)


def lower_x(plane):
    return shifted(plane, BX, 1)


def lower_y(plane):
    return shifted(plane, BY, 1)


def exchange(local, rows_x, rows_y):
    from_below = lower_y(local[:, rows_y:])
    from_above = upper_y(local[:, 0:1])
    local = jnp.concatenate(
        [local[:, 0:1] + from_below, local[:, 1:rows_y], local[:, rows_y:] + from_above], 1
    )
    from_below = lower_x(local[rows_x:])
    from_above = upper_x(local[0:1])
    return jnp.concatenate(
        [local[0:1] + from_below, local[1:rows_x], local[rows_x:] + from_above], 0
    )


def global_sums(terms):
    return (over_axes(terms[0], BX_BY), over_axes(terms[1], BX_BY))


def widen(dof_field):
    widened = jnp.concatenate([dof_field, upper_x(dof_field[0:1])], 0)
    widened = jnp.concatenate([widened, upper_y(widened[:, 0:1])], 1)
    return widened


def pad_top(dof_field):
    return jnp.pad(dof_field, ((0, 0), (0, 0), (0, 1)))


def collect(contributions, rows_x, rows_y, rows_z):
    summed = contributions[:, :, :rows_z]
    arrived = lower_y(summed[:, rows_y:])
    summed = jnp.concatenate([summed[:, 0:1] + arrived, summed[:, 1:rows_y]], 1)
    arrived = lower_x(summed[rows_x:])
    summed = jnp.concatenate([summed[0:1] + arrived, summed[1:rows_x]], 0)
    return summed


def shards(cotangent, pointwise):
    rows_x, rows_y, rows_z = cotangent.shape
    total_x = rows_x * lax.axis_size(BX)
    total_y = rows_y * lax.axis_size(BY)
    extent = cotangent.shape
    place_x = lax.broadcasted_iota(jnp.int32, extent, 0) + lax.axis_index(BX) * rows_x
    place_y = lax.broadcasted_iota(jnp.int32, extent, 1) + lax.axis_index(BY) * rows_y
    place_z = lax.broadcasted_iota(jnp.int32, extent, 2)
    inside = (
        (place_x > 0) & (place_y > 0) & (place_z > 0) & (place_x < total_x) & (place_y < total_y)
    )
    interior = jnp.where(inside, 1.0, 0.0).astype(jnp.float32)
    wide_extent = (rows_x + 1, rows_y + 1, rows_z)
    wide_x = lax.broadcasted_iota(jnp.int32, wide_extent, 0) + lax.axis_index(BX) * rows_x
    wide_y = lax.broadcasted_iota(jnp.int32, wide_extent, 1) + lax.axis_index(BY) * rows_y
    wide_z = lax.broadcasted_iota(jnp.int32, wide_extent, 2)
    wide_inside = (
        (wide_x > 0) & (wide_y > 0) & (wide_z > 0) & (wide_x < total_x) & (wide_y < total_y)
    )
    wide_interior = jnp.where(wide_inside, 1.0, 0.0).astype(jnp.float32)
    counts = pointwise.shape[4:]
    coeffs = point_layout(pointwise)
    anchor = (cotangent[0, 0, 0] * 0.0).astype(jnp.int32)
    residual = cotangent * interior
    wide_residual = widen(residual)
    wide_diagonal = exchange(band_diagonal(coeffs, counts, anchor)[:, :, :rows_z], rows_x, rows_y)
    diagonal = wide_diagonal[:rows_x, :rows_y]

    def contributions(wide_field):
        return band_operator(pad_top(wide_field), coeffs, counts, anchor)[:, :, :rows_z]

    wide_precond = wide_residual / wide_diagonal
    precond = wide_precond[:rows_x, :rows_y]
    wide_image = exchange(contributions(wide_precond), rows_x, rows_y) * wide_interior
    image = wide_image[:rows_x, :rows_y]
    wide_scaled = wide_image / wide_diagonal
    scaled = wide_scaled[:rows_x, :rows_y]
    second = collect(contributions(wide_scaled), rows_x, rows_y, rows_z) * interior
    products = jnp.stack(
        [
            residual * precond,
            precond * image,
            residual * scaled,
            image * scaled,
            precond * second,
            scaled * second,
        ]
    )
    terms = jnp.sum(products.reshape(6, -1, products.shape[-1]), axis=(1, 2))
    summed = over_axes(terms, BX_BY)
    rz_now, curvature, cross_r, cross_q, cross_z, curvature_w = [summed[k] for k in range(6)]
    alpha = rz_now / curvature
    fresh = rz_now - alpha * cross_r - alpha * curvature + alpha * alpha * cross_q
    ratio = fresh / rz_now
    grow = 1.0 + ratio
    next_curvature = (
        grow * grow * curvature - alpha * grow * (cross_z + cross_q) + alpha * alpha * curvature_w
    )
    next_alpha = fresh / next_curvature
    residual = residual - alpha * image
    direction = residual / diagonal + ratio * precond
    direction_image = image - alpha * second + ratio * image
    adjoint = alpha * precond + next_alpha * direction
    residual = residual - next_alpha * direction_image
    return (adjoint, residual)


def solution(mesh):
    split = Mesh(mesh.devices.reshape(4, 3, 4, 8, 2), ("bx_0", "bx_1", "by_0", "by_1", "by_2"))
    in_specs = (P(BX, BY, None), P(None, None, None, None, BX, BY, None))
    out_specs = (P(BX, BY, None), P(BX, BY, None))
    return jax.shard_map(
        shards, mesh=split, in_specs=in_specs, out_specs=out_specs, check_vma=False
    )
```

```python
import math

import jax
import jax.numpy as jnp
import numpy as np
from jax import lax
from jax.sharding import Mesh
from jax.sharding import PartitionSpec as P

ITERS = 2
BX = ("bx_0", "bx_1")
BY = ("by_0", "by_1", "by_2")
BX_BY = ("bx_0", "bx_1", "by_0", "by_1", "by_2")


EINSUM_FORMS = ("pa,abcxyz->pbcxyz", "pb,abcxyz->apcxyz", "pc,abcxyz->abpxyz")


def shifted(value, axis, steps):
    count = lax.axis_size(axis)
    initial, last = (max(0, -steps), min(count, count - steps))
    return lax.ppermute(value, axis, [(source, source + steps) for source in range(initial, last)])


def over_axes(value, axes):
    for axis in axes:
        value = lax.psum(value, axis)
    return value


def gauss_tables():
    inner_point = math.sqrt(3.0 / 7.0 - 2.0 / 7.0 * math.sqrt(6.0 / 5.0))
    outer_point = math.sqrt(3.0 / 7.0 + 2.0 / 7.0 * math.sqrt(6.0 / 5.0))
    points = [-outer_point, -inner_point, inner_point, outer_point]
    lobatto = [-1.0, -1.0 / math.sqrt(5.0), 1.0 / math.sqrt(5.0), 1.0]
    values = np.zeros((4, 4))
    slopes = np.zeros((4, 4))
    for a in range(4):
        others = [lobatto[k] for k in range(4) if k != a]
        scaling = (lobatto[a] - others[0]) * (lobatto[a] - others[1]) * (lobatto[a] - others[2])
        for q in range(4):
            sample = points[q]
            values[q, a] = (
                (sample - others[0]) * (sample - others[1]) * (sample - others[2]) / scaling
            )
            slopes[q, a] = (
                (sample - others[1]) * (sample - others[2])
                + (sample - others[0]) * (sample - others[2])
                + (sample - others[0]) * (sample - others[1])
            ) / scaling
    return (values, slopes)


def apply_table(weights_1d, operand, stack_pos):
    return jnp.einsum(EINSUM_FORMS[stack_pos], weights_1d, operand, precision=lax.Precision.HIGHEST)


def split_axis(dof_field, axis_pos, stack_pos):
    elem_count = (dof_field.shape[axis_pos] - 1) // 3
    widths = [(0, 0)] * dof_field.ndim
    widths[axis_pos] = (0, 2)
    padded = jnp.pad(dof_field, widths)
    shaped = padded.reshape(
        dof_field.shape[:axis_pos] + (elem_count + 1, 3) + dof_field.shape[axis_pos + 1 :]
    )
    lower_rows = lax.slice_in_dim(shaped, 0, elem_count, axis=axis_pos)
    upper_rows = lax.slice_in_dim(shaped, 1, elem_count + 1, axis=axis_pos)
    pieces = [lax.index_in_dim(lower_rows, k, axis_pos + 1, keepdims=False) for k in range(3)]
    pieces.append(lax.index_in_dim(upper_rows, 0, axis_pos + 1, keepdims=False))
    return jnp.stack(pieces, stack_pos)


def merge_axis(parts, axis_pos, stack_pos):
    pieces = [lax.index_in_dim(parts, k, stack_pos, keepdims=False) for k in range(4)]
    target = axis_pos - 1
    extent = pieces[0].shape
    elem_count = extent[target]
    ending = [(0, 0)] * len(extent)
    ending[target] = (0, 1)
    leading = [(0, 0)] * len(extent)
    leading[target] = (1, 0)
    head_piece = jnp.pad(pieces[0], ending) + jnp.pad(pieces[3], leading)
    stacked = jnp.stack(
        [head_piece, jnp.pad(pieces[1], ending), jnp.pad(pieces[2], ending)], target + 1
    )
    merged = stacked.reshape(extent[:target] + (3 * (elem_count + 1),) + extent[target + 1 :])
    return lax.slice_in_dim(merged, 0, 3 * elem_count + 1, axis=target)


def element_action(elements, pointwise):
    table_pair = gauss_tables()
    values = jnp.asarray(table_pair[0], jnp.float32)
    slopes = jnp.asarray(table_pair[1], jnp.float32)
    coeffs = pointwise.astype(jnp.float32)
    x_value = apply_table(values, elements, 0)
    x_slope = apply_table(slopes, elements, 0)
    value_value = apply_table(values, x_value, 1)
    value_slope = apply_table(slopes, x_value, 1)
    slope_value = apply_table(values, x_slope, 1)
    point_value = apply_table(values, value_value, 2)
    grad_z = apply_table(slopes, value_value, 2)
    grad_y = apply_table(values, value_slope, 2)
    grad_x = apply_table(values, slope_value, 2)
    flux_x = coeffs[1] * grad_x + coeffs[4] * grad_y + coeffs[5] * grad_z
    flux_y = coeffs[4] * grad_x + coeffs[2] * grad_y + coeffs[6] * grad_z
    flux_z = coeffs[5] * grad_x + coeffs[6] * grad_y + coeffs[3] * grad_z
    mass_term = coeffs[0] * point_value
    back_plain = apply_table(values.T, mass_term, 2) + apply_table(slopes.T, flux_z, 2)
    back_fluxx = apply_table(values.T, flux_x, 2)
    back_fluxy = apply_table(values.T, flux_y, 2)
    near_sum = apply_table(values.T, back_plain, 1) + apply_table(slopes.T, back_fluxy, 1)
    far_sum = apply_table(values.T, back_fluxx, 1)
    return apply_table(values.T, near_sum, 0) + apply_table(slopes.T, far_sum, 0)


def diagonal_action(pointwise):
    table_pair = gauss_tables()
    values = jnp.asarray(table_pair[0], jnp.float32)
    slopes = jnp.asarray(table_pair[1], jnp.float32)
    coeffs = pointwise.astype(jnp.float32)
    square_v = values * values
    square_s = slopes * slopes
    mixed_vs = values * slopes

    def triple(table_x, table_y, table_z, term):
        return apply_table(table_x.T, apply_table(table_y.T, apply_table(table_z.T, term, 2), 1), 0)

    running_total = triple(square_v, square_v, square_v, coeffs[0])
    running_total = running_total + triple(square_s, square_v, square_v, coeffs[1])
    running_total = running_total + triple(square_v, square_s, square_v, coeffs[2])
    running_total = running_total + triple(square_v, square_v, square_s, coeffs[3])
    running_total = running_total + 2.0 * triple(mixed_vs, mixed_vs, square_v, coeffs[4])
    running_total = running_total + 2.0 * triple(mixed_vs, square_v, mixed_vs, coeffs[5])
    running_total = running_total + 2.0 * triple(square_v, mixed_vs, mixed_vs, coeffs[6])
    return running_total


def to_dofs(parts):
    return merge_axis(merge_axis(merge_axis(parts, 5, 2), 3, 1), 1, 0)


def element_block(dof_block, pointwise):
    elements = split_axis(split_axis(split_axis(dof_block, 0, 0), 2, 1), 4, 2)
    return to_dofs(element_action(elements, pointwise))


def banded(table, count):
    band = np.zeros((3 * count + 1, 4, count))
    for index in range(count):
        band[3 * index : 3 * index + 4, :, index] = table.T
    return band


def planar(table_x, table_y, count_x, count_y):
    kron = np.einsum("xpi,yqj->piqjxy", banded(table_x, count_x), banded(table_y, count_y))
    return jnp.asarray(kron.reshape(16 * count_x * count_y, -1), jnp.float32)


def long_axis(table, count, anchor):
    shape = (3 * count + 1, 4, count)
    offset = lax.broadcasted_iota(jnp.int32, shape, 0) - 3 * lax.broadcasted_iota(jnp.int32, shape, 2)
    offset = offset + anchor
    band = jnp.zeros(shape, jnp.float32)
    for node in range(4):
        column = jnp.asarray(table[:, node], jnp.float32)[None, :, None]
        band = band + jnp.where(offset == node, column, 0.0)
    return band.reshape(3 * count + 1, 4 * count)


def mat(left, right):
    return jnp.matmul(left, right, precision=lax.Precision.HIGHEST)


def point_layout(pointwise):
    count_x, count_y, count_z = pointwise.shape[4:]
    coeffs = pointwise.astype(jnp.float32).transpose(0, 1, 4, 2, 5, 3, 6)
    return coeffs.reshape(7, 16 * count_x * count_y, 4 * count_z)


def band_operator(field, coeffs, counts, anchor):
    count_x, count_y, count_z = counts
    values, slopes = gauss_tables()
    plain = planar(values, values, count_x, count_y)
    along_x = planar(slopes, values, count_x, count_y)
    along_y = planar(values, slopes, count_x, count_y)
    z_tables = jnp.concatenate([long_axis(values, count_z, anchor), long_axis(slopes, count_z, anchor)], 1)
    rows = field.shape[0] * field.shape[1]
    width = 4 * count_z
    through_z = mat(field.reshape(rows, field.shape[2]), z_tables)
    z_value = through_z[:, :width]
    point_value = mat(plain, z_value)
    grad_x = mat(along_x, z_value)
    grad_y = mat(along_y, z_value)
    grad_z = mat(plain, through_z[:, width:])
    flux_x = coeffs[1] * grad_x + coeffs[4] * grad_y + coeffs[5] * grad_z
    flux_y = coeffs[4] * grad_x + coeffs[2] * grad_y + coeffs[6] * grad_z
    flux_z = coeffs[5] * grad_x + coeffs[6] * grad_y + coeffs[3] * grad_z
    mass_term = coeffs[0] * point_value
    backward = jnp.concatenate([plain, along_x, along_y], 0).T
    near = mat(backward, jnp.concatenate([mass_term, flux_x, flux_y], 0))
    far = mat(plain.T, flux_z)
    merged = mat(jnp.concatenate([near, far], 1), z_tables.T)
    return merged.reshape(field.shape)


def band_diagonal(coeffs, counts, anchor):
    count_x, count_y, count_z = counts
    values, slopes = gauss_tables()
    square_v = values * values
    square_s = slopes * slopes
    mixed = values * slopes
    groups = [
        (square_v, [(square_v, square_v, 0, 1.0), (square_s, square_v, 1, 1.0),
                    (square_v, square_s, 2, 1.0), (mixed, mixed, 4, 2.0)]),
        (square_s, [(square_v, square_v, 3, 1.0)]),
        (mixed, [(mixed, square_v, 5, 2.0), (square_v, mixed, 6, 2.0)]),
    ]
    total = 0.0
    for z_table, members in groups:
        inner = 0.0
        for table_x, table_y, entry, factor in members:
            inner = inner + mat(factor * planar(table_x, table_y, count_x, count_y).T, coeffs[entry])
        total = total + mat(inner, long_axis(z_table, count_z, anchor).T)
    return total.reshape(3 * count_x + 1, 3 * count_y + 1, 3 * count_z + 1)


def upper_x(plane):
    return shifted(plane, BX, -1)


def upper_y(plane):
    return shifted(plane, BY, -1)


def lower_x(plane):
    return shifted(plane, BX, 1)


def lower_y(plane):
    return shifted(plane, BY, 1)


def moved(value, steps_x, steps_y):
    count_x = lax.axis_size(BX)
    count_y = lax.axis_size(BY)
    pairs = []
    for source_x in range(count_x):
        for source_y in range(count_y):
            target_x, target_y = source_x + steps_x, source_y + steps_y
            if 0 <= target_x < count_x and 0 <= target_y < count_y:
                pairs.append((source_x * count_y + source_y, target_x * count_y + target_y))
    return lax.ppermute(value, BX_BY, pairs)


def gather_contributions(contributions, rows_x, rows_y, rows_z):
    own = contributions[:rows_x, :rows_y, :rows_z]
    from_x = lower_x(contributions[rows_x:, :rows_y, :rows_z])
    from_y = lower_y(contributions[:rows_x, rows_y:, :rows_z])
    from_corner = moved(contributions[rows_x:, rows_y:, :rows_z], 1, 1)
    head = own[0:1] + from_x
    head = jnp.concatenate([head[:, 0:1] + from_corner, head[:, 1:]], 1)
    own = jnp.concatenate([head, own[1:]], 0)
    return jnp.concatenate([own[:, 0:1] + from_y, own[:, 1:]], 1)


def global_sums(terms):
    return (over_axes(terms[0], BX_BY), over_axes(terms[1], BX_BY))


def widen(dof_field):
    widened = jnp.concatenate([dof_field, upper_x(dof_field[0:1])], 0)
    widened = jnp.concatenate([widened, upper_y(widened[:, 0:1])], 1)
    return widened


def pad_top(dof_field):
    return jnp.pad(dof_field, ((0, 0), (0, 0), (0, 1)))


def collect(contributions, rows_x, rows_y, rows_z):
    summed = contributions[:, :, :rows_z]
    arrived = lower_y(summed[:, rows_y:])
    summed = jnp.concatenate([summed[:, 0:1] + arrived, summed[:, 1:rows_y]], 1)
    arrived = lower_x(summed[rows_x:])
    summed = jnp.concatenate([summed[0:1] + arrived, summed[1:rows_x]], 0)
    return summed


def shards(cotangent, pointwise):
    rows_x, rows_y, rows_z = cotangent.shape
    total_x = rows_x * lax.axis_size(BX)
    total_y = rows_y * lax.axis_size(BY)
    extent = cotangent.shape
    place_x = lax.broadcasted_iota(jnp.int32, extent, 0) + lax.axis_index(BX) * rows_x
    place_y = lax.broadcasted_iota(jnp.int32, extent, 1) + lax.axis_index(BY) * rows_y
    place_z = lax.broadcasted_iota(jnp.int32, extent, 2)
    inside = (
        (place_x > 0) & (place_y > 0) & (place_z > 0) & (place_x < total_x) & (place_y < total_y)
    )
    interior = jnp.where(inside, 1.0, 0.0).astype(jnp.float32)
    counts = pointwise.shape[4:]
    coeffs = point_layout(pointwise)
    anchor = (cotangent[0, 0, 0] * 0.0).astype(jnp.int32)
    diagonal = collect(band_diagonal(coeffs, counts, anchor), rows_x, rows_y, rows_z)

    wide_extent = (rows_x + 1, rows_y + 1, rows_z)
    wide_x = lax.broadcasted_iota(jnp.int32, wide_extent, 0) + lax.axis_index(BX) * rows_x
    wide_y = lax.broadcasted_iota(jnp.int32, wide_extent, 1) + lax.axis_index(BY) * rows_y
    wide_z = lax.broadcasted_iota(jnp.int32, wide_extent, 2)
    wide_inside = (
        (wide_x > 0) & (wide_y > 0) & (wide_z > 0) & (wide_x < total_x) & (wide_y < total_y)
    )
    wide_interior = jnp.where(wide_inside, 1.0, 0.0).astype(jnp.float32)

    def contributions(wide_field):
        return band_operator(pad_top(wide_field), coeffs, counts, anchor)[:, :, :rows_z]

    def local_dot(left, right):
        return jnp.sum(left * right)

    residual = cotangent * interior
    precond = residual / diagonal
    wide_precond = widen(precond)
    image = collect(contributions(wide_precond), rows_x, rows_y, rows_z) * interior
    scaled = image / diagonal
    wide_scaled = widen(scaled)
    raw_second = contributions(wide_scaled)
    masked_second = raw_second * wide_interior
    products = jnp.stack(
        [residual * precond, precond * image, residual * scaled, image * scaled]
    )
    wide_products = jnp.stack([wide_precond * masked_second, wide_scaled * masked_second])
    terms = jnp.concatenate(
        [
            jnp.sum(products.reshape(4, -1, products.shape[-1]), axis=(1, 2)),
            jnp.sum(wide_products.reshape(2, -1, wide_products.shape[-1]), axis=(1, 2)),
        ]
    )
    second = gather_contributions(raw_second, rows_x, rows_y, rows_z) * interior
    summed = over_axes(terms, BX_BY)
    rz_now, curvature, cross_r, cross_q, cross_z, curvature_w = [summed[k] for k in range(6)]
    alpha = rz_now / curvature
    fresh = rz_now - alpha * cross_r - alpha * curvature + alpha * alpha * cross_q
    ratio = fresh / rz_now
    grow = 1.0 + ratio
    next_curvature = (
        grow * grow * curvature - alpha * grow * (cross_z + cross_q) + alpha * alpha * curvature_w
    )
    next_alpha = fresh / next_curvature
    residual = residual - alpha * image
    direction = residual / diagonal + ratio * precond
    direction_image = image - alpha * second + ratio * image
    adjoint = alpha * precond + next_alpha * direction
    residual = residual - next_alpha * direction_image
    return (adjoint, residual)


def solution(mesh):
    split = Mesh(mesh.devices.reshape(4, 3, 4, 8, 2), ("bx_0", "bx_1", "by_0", "by_1", "by_2"))
    in_specs = (P(BX, BY, None), P(None, None, None, None, BX, BY, None))
    out_specs = (P(BX, BY, None), P(BX, BY, None))
    return jax.shard_map(
        shards, mesh=split, in_specs=in_specs, out_specs=out_specs, check_vma=False
    )
```

```python
import math

import jax
import jax.numpy as jnp
import numpy as np
from jax import lax
from jax.sharding import Mesh
from jax.sharding import PartitionSpec as P

ITERS = 2
BX = ("bx_0", "bx_1")
BY = ("by_0", "by_1", "by_2")
BX_BY = ("bx_0", "bx_1", "by_0", "by_1", "by_2")


EINSUM_FORMS = ("pa,abcxyz->pbcxyz", "pb,abcxyz->apcxyz", "pc,abcxyz->abpxyz")


def shifted(value, axis, steps):
    count = lax.axis_size(axis)
    initial, last = (max(0, -steps), min(count, count - steps))
    return lax.ppermute(value, axis, [(source, source + steps) for source in range(initial, last)])


def over_axes(value, axes):
    for axis in axes:
        value = lax.psum(value, axis)
    return value


def gauss_tables():
    inner_point = math.sqrt(3.0 / 7.0 - 2.0 / 7.0 * math.sqrt(6.0 / 5.0))
    outer_point = math.sqrt(3.0 / 7.0 + 2.0 / 7.0 * math.sqrt(6.0 / 5.0))
    points = [-outer_point, -inner_point, inner_point, outer_point]
    lobatto = [-1.0, -1.0 / math.sqrt(5.0), 1.0 / math.sqrt(5.0), 1.0]
    values = np.zeros((4, 4))
    slopes = np.zeros((4, 4))
    for a in range(4):
        others = [lobatto[k] for k in range(4) if k != a]
        scaling = (lobatto[a] - others[0]) * (lobatto[a] - others[1]) * (lobatto[a] - others[2])
        for q in range(4):
            sample = points[q]
            values[q, a] = (
                (sample - others[0]) * (sample - others[1]) * (sample - others[2]) / scaling
            )
            slopes[q, a] = (
                (sample - others[1]) * (sample - others[2])
                + (sample - others[0]) * (sample - others[2])
                + (sample - others[0]) * (sample - others[1])
            ) / scaling
    return (values, slopes)


def apply_table(weights_1d, operand, stack_pos):
    return jnp.einsum(EINSUM_FORMS[stack_pos], weights_1d, operand, precision=lax.Precision.HIGHEST)


def split_axis(dof_field, axis_pos, stack_pos):
    elem_count = (dof_field.shape[axis_pos] - 1) // 3
    widths = [(0, 0)] * dof_field.ndim
    widths[axis_pos] = (0, 2)
    padded = jnp.pad(dof_field, widths)
    shaped = padded.reshape(
        dof_field.shape[:axis_pos] + (elem_count + 1, 3) + dof_field.shape[axis_pos + 1 :]
    )
    lower_rows = lax.slice_in_dim(shaped, 0, elem_count, axis=axis_pos)
    upper_rows = lax.slice_in_dim(shaped, 1, elem_count + 1, axis=axis_pos)
    pieces = [lax.index_in_dim(lower_rows, k, axis_pos + 1, keepdims=False) for k in range(3)]
    pieces.append(lax.index_in_dim(upper_rows, 0, axis_pos + 1, keepdims=False))
    return jnp.stack(pieces, stack_pos)


def merge_axis(parts, axis_pos, stack_pos):
    pieces = [lax.index_in_dim(parts, k, stack_pos, keepdims=False) for k in range(4)]
    target = axis_pos - 1
    extent = pieces[0].shape
    elem_count = extent[target]
    ending = [(0, 0)] * len(extent)
    ending[target] = (0, 1)
    leading = [(0, 0)] * len(extent)
    leading[target] = (1, 0)
    head_piece = jnp.pad(pieces[0], ending) + jnp.pad(pieces[3], leading)
    stacked = jnp.stack(
        [head_piece, jnp.pad(pieces[1], ending), jnp.pad(pieces[2], ending)], target + 1
    )
    merged = stacked.reshape(extent[:target] + (3 * (elem_count + 1),) + extent[target + 1 :])
    return lax.slice_in_dim(merged, 0, 3 * elem_count + 1, axis=target)


def element_action(elements, pointwise):
    table_pair = gauss_tables()
    values = jnp.asarray(table_pair[0], jnp.float32)
    slopes = jnp.asarray(table_pair[1], jnp.float32)
    coeffs = pointwise.astype(jnp.float32)
    x_value = apply_table(values, elements, 0)
    x_slope = apply_table(slopes, elements, 0)
    value_value = apply_table(values, x_value, 1)
    value_slope = apply_table(slopes, x_value, 1)
    slope_value = apply_table(values, x_slope, 1)
    point_value = apply_table(values, value_value, 2)
    grad_z = apply_table(slopes, value_value, 2)
    grad_y = apply_table(values, value_slope, 2)
    grad_x = apply_table(values, slope_value, 2)
    flux_x = coeffs[1] * grad_x + coeffs[4] * grad_y + coeffs[5] * grad_z
    flux_y = coeffs[4] * grad_x + coeffs[2] * grad_y + coeffs[6] * grad_z
    flux_z = coeffs[5] * grad_x + coeffs[6] * grad_y + coeffs[3] * grad_z
    mass_term = coeffs[0] * point_value
    back_plain = apply_table(values.T, mass_term, 2) + apply_table(slopes.T, flux_z, 2)
    back_fluxx = apply_table(values.T, flux_x, 2)
    back_fluxy = apply_table(values.T, flux_y, 2)
    near_sum = apply_table(values.T, back_plain, 1) + apply_table(slopes.T, back_fluxy, 1)
    far_sum = apply_table(values.T, back_fluxx, 1)
    return apply_table(values.T, near_sum, 0) + apply_table(slopes.T, far_sum, 0)


def diagonal_action(pointwise):
    table_pair = gauss_tables()
    values = jnp.asarray(table_pair[0], jnp.float32)
    slopes = jnp.asarray(table_pair[1], jnp.float32)
    coeffs = pointwise.astype(jnp.float32)
    square_v = values * values
    square_s = slopes * slopes
    mixed_vs = values * slopes

    def triple(table_x, table_y, table_z, term):
        return apply_table(table_x.T, apply_table(table_y.T, apply_table(table_z.T, term, 2), 1), 0)

    running_total = triple(square_v, square_v, square_v, coeffs[0])
    running_total = running_total + triple(square_s, square_v, square_v, coeffs[1])
    running_total = running_total + triple(square_v, square_s, square_v, coeffs[2])
    running_total = running_total + triple(square_v, square_v, square_s, coeffs[3])
    running_total = running_total + 2.0 * triple(mixed_vs, mixed_vs, square_v, coeffs[4])
    running_total = running_total + 2.0 * triple(mixed_vs, square_v, mixed_vs, coeffs[5])
    running_total = running_total + 2.0 * triple(square_v, mixed_vs, mixed_vs, coeffs[6])
    return running_total


def to_dofs(parts):
    return merge_axis(merge_axis(merge_axis(parts, 5, 2), 3, 1), 1, 0)


def element_block(dof_block, pointwise):
    elements = split_axis(split_axis(split_axis(dof_block, 0, 0), 2, 1), 4, 2)
    return to_dofs(element_action(elements, pointwise))


def banded(table, count):
    band = np.zeros((3 * count + 1, 4, count))
    for index in range(count):
        band[3 * index : 3 * index + 4, :, index] = table.T
    return band


def planar(table_x, table_y, count_x, count_y):
    kron = np.einsum("xpi,yqj->piqjxy", banded(table_x, count_x), banded(table_y, count_y))
    return jnp.asarray(kron.reshape(16 * count_x * count_y, -1), jnp.float32)


def long_axis(table, count, anchor):
    shape = (3 * count + 1, 4, count)
    offset = lax.broadcasted_iota(jnp.int32, shape, 0) - 3 * lax.broadcasted_iota(jnp.int32, shape, 2)
    offset = offset + anchor
    band = jnp.zeros(shape, jnp.float32)
    for node in range(4):
        column = jnp.asarray(table[:, node], jnp.float32)[None, :, None]
        band = band + jnp.where(offset == node, column, 0.0)
    return band.reshape(3 * count + 1, 4 * count)


def mat(left, right):
    return jnp.matmul(left, right, precision=lax.Precision.HIGHEST)


def point_layout(pointwise):
    count_x, count_y, count_z = pointwise.shape[4:]
    coeffs = pointwise.astype(jnp.float32).transpose(0, 1, 4, 2, 5, 3, 6)
    return coeffs.reshape(7, 16 * count_x * count_y, 4 * count_z)


def band_operator(field, coeffs, counts, anchor):
    count_x, count_y, count_z = counts
    values, slopes = gauss_tables()
    plain = planar(values, values, count_x, count_y)
    along_x = planar(slopes, values, count_x, count_y)
    along_y = planar(values, slopes, count_x, count_y)
    z_tables = jnp.concatenate([long_axis(values, count_z, anchor), long_axis(slopes, count_z, anchor)], 1)
    rows = field.shape[0] * field.shape[1]
    width = 4 * count_z
    through_z = mat(field.reshape(rows, field.shape[2]), z_tables)
    z_value = through_z[:, :width]
    point_value = mat(plain, z_value)
    grad_x = mat(along_x, z_value)
    grad_y = mat(along_y, z_value)
    grad_z = mat(plain, through_z[:, width:])
    flux_x = coeffs[1] * grad_x + coeffs[4] * grad_y + coeffs[5] * grad_z
    flux_y = coeffs[4] * grad_x + coeffs[2] * grad_y + coeffs[6] * grad_z
    flux_z = coeffs[5] * grad_x + coeffs[6] * grad_y + coeffs[3] * grad_z
    mass_term = coeffs[0] * point_value
    backward = jnp.concatenate([plain, along_x, along_y], 0).T
    near = mat(backward, jnp.concatenate([mass_term, flux_x, flux_y], 0))
    far = mat(plain.T, flux_z)
    merged = mat(jnp.concatenate([near, far], 1), z_tables.T)
    return merged.reshape(field.shape)


def band_diagonal(coeffs, counts, anchor):
    count_x, count_y, count_z = counts
    values, slopes = gauss_tables()
    square_v = values * values
    square_s = slopes * slopes
    mixed = values * slopes
    groups = [
        (square_v, [(square_v, square_v, 0, 1.0), (square_s, square_v, 1, 1.0),
                    (square_v, square_s, 2, 1.0), (mixed, mixed, 4, 2.0)]),
        (square_s, [(square_v, square_v, 3, 1.0)]),
        (mixed, [(mixed, square_v, 5, 2.0), (square_v, mixed, 6, 2.0)]),
    ]
    total = 0.0
    for z_table, members in groups:
        inner = 0.0
        for table_x, table_y, entry, factor in members:
            inner = inner + mat(factor * planar(table_x, table_y, count_x, count_y).T, coeffs[entry])
        total = total + mat(inner, long_axis(z_table, count_z, anchor).T)
    return total.reshape(3 * count_x + 1, 3 * count_y + 1, 3 * count_z + 1)


def upper_x(plane):
    return shifted(plane, BX, -1)


def upper_y(plane):
    return shifted(plane, BY, -1)


def lower_x(plane):
    return shifted(plane, BX, 1)


def lower_y(plane):
    return shifted(plane, BY, 1)


def global_sums(terms):
    return (over_axes(terms[0], BX_BY), over_axes(terms[1], BX_BY))


def widen(dof_field):
    widened = jnp.concatenate([dof_field, upper_x(dof_field[0:1])], 0)
    widened = jnp.concatenate([widened, upper_y(widened[:, 0:1])], 1)
    return widened


def pad_top(dof_field):
    return jnp.pad(dof_field, ((0, 0), (0, 0), (0, 1)))


def collect(contributions, rows_x, rows_y, rows_z):
    summed = contributions[:, :, :rows_z]
    arrived = lower_y(summed[:, rows_y:])
    summed = jnp.concatenate([summed[:, 0:1] + arrived, summed[:, 1:rows_y]], 1)
    arrived = lower_x(summed[rows_x:])
    summed = jnp.concatenate([summed[0:1] + arrived, summed[1:rows_x]], 0)
    return summed


def shards(cotangent, pointwise):
    rows_x, rows_y, rows_z = cotangent.shape
    total_x = rows_x * lax.axis_size(BX)
    total_y = rows_y * lax.axis_size(BY)
    extent = cotangent.shape
    place_x = lax.broadcasted_iota(jnp.int32, extent, 0) + lax.axis_index(BX) * rows_x
    place_y = lax.broadcasted_iota(jnp.int32, extent, 1) + lax.axis_index(BY) * rows_y
    place_z = lax.broadcasted_iota(jnp.int32, extent, 2)
    inside = (
        (place_x > 0) & (place_y > 0) & (place_z > 0) & (place_x < total_x) & (place_y < total_y)
    )
    interior = jnp.where(inside, 1.0, 0.0).astype(jnp.float32)
    counts = pointwise.shape[4:]
    coeffs = point_layout(pointwise)
    anchor = (cotangent[0, 0, 0] * 0.0).astype(jnp.int32)
    diagonal = collect(band_diagonal(coeffs, counts, anchor), rows_x, rows_y, rows_z)

    wide_extent = (rows_x + 1, rows_y + 1, rows_z)
    wide_x = lax.broadcasted_iota(jnp.int32, wide_extent, 0) + lax.axis_index(BX) * rows_x
    wide_y = lax.broadcasted_iota(jnp.int32, wide_extent, 1) + lax.axis_index(BY) * rows_y
    wide_z = lax.broadcasted_iota(jnp.int32, wide_extent, 2)
    wide_inside = (
        (wide_x > 0) & (wide_y > 0) & (wide_z > 0) & (wide_x < total_x) & (wide_y < total_y)
    )
    wide_interior = jnp.where(wide_inside, 1.0, 0.0).astype(jnp.float32)

    def contributions(wide_field):
        return band_operator(pad_top(wide_field), coeffs, counts, anchor)[:, :, :rows_z]

    def local_dot(left, right):
        return jnp.sum(left * right)

    residual = cotangent * interior
    precond = residual / diagonal
    wide_precond = widen(precond)
    image = collect(contributions(wide_precond), rows_x, rows_y, rows_z) * interior
    scaled = image / diagonal
    wide_scaled = widen(scaled)
    raw_second = contributions(wide_scaled)
    masked_second = raw_second * wide_interior
    products = jnp.stack(
        [residual * precond, precond * image, residual * scaled, image * scaled]
    )
    wide_products = jnp.stack([wide_precond * masked_second, wide_scaled * masked_second])
    terms = jnp.concatenate(
        [
            jnp.sum(products.reshape(4, -1, products.shape[-1]), axis=(1, 2)),
            jnp.sum(wide_products.reshape(2, -1, wide_products.shape[-1]), axis=(1, 2)),
        ]
    )
    arrived = lower_x(raw_second[rows_x:])
    partial = jnp.concatenate([raw_second[0:1] + arrived, raw_second[1:rows_x]], 0)
    summed = lax.psum(terms, BX_BY[0])
    summed, partial = lax.optimization_barrier((summed, partial))
    arrived = lower_y(partial[:, rows_y:])
    second = jnp.concatenate([partial[:, 0:1] + arrived, partial[:, 1:rows_y]], 1) * interior
    summed = lax.psum(summed, BX_BY[1])
    summed, second = lax.optimization_barrier((summed, second))
    for axis in BX_BY[2:]:
        summed = lax.psum(summed, axis)
    rz_now, curvature, cross_r, cross_q, cross_z, curvature_w = [summed[k] for k in range(6)]
    alpha = rz_now / curvature
    fresh = rz_now - alpha * cross_r - alpha * curvature + alpha * alpha * cross_q
    ratio = fresh / rz_now
    grow = 1.0 + ratio
    next_curvature = (
        grow * grow * curvature - alpha * grow * (cross_z + cross_q) + alpha * alpha * curvature_w
    )
    next_alpha = fresh / next_curvature
    residual = residual - alpha * image
    direction = residual / diagonal + ratio * precond
    direction_image = image - alpha * second + ratio * image
    adjoint = alpha * precond + next_alpha * direction
    residual = residual - next_alpha * direction_image
    return (adjoint, residual)


def solution(mesh):
    split = Mesh(mesh.devices.reshape(4, 3, 4, 8, 2), ("bx_0", "bx_1", "by_0", "by_1", "by_2"))
    in_specs = (P(BX, BY, None), P(None, None, None, None, BX, BY, None))
    out_specs = (P(BX, BY, None), P(BX, BY, None))
    return jax.shard_map(
        shards, mesh=split, in_specs=in_specs, out_specs=out_specs, check_vma=False
    )
```

```python
import math

import jax
import jax.numpy as jnp
import numpy as np
from jax import lax
from jax.sharding import Mesh
from jax.sharding import PartitionSpec as P

ITERS = 2
BX = ("bx_0", "bx_1")
BY = ("by_0", "by_1", "by_2")
BX_BY = ("bx_0", "bx_1", "by_0", "by_1", "by_2")


EINSUM_FORMS = ("pa,abcxyz->pbcxyz", "pb,abcxyz->apcxyz", "pc,abcxyz->abpxyz")


def shifted(value, axis, steps):
    count = lax.axis_size(axis)
    initial, last = (max(0, -steps), min(count, count - steps))
    return lax.ppermute(value, axis, [(source, source + steps) for source in range(initial, last)])


def over_axes(value, axes):
    for axis in axes:
        value = lax.psum(value, axis)
    return value


def gauss_tables():
    inner_point = math.sqrt(3.0 / 7.0 - 2.0 / 7.0 * math.sqrt(6.0 / 5.0))
    outer_point = math.sqrt(3.0 / 7.0 + 2.0 / 7.0 * math.sqrt(6.0 / 5.0))
    points = [-outer_point, -inner_point, inner_point, outer_point]
    lobatto = [-1.0, -1.0 / math.sqrt(5.0), 1.0 / math.sqrt(5.0), 1.0]
    values = np.zeros((4, 4))
    slopes = np.zeros((4, 4))
    for a in range(4):
        others = [lobatto[k] for k in range(4) if k != a]
        scaling = (lobatto[a] - others[0]) * (lobatto[a] - others[1]) * (lobatto[a] - others[2])
        for q in range(4):
            sample = points[q]
            values[q, a] = (
                (sample - others[0]) * (sample - others[1]) * (sample - others[2]) / scaling
            )
            slopes[q, a] = (
                (sample - others[1]) * (sample - others[2])
                + (sample - others[0]) * (sample - others[2])
                + (sample - others[0]) * (sample - others[1])
            ) / scaling
    return (values, slopes)


def apply_table(weights_1d, operand, stack_pos):
    return jnp.einsum(EINSUM_FORMS[stack_pos], weights_1d, operand, precision=lax.Precision.HIGHEST)


def split_axis(dof_field, axis_pos, stack_pos):
    elem_count = (dof_field.shape[axis_pos] - 1) // 3
    widths = [(0, 0)] * dof_field.ndim
    widths[axis_pos] = (0, 2)
    padded = jnp.pad(dof_field, widths)
    shaped = padded.reshape(
        dof_field.shape[:axis_pos] + (elem_count + 1, 3) + dof_field.shape[axis_pos + 1 :]
    )
    lower_rows = lax.slice_in_dim(shaped, 0, elem_count, axis=axis_pos)
    upper_rows = lax.slice_in_dim(shaped, 1, elem_count + 1, axis=axis_pos)
    pieces = [lax.index_in_dim(lower_rows, k, axis_pos + 1, keepdims=False) for k in range(3)]
    pieces.append(lax.index_in_dim(upper_rows, 0, axis_pos + 1, keepdims=False))
    return jnp.stack(pieces, stack_pos)


def merge_axis(parts, axis_pos, stack_pos):
    pieces = [lax.index_in_dim(parts, k, stack_pos, keepdims=False) for k in range(4)]
    target = axis_pos - 1
    extent = pieces[0].shape
    elem_count = extent[target]
    ending = [(0, 0)] * len(extent)
    ending[target] = (0, 1)
    leading = [(0, 0)] * len(extent)
    leading[target] = (1, 0)
    head_piece = jnp.pad(pieces[0], ending) + jnp.pad(pieces[3], leading)
    stacked = jnp.stack(
        [head_piece, jnp.pad(pieces[1], ending), jnp.pad(pieces[2], ending)], target + 1
    )
    merged = stacked.reshape(extent[:target] + (3 * (elem_count + 1),) + extent[target + 1 :])
    return lax.slice_in_dim(merged, 0, 3 * elem_count + 1, axis=target)


def element_action(elements, pointwise):
    table_pair = gauss_tables()
    values = jnp.asarray(table_pair[0], jnp.float32)
    slopes = jnp.asarray(table_pair[1], jnp.float32)
    coeffs = pointwise.astype(jnp.float32)
    x_value = apply_table(values, elements, 0)
    x_slope = apply_table(slopes, elements, 0)
    value_value = apply_table(values, x_value, 1)
    value_slope = apply_table(slopes, x_value, 1)
    slope_value = apply_table(values, x_slope, 1)
    point_value = apply_table(values, value_value, 2)
    grad_z = apply_table(slopes, value_value, 2)
    grad_y = apply_table(values, value_slope, 2)
    grad_x = apply_table(values, slope_value, 2)
    flux_x = coeffs[1] * grad_x + coeffs[4] * grad_y + coeffs[5] * grad_z
    flux_y = coeffs[4] * grad_x + coeffs[2] * grad_y + coeffs[6] * grad_z
    flux_z = coeffs[5] * grad_x + coeffs[6] * grad_y + coeffs[3] * grad_z
    mass_term = coeffs[0] * point_value
    back_plain = apply_table(values.T, mass_term, 2) + apply_table(slopes.T, flux_z, 2)
    back_fluxx = apply_table(values.T, flux_x, 2)
    back_fluxy = apply_table(values.T, flux_y, 2)
    near_sum = apply_table(values.T, back_plain, 1) + apply_table(slopes.T, back_fluxy, 1)
    far_sum = apply_table(values.T, back_fluxx, 1)
    return apply_table(values.T, near_sum, 0) + apply_table(slopes.T, far_sum, 0)


def diagonal_action(pointwise):
    table_pair = gauss_tables()
    values = jnp.asarray(table_pair[0], jnp.float32)
    slopes = jnp.asarray(table_pair[1], jnp.float32)
    coeffs = pointwise.astype(jnp.float32)
    square_v = values * values
    square_s = slopes * slopes
    mixed_vs = values * slopes

    def triple(table_x, table_y, table_z, term):
        return apply_table(table_x.T, apply_table(table_y.T, apply_table(table_z.T, term, 2), 1), 0)

    running_total = triple(square_v, square_v, square_v, coeffs[0])
    running_total = running_total + triple(square_s, square_v, square_v, coeffs[1])
    running_total = running_total + triple(square_v, square_s, square_v, coeffs[2])
    running_total = running_total + triple(square_v, square_v, square_s, coeffs[3])
    running_total = running_total + 2.0 * triple(mixed_vs, mixed_vs, square_v, coeffs[4])
    running_total = running_total + 2.0 * triple(mixed_vs, square_v, mixed_vs, coeffs[5])
    running_total = running_total + 2.0 * triple(square_v, mixed_vs, mixed_vs, coeffs[6])
    return running_total


def to_dofs(parts):
    return merge_axis(merge_axis(merge_axis(parts, 5, 2), 3, 1), 1, 0)


def element_block(dof_block, pointwise):
    elements = split_axis(split_axis(split_axis(dof_block, 0, 0), 2, 1), 4, 2)
    return to_dofs(element_action(elements, pointwise))


def banded(table, count):
    band = np.zeros((3 * count + 1, 4, count))
    for index in range(count):
        band[3 * index : 3 * index + 4, :, index] = table.T
    return band


def planar(table_x, table_y, count_x, count_y):
    kron = np.einsum("xpi,yqj->piqjxy", banded(table_x, count_x), banded(table_y, count_y))
    return jnp.asarray(kron.reshape(16 * count_x * count_y, -1), jnp.float32)


def long_axis(table, count, anchor):
    shape = (3 * count + 1, 4, count)
    offset = lax.broadcasted_iota(jnp.int32, shape, 0) - 3 * lax.broadcasted_iota(jnp.int32, shape, 2)
    offset = offset + anchor
    band = jnp.zeros(shape, jnp.float32)
    for node in range(4):
        column = jnp.asarray(table[:, node], jnp.float32)[None, :, None]
        band = band + jnp.where(offset == node, column, 0.0)
    return band.reshape(3 * count + 1, 4 * count)


def mat(left, right):
    return jnp.matmul(left, right, precision=lax.Precision.HIGHEST)


def point_layout(pointwise):
    count_x, count_y, count_z = pointwise.shape[4:]
    coeffs = pointwise.astype(jnp.float32).transpose(0, 1, 4, 2, 5, 3, 6)
    return coeffs.reshape(7, 16 * count_x * count_y, 4 * count_z)


def band_operator(field, coeffs, counts, anchor):
    count_x, count_y, count_z = counts
    values, slopes = gauss_tables()
    plain = planar(values, values, count_x, count_y)
    along_x = planar(slopes, values, count_x, count_y)
    along_y = planar(values, slopes, count_x, count_y)
    z_tables = jnp.concatenate([long_axis(values, count_z, anchor), long_axis(slopes, count_z, anchor)], 1)
    rows = field.shape[0] * field.shape[1]
    width = 4 * count_z
    through_z = mat(field.reshape(rows, field.shape[2]), z_tables)
    z_value = through_z[:, :width]
    point_value = mat(plain, z_value)
    grad_x = mat(along_x, z_value)
    grad_y = mat(along_y, z_value)
    grad_z = mat(plain, through_z[:, width:])
    flux_x = coeffs[1] * grad_x + coeffs[4] * grad_y + coeffs[5] * grad_z
    flux_y = coeffs[4] * grad_x + coeffs[2] * grad_y + coeffs[6] * grad_z
    flux_z = coeffs[5] * grad_x + coeffs[6] * grad_y + coeffs[3] * grad_z
    mass_term = coeffs[0] * point_value
    backward = jnp.concatenate([plain, along_x, along_y], 0).T
    near = mat(backward, jnp.concatenate([mass_term, flux_x, flux_y], 0))
    far = mat(plain.T, flux_z)
    merged = mat(jnp.concatenate([near, far], 1), z_tables.T)
    return merged.reshape(field.shape)


def band_diagonal(coeffs, counts, anchor):
    count_x, count_y, count_z = counts
    values, slopes = gauss_tables()
    square_v = values * values
    square_s = slopes * slopes
    mixed = values * slopes
    groups = [
        (square_v, [(square_v, square_v, 0, 1.0), (square_s, square_v, 1, 1.0),
                    (square_v, square_s, 2, 1.0), (mixed, mixed, 4, 2.0)]),
        (square_s, [(square_v, square_v, 3, 1.0)]),
        (mixed, [(mixed, square_v, 5, 2.0), (square_v, mixed, 6, 2.0)]),
    ]
    total = 0.0
    for z_table, members in groups:
        inner = 0.0
        for table_x, table_y, entry, factor in members:
            inner = inner + mat(factor * planar(table_x, table_y, count_x, count_y).T, coeffs[entry])
        total = total + mat(inner, long_axis(z_table, count_z, anchor).T)
    return total.reshape(3 * count_x + 1, 3 * count_y + 1, 3 * count_z + 1)


def upper_x(plane):
    return shifted(plane, BX, -1)


def upper_y(plane):
    return shifted(plane, BY, -1)


def lower_x(plane):
    return shifted(plane, BX, 1)


def lower_y(plane):
    return shifted(plane, BY, 1)


def global_sums(terms):
    return (over_axes(terms[0], BX_BY), over_axes(terms[1], BX_BY))


def widen(dof_field):
    widened = jnp.concatenate([dof_field, upper_x(dof_field[0:1])], 0)
    widened = jnp.concatenate([widened, upper_y(widened[:, 0:1])], 1)
    return widened


def pad_top(dof_field):
    return jnp.pad(dof_field, ((0, 0), (0, 0), (0, 1)))


def collect(contributions, rows_x, rows_y, rows_z):
    summed = contributions[:, :, :rows_z]
    arrived = lower_y(summed[:, rows_y:])
    summed = jnp.concatenate([summed[:, 0:1] + arrived, summed[:, 1:rows_y]], 1)
    arrived = lower_x(summed[rows_x:])
    summed = jnp.concatenate([summed[0:1] + arrived, summed[1:rows_x]], 0)
    return summed


def shards(cotangent, pointwise):
    rows_x, rows_y, rows_z = cotangent.shape
    total_x = rows_x * lax.axis_size(BX)
    total_y = rows_y * lax.axis_size(BY)
    extent = cotangent.shape
    place_x = lax.broadcasted_iota(jnp.int32, extent, 0) + lax.axis_index(BX) * rows_x
    place_y = lax.broadcasted_iota(jnp.int32, extent, 1) + lax.axis_index(BY) * rows_y
    place_z = lax.broadcasted_iota(jnp.int32, extent, 2)
    inside = (
        (place_x > 0) & (place_y > 0) & (place_z > 0) & (place_x < total_x) & (place_y < total_y)
    )
    interior = jnp.where(inside, 1.0, 0.0).astype(jnp.float32)
    counts = pointwise.shape[4:]
    coeffs = point_layout(pointwise)
    anchor = (cotangent[0, 0, 0] * 0.0).astype(jnp.int32)
    diagonal = collect(band_diagonal(coeffs, counts, anchor), rows_x, rows_y, rows_z)

    wide_extent = (rows_x + 1, rows_y + 1, rows_z)
    wide_x = lax.broadcasted_iota(jnp.int32, wide_extent, 0) + lax.axis_index(BX) * rows_x
    wide_y = lax.broadcasted_iota(jnp.int32, wide_extent, 1) + lax.axis_index(BY) * rows_y
    wide_z = lax.broadcasted_iota(jnp.int32, wide_extent, 2)
    wide_inside = (
        (wide_x > 0) & (wide_y > 0) & (wide_z > 0) & (wide_x < total_x) & (wide_y < total_y)
    )
    wide_interior = jnp.where(wide_inside, 1.0, 0.0).astype(jnp.float32)

    def contributions(wide_field):
        return band_operator(pad_top(wide_field), coeffs, counts, anchor)[:, :, :rows_z]

    def local_dot(left, right):
        return jnp.sum(left * right)

    residual = cotangent * interior
    precond = residual / diagonal
    wide_precond = widen(precond)
    image = collect(contributions(wide_precond), rows_x, rows_y, rows_z) * interior
    scaled = image / diagonal
    wide_scaled = widen(scaled)
    raw_second = contributions(wide_scaled)
    masked_second = raw_second * wide_interior
    products = jnp.stack(
        [residual * precond, precond * image, residual * scaled, image * scaled]
    )
    wide_products = jnp.stack([wide_precond * masked_second, wide_scaled * masked_second])
    terms = jnp.concatenate(
        [
            jnp.sum(products.reshape(4, -1, products.shape[-1]), axis=(1, 2)),
            jnp.sum(wide_products.reshape(2, -1, wide_products.shape[-1]), axis=(1, 2)),
        ]
    )
    arrived = lower_x(raw_second[rows_x:])
    partial = jnp.concatenate([raw_second[0:1] + arrived, raw_second[1:rows_x]], 0)
    summed = lax.psum(terms, BX_BY[0])
    summed, partial = lax.optimization_barrier((summed, partial))
    arrived = lower_y(partial[:, rows_y:])
    second = jnp.concatenate([partial[:, 0:1] + arrived, partial[:, 1:rows_y]], 1) * interior
    summed = lax.psum(summed, BX_BY[1])
    summed, second = lax.optimization_barrier((summed, second))
    for axis in BX_BY[2:]:
        summed = lax.psum(summed, axis)
    parts = lax.optimization_barrier(jnp.broadcast_to(summed[:, None, None, None], (6, 1, 1, rows_z)))
    rz_now, curvature, cross_r, cross_q, cross_z, curvature_w = [parts[k] for k in range(6)]
    alpha = rz_now / curvature
    fresh = rz_now - alpha * cross_r - alpha * curvature + alpha * alpha * cross_q
    ratio = fresh / rz_now
    grow = 1.0 + ratio
    next_curvature = (
        grow * grow * curvature - alpha * grow * (cross_z + cross_q) + alpha * alpha * curvature_w
    )
    next_alpha = fresh / next_curvature
    residual = residual - alpha * image
    direction = residual / diagonal + ratio * precond
    direction_image = image - alpha * second + ratio * image
    adjoint = alpha * precond + next_alpha * direction
    residual = residual - next_alpha * direction_image
    return (adjoint, residual)


def solution(mesh):
    split = Mesh(mesh.devices.reshape(4, 3, 4, 8, 2), ("bx_0", "bx_1", "by_0", "by_1", "by_2"))
    in_specs = (P(BX, BY, None), P(None, None, None, None, BX, BY, None))
    out_specs = (P(BX, BY, None), P(BX, BY, None))
    return jax.shard_map(
        shards, mesh=split, in_specs=in_specs, out_specs=out_specs, check_vma=False
    )
```

```python
import math

import jax
import jax.numpy as jnp
import numpy as np
from jax import lax
from jax.sharding import Mesh
from jax.sharding import PartitionSpec as P

ITERS = 2
BX = ("bx_0", "bx_1")
BY = ("by_0", "by_1", "by_2")
BX_BY = ("bx_0", "bx_1", "by_0", "by_1", "by_2")


EINSUM_FORMS = ("pa,abcxyz->pbcxyz", "pb,abcxyz->apcxyz", "pc,abcxyz->abpxyz")


def shifted(value, axis, steps):
    count = lax.axis_size(axis)
    initial, last = (max(0, -steps), min(count, count - steps))
    return lax.ppermute(value, axis, [(source, source + steps) for source in range(initial, last)])


def over_axes(value, axes):
    for axis in axes:
        value = lax.psum(value, axis)
    return value


def gauss_tables():
    inner_point = math.sqrt(3.0 / 7.0 - 2.0 / 7.0 * math.sqrt(6.0 / 5.0))
    outer_point = math.sqrt(3.0 / 7.0 + 2.0 / 7.0 * math.sqrt(6.0 / 5.0))
    points = [-outer_point, -inner_point, inner_point, outer_point]
    lobatto = [-1.0, -1.0 / math.sqrt(5.0), 1.0 / math.sqrt(5.0), 1.0]
    values = np.zeros((4, 4))
    slopes = np.zeros((4, 4))
    for a in range(4):
        others = [lobatto[k] for k in range(4) if k != a]
        scaling = (lobatto[a] - others[0]) * (lobatto[a] - others[1]) * (lobatto[a] - others[2])
        for q in range(4):
            sample = points[q]
            values[q, a] = (
                (sample - others[0]) * (sample - others[1]) * (sample - others[2]) / scaling
            )
            slopes[q, a] = (
                (sample - others[1]) * (sample - others[2])
                + (sample - others[0]) * (sample - others[2])
                + (sample - others[0]) * (sample - others[1])
            ) / scaling
    return (values, slopes)


def apply_table(weights_1d, operand, stack_pos):
    return jnp.einsum(EINSUM_FORMS[stack_pos], weights_1d, operand, precision=lax.Precision.HIGHEST)


def split_axis(dof_field, axis_pos, stack_pos):
    elem_count = (dof_field.shape[axis_pos] - 1) // 3
    widths = [(0, 0)] * dof_field.ndim
    widths[axis_pos] = (0, 2)
    padded = jnp.pad(dof_field, widths)
    shaped = padded.reshape(
        dof_field.shape[:axis_pos] + (elem_count + 1, 3) + dof_field.shape[axis_pos + 1 :]
    )
    lower_rows = lax.slice_in_dim(shaped, 0, elem_count, axis=axis_pos)
    upper_rows = lax.slice_in_dim(shaped, 1, elem_count + 1, axis=axis_pos)
    pieces = [lax.index_in_dim(lower_rows, k, axis_pos + 1, keepdims=False) for k in range(3)]
    pieces.append(lax.index_in_dim(upper_rows, 0, axis_pos + 1, keepdims=False))
    return jnp.stack(pieces, stack_pos)


def merge_axis(parts, axis_pos, stack_pos):
    pieces = [lax.index_in_dim(parts, k, stack_pos, keepdims=False) for k in range(4)]
    target = axis_pos - 1
    extent = pieces[0].shape
    elem_count = extent[target]
    ending = [(0, 0)] * len(extent)
    ending[target] = (0, 1)
    leading = [(0, 0)] * len(extent)
    leading[target] = (1, 0)
    head_piece = jnp.pad(pieces[0], ending) + jnp.pad(pieces[3], leading)
    stacked = jnp.stack(
        [head_piece, jnp.pad(pieces[1], ending), jnp.pad(pieces[2], ending)], target + 1
    )
    merged = stacked.reshape(extent[:target] + (3 * (elem_count + 1),) + extent[target + 1 :])
    return lax.slice_in_dim(merged, 0, 3 * elem_count + 1, axis=target)


def element_action(elements, pointwise):
    table_pair = gauss_tables()
    values = jnp.asarray(table_pair[0], jnp.float32)
    slopes = jnp.asarray(table_pair[1], jnp.float32)
    coeffs = pointwise.astype(jnp.float32)
    x_value = apply_table(values, elements, 0)
    x_slope = apply_table(slopes, elements, 0)
    value_value = apply_table(values, x_value, 1)
    value_slope = apply_table(slopes, x_value, 1)
    slope_value = apply_table(values, x_slope, 1)
    point_value = apply_table(values, value_value, 2)
    grad_z = apply_table(slopes, value_value, 2)
    grad_y = apply_table(values, value_slope, 2)
    grad_x = apply_table(values, slope_value, 2)
    flux_x = coeffs[1] * grad_x + coeffs[4] * grad_y + coeffs[5] * grad_z
    flux_y = coeffs[4] * grad_x + coeffs[2] * grad_y + coeffs[6] * grad_z
    flux_z = coeffs[5] * grad_x + coeffs[6] * grad_y + coeffs[3] * grad_z
    mass_term = coeffs[0] * point_value
    back_plain = apply_table(values.T, mass_term, 2) + apply_table(slopes.T, flux_z, 2)
    back_fluxx = apply_table(values.T, flux_x, 2)
    back_fluxy = apply_table(values.T, flux_y, 2)
    near_sum = apply_table(values.T, back_plain, 1) + apply_table(slopes.T, back_fluxy, 1)
    far_sum = apply_table(values.T, back_fluxx, 1)
    return apply_table(values.T, near_sum, 0) + apply_table(slopes.T, far_sum, 0)


def diagonal_action(pointwise):
    table_pair = gauss_tables()
    values = jnp.asarray(table_pair[0], jnp.float32)
    slopes = jnp.asarray(table_pair[1], jnp.float32)
    coeffs = pointwise.astype(jnp.float32)
    square_v = values * values
    square_s = slopes * slopes
    mixed_vs = values * slopes

    def triple(table_x, table_y, table_z, term):
        return apply_table(table_x.T, apply_table(table_y.T, apply_table(table_z.T, term, 2), 1), 0)

    running_total = triple(square_v, square_v, square_v, coeffs[0])
    running_total = running_total + triple(square_s, square_v, square_v, coeffs[1])
    running_total = running_total + triple(square_v, square_s, square_v, coeffs[2])
    running_total = running_total + triple(square_v, square_v, square_s, coeffs[3])
    running_total = running_total + 2.0 * triple(mixed_vs, mixed_vs, square_v, coeffs[4])
    running_total = running_total + 2.0 * triple(mixed_vs, square_v, mixed_vs, coeffs[5])
    running_total = running_total + 2.0 * triple(square_v, mixed_vs, mixed_vs, coeffs[6])
    return running_total


def to_dofs(parts):
    return merge_axis(merge_axis(merge_axis(parts, 5, 2), 3, 1), 1, 0)


def element_block(dof_block, pointwise):
    elements = split_axis(split_axis(split_axis(dof_block, 0, 0), 2, 1), 4, 2)
    return to_dofs(element_action(elements, pointwise))


def banded(table, count):
    band = np.zeros((3 * count + 1, 4, count))
    for index in range(count):
        band[3 * index : 3 * index + 4, :, index] = table.T
    return band


def planar(table_x, table_y, count_x, count_y):
    kron = np.einsum("xpi,yqj->piqjxy", banded(table_x, count_x), banded(table_y, count_y))
    return jnp.asarray(kron.reshape(16 * count_x * count_y, -1), jnp.float32)


def long_axis(table, count, anchor):
    shape = (3 * count + 1, 4, count)
    offset = lax.broadcasted_iota(jnp.int32, shape, 0) - 3 * lax.broadcasted_iota(jnp.int32, shape, 2)
    offset = offset + anchor
    band = jnp.zeros(shape, jnp.float32)
    for node in range(4):
        column = jnp.asarray(table[:, node], jnp.float32)[None, :, None]
        band = band + jnp.where(offset == node, column, 0.0)
    return band.reshape(3 * count + 1, 4 * count)


def mat(left, right):
    return jnp.matmul(left, right, precision=lax.Precision.HIGH)


def point_layout(pointwise):
    count_x, count_y, count_z = pointwise.shape[4:]
    coeffs = pointwise.astype(jnp.float32).transpose(0, 1, 4, 2, 5, 3, 6)
    return coeffs.reshape(7, 16 * count_x * count_y, 4 * count_z)


def band_operator(field, coeffs, counts, anchor):
    count_x, count_y, count_z = counts
    values, slopes = gauss_tables()
    plain = planar(values, values, count_x, count_y)
    along_x = planar(slopes, values, count_x, count_y)
    along_y = planar(values, slopes, count_x, count_y)
    z_tables = jnp.concatenate([long_axis(values, count_z, anchor), long_axis(slopes, count_z, anchor)], 1)
    rows = field.shape[0] * field.shape[1]
    width = 4 * count_z
    through_z = mat(field.reshape(rows, field.shape[2]), z_tables)
    z_value = through_z[:, :width]
    point_value = mat(plain, z_value)
    grad_x = mat(along_x, z_value)
    grad_y = mat(along_y, z_value)
    grad_z = mat(plain, through_z[:, width:])
    flux_x = coeffs[1] * grad_x + coeffs[4] * grad_y + coeffs[5] * grad_z
    flux_y = coeffs[4] * grad_x + coeffs[2] * grad_y + coeffs[6] * grad_z
    flux_z = coeffs[5] * grad_x + coeffs[6] * grad_y + coeffs[3] * grad_z
    mass_term = coeffs[0] * point_value
    backward = jnp.concatenate([plain, along_x, along_y], 0).T
    near = mat(backward, jnp.concatenate([mass_term, flux_x, flux_y], 0))
    far = mat(plain.T, flux_z)
    merged = mat(jnp.concatenate([near, far], 1), z_tables.T)
    return merged.reshape(field.shape)


def band_diagonal(coeffs, counts, anchor):
    count_x, count_y, count_z = counts
    values, slopes = gauss_tables()
    square_v = values * values
    square_s = slopes * slopes
    mixed = values * slopes
    groups = [
        (square_v, [(square_v, square_v, 0, 1.0), (square_s, square_v, 1, 1.0),
                    (square_v, square_s, 2, 1.0), (mixed, mixed, 4, 2.0)]),
        (square_s, [(square_v, square_v, 3, 1.0)]),
        (mixed, [(mixed, square_v, 5, 2.0), (square_v, mixed, 6, 2.0)]),
    ]
    total = 0.0
    for z_table, members in groups:
        inner = 0.0
        for table_x, table_y, entry, factor in members:
            inner = inner + mat(factor * planar(table_x, table_y, count_x, count_y).T, coeffs[entry])
        total = total + mat(inner, long_axis(z_table, count_z, anchor).T)
    return total.reshape(3 * count_x + 1, 3 * count_y + 1, 3 * count_z + 1)


def upper_x(plane):
    return shifted(plane, BX, -1)


def upper_y(plane):
    return shifted(plane, BY, -1)


def lower_x(plane):
    return shifted(plane, BX, 1)


def lower_y(plane):
    return shifted(plane, BY, 1)


def global_sums(terms):
    return (over_axes(terms[0], BX_BY), over_axes(terms[1], BX_BY))


def widen(dof_field):
    widened = jnp.concatenate([dof_field, upper_x(dof_field[0:1])], 0)
    widened = jnp.concatenate([widened, upper_y(widened[:, 0:1])], 1)
    return widened


def pad_top(dof_field):
    return jnp.pad(dof_field, ((0, 0), (0, 0), (0, 1)))


def collect(contributions, rows_x, rows_y, rows_z):
    summed = contributions[:, :, :rows_z]
    arrived = lower_y(summed[:, rows_y:])
    summed = jnp.concatenate([summed[:, 0:1] + arrived, summed[:, 1:rows_y]], 1)
    arrived = lower_x(summed[rows_x:])
    summed = jnp.concatenate([summed[0:1] + arrived, summed[1:rows_x]], 0)
    return summed


def shards(cotangent, pointwise):
    rows_x, rows_y, rows_z = cotangent.shape
    total_x = rows_x * lax.axis_size(BX)
    total_y = rows_y * lax.axis_size(BY)
    extent = cotangent.shape
    place_x = lax.broadcasted_iota(jnp.int32, extent, 0) + lax.axis_index(BX) * rows_x
    place_y = lax.broadcasted_iota(jnp.int32, extent, 1) + lax.axis_index(BY) * rows_y
    place_z = lax.broadcasted_iota(jnp.int32, extent, 2)
    inside = (
        (place_x > 0) & (place_y > 0) & (place_z > 0) & (place_x < total_x) & (place_y < total_y)
    )
    interior = jnp.where(inside, 1.0, 0.0).astype(jnp.float32)
    counts = pointwise.shape[4:]
    coeffs = point_layout(pointwise)
    anchor = (cotangent[0, 0, 0] * 0.0).astype(jnp.int32)
    diagonal = collect(band_diagonal(coeffs, counts, anchor), rows_x, rows_y, rows_z)

    wide_extent = (rows_x + 1, rows_y + 1, rows_z)
    wide_x = lax.broadcasted_iota(jnp.int32, wide_extent, 0) + lax.axis_index(BX) * rows_x
    wide_y = lax.broadcasted_iota(jnp.int32, wide_extent, 1) + lax.axis_index(BY) * rows_y
    wide_z = lax.broadcasted_iota(jnp.int32, wide_extent, 2)
    wide_inside = (
        (wide_x > 0) & (wide_y > 0) & (wide_z > 0) & (wide_x < total_x) & (wide_y < total_y)
    )
    wide_interior = jnp.where(wide_inside, 1.0, 0.0).astype(jnp.float32)

    def contributions(wide_field):
        return band_operator(pad_top(wide_field), coeffs, counts, anchor)[:, :, :rows_z]

    def local_dot(left, right):
        return jnp.sum(left * right)

    residual = cotangent * interior
    precond = residual / diagonal
    wide_precond = widen(precond)
    image = collect(contributions(wide_precond), rows_x, rows_y, rows_z) * interior
    scaled = image / diagonal
    wide_scaled = widen(scaled)
    raw_second = contributions(wide_scaled)
    masked_second = raw_second * wide_interior
    products = jnp.stack(
        [residual * precond, precond * image, residual * scaled, image * scaled]
    )
    wide_products = jnp.stack([wide_precond * masked_second, wide_scaled * masked_second])
    terms = jnp.concatenate(
        [
            jnp.sum(products.reshape(4, -1, products.shape[-1]), axis=(1, 2)),
            jnp.sum(wide_products.reshape(2, -1, wide_products.shape[-1]), axis=(1, 2)),
        ]
    )
    arrived = lower_x(raw_second[rows_x:])
    partial = jnp.concatenate([raw_second[0:1] + arrived, raw_second[1:rows_x]], 0)
    summed = lax.psum(terms, BX_BY[0])
    summed, partial = lax.optimization_barrier((summed, partial))
    arrived = lower_y(partial[:, rows_y:])
    second = jnp.concatenate([partial[:, 0:1] + arrived, partial[:, 1:rows_y]], 1) * interior
    summed = lax.psum(summed, BX_BY[1])
    summed, second = lax.optimization_barrier((summed, second))
    for axis in BX_BY[2:]:
        summed = lax.psum(summed, axis)
    parts = lax.optimization_barrier(jnp.broadcast_to(summed[:, None, None, None], (6, 1, 1, rows_z)))
    rz_now, curvature, cross_r, cross_q, cross_z, curvature_w = [parts[k] for k in range(6)]
    alpha = rz_now / curvature
    fresh = rz_now - alpha * cross_r - alpha * curvature + alpha * alpha * cross_q
    ratio = fresh / rz_now
    grow = 1.0 + ratio
    next_curvature = (
        grow * grow * curvature - alpha * grow * (cross_z + cross_q) + alpha * alpha * curvature_w
    )
    next_alpha = fresh / next_curvature
    residual = residual - alpha * image
    direction = residual / diagonal + ratio * precond
    direction_image = image - alpha * second + ratio * image
    adjoint = alpha * precond + next_alpha * direction
    residual = residual - next_alpha * direction_image
    return (adjoint, residual)


def solution(mesh):
    split = Mesh(mesh.devices.reshape(4, 3, 4, 8, 2), ("bx_0", "bx_1", "by_0", "by_1", "by_2"))
    in_specs = (P(BX, BY, None), P(None, None, None, None, BX, BY, None))
    out_specs = (P(BX, BY, None), P(BX, BY, None))
    return jax.shard_map(
        shards, mesh=split, in_specs=in_specs, out_specs=out_specs, check_vma=False
    )
```

```python
import math

import jax
import jax.numpy as jnp
import numpy as np
from jax import lax
from jax.sharding import Mesh
from jax.sharding import PartitionSpec as P

ITERS = 2
BX = ("bx_0", "bx_1")
BY = ("by_0", "by_1", "by_2")
BX_BY = ("bx_0", "bx_1", "by_0", "by_1", "by_2")


EINSUM_FORMS = ("pa,abcxyz->pbcxyz", "pb,abcxyz->apcxyz", "pc,abcxyz->abpxyz")


def shifted(value, axis, steps):
    count = lax.axis_size(axis)
    initial, last = (max(0, -steps), min(count, count - steps))
    return lax.ppermute(value, axis, [(source, source + steps) for source in range(initial, last)])


def over_axes(value, axes):
    for axis in axes:
        value = lax.psum(value, axis)
    return value


def gauss_tables():
    inner_point = math.sqrt(3.0 / 7.0 - 2.0 / 7.0 * math.sqrt(6.0 / 5.0))
    outer_point = math.sqrt(3.0 / 7.0 + 2.0 / 7.0 * math.sqrt(6.0 / 5.0))
    points = [-outer_point, -inner_point, inner_point, outer_point]
    lobatto = [-1.0, -1.0 / math.sqrt(5.0), 1.0 / math.sqrt(5.0), 1.0]
    values = np.zeros((4, 4))
    slopes = np.zeros((4, 4))
    for a in range(4):
        others = [lobatto[k] for k in range(4) if k != a]
        scaling = (lobatto[a] - others[0]) * (lobatto[a] - others[1]) * (lobatto[a] - others[2])
        for q in range(4):
            sample = points[q]
            values[q, a] = (
                (sample - others[0]) * (sample - others[1]) * (sample - others[2]) / scaling
            )
            slopes[q, a] = (
                (sample - others[1]) * (sample - others[2])
                + (sample - others[0]) * (sample - others[2])
                + (sample - others[0]) * (sample - others[1])
            ) / scaling
    return (values, slopes)


def apply_table(weights_1d, operand, stack_pos):
    return jnp.einsum(EINSUM_FORMS[stack_pos], weights_1d, operand, precision=lax.Precision.HIGHEST)


def split_axis(dof_field, axis_pos, stack_pos):
    elem_count = (dof_field.shape[axis_pos] - 1) // 3
    widths = [(0, 0)] * dof_field.ndim
    widths[axis_pos] = (0, 2)
    padded = jnp.pad(dof_field, widths)
    shaped = padded.reshape(
        dof_field.shape[:axis_pos] + (elem_count + 1, 3) + dof_field.shape[axis_pos + 1 :]
    )
    lower_rows = lax.slice_in_dim(shaped, 0, elem_count, axis=axis_pos)
    upper_rows = lax.slice_in_dim(shaped, 1, elem_count + 1, axis=axis_pos)
    pieces = [lax.index_in_dim(lower_rows, k, axis_pos + 1, keepdims=False) for k in range(3)]
    pieces.append(lax.index_in_dim(upper_rows, 0, axis_pos + 1, keepdims=False))
    return jnp.stack(pieces, stack_pos)


def merge_axis(parts, axis_pos, stack_pos):
    pieces = [lax.index_in_dim(parts, k, stack_pos, keepdims=False) for k in range(4)]
    target = axis_pos - 1
    extent = pieces[0].shape
    elem_count = extent[target]
    ending = [(0, 0)] * len(extent)
    ending[target] = (0, 1)
    leading = [(0, 0)] * len(extent)
    leading[target] = (1, 0)
    head_piece = jnp.pad(pieces[0], ending) + jnp.pad(pieces[3], leading)
    stacked = jnp.stack(
        [head_piece, jnp.pad(pieces[1], ending), jnp.pad(pieces[2], ending)], target + 1
    )
    merged = stacked.reshape(extent[:target] + (3 * (elem_count + 1),) + extent[target + 1 :])
    return lax.slice_in_dim(merged, 0, 3 * elem_count + 1, axis=target)


def element_action(elements, pointwise):
    table_pair = gauss_tables()
    values = jnp.asarray(table_pair[0], jnp.float32)
    slopes = jnp.asarray(table_pair[1], jnp.float32)
    coeffs = pointwise.astype(jnp.float32)
    x_value = apply_table(values, elements, 0)
    x_slope = apply_table(slopes, elements, 0)
    value_value = apply_table(values, x_value, 1)
    value_slope = apply_table(slopes, x_value, 1)
    slope_value = apply_table(values, x_slope, 1)
    point_value = apply_table(values, value_value, 2)
    grad_z = apply_table(slopes, value_value, 2)
    grad_y = apply_table(values, value_slope, 2)
    grad_x = apply_table(values, slope_value, 2)
    flux_x = coeffs[1] * grad_x + coeffs[4] * grad_y + coeffs[5] * grad_z
    flux_y = coeffs[4] * grad_x + coeffs[2] * grad_y + coeffs[6] * grad_z
    flux_z = coeffs[5] * grad_x + coeffs[6] * grad_y + coeffs[3] * grad_z
    mass_term = coeffs[0] * point_value
    back_plain = apply_table(values.T, mass_term, 2) + apply_table(slopes.T, flux_z, 2)
    back_fluxx = apply_table(values.T, flux_x, 2)
    back_fluxy = apply_table(values.T, flux_y, 2)
    near_sum = apply_table(values.T, back_plain, 1) + apply_table(slopes.T, back_fluxy, 1)
    far_sum = apply_table(values.T, back_fluxx, 1)
    return apply_table(values.T, near_sum, 0) + apply_table(slopes.T, far_sum, 0)


def diagonal_action(pointwise):
    table_pair = gauss_tables()
    values = jnp.asarray(table_pair[0], jnp.float32)
    slopes = jnp.asarray(table_pair[1], jnp.float32)
    coeffs = pointwise.astype(jnp.float32)
    square_v = values * values
    square_s = slopes * slopes
    mixed_vs = values * slopes

    def triple(table_x, table_y, table_z, term):
        return apply_table(table_x.T, apply_table(table_y.T, apply_table(table_z.T, term, 2), 1), 0)

    running_total = triple(square_v, square_v, square_v, coeffs[0])
    running_total = running_total + triple(square_s, square_v, square_v, coeffs[1])
    running_total = running_total + triple(square_v, square_s, square_v, coeffs[2])
    running_total = running_total + triple(square_v, square_v, square_s, coeffs[3])
    running_total = running_total + 2.0 * triple(mixed_vs, mixed_vs, square_v, coeffs[4])
    running_total = running_total + 2.0 * triple(mixed_vs, square_v, mixed_vs, coeffs[5])
    running_total = running_total + 2.0 * triple(square_v, mixed_vs, mixed_vs, coeffs[6])
    return running_total


def to_dofs(parts):
    return merge_axis(merge_axis(merge_axis(parts, 5, 2), 3, 1), 1, 0)


def element_block(dof_block, pointwise):
    elements = split_axis(split_axis(split_axis(dof_block, 0, 0), 2, 1), 4, 2)
    return to_dofs(element_action(elements, pointwise))


def banded(table, count):
    band = np.zeros((3 * count + 1, 4, count))
    for index in range(count):
        band[3 * index : 3 * index + 4, :, index] = table.T
    return band


def planar(table_x, table_y, count_x, count_y):
    kron = np.einsum("xpi,yqj->piqjxy", banded(table_x, count_x), banded(table_y, count_y))
    return jnp.asarray(kron.reshape(16 * count_x * count_y, -1), jnp.float32)


def long_axis(table, count, anchor):
    shape = (3 * count + 1, 4, count)
    offset = lax.broadcasted_iota(jnp.int32, shape, 0) - 3 * lax.broadcasted_iota(jnp.int32, shape, 2)
    offset = offset + anchor
    band = jnp.zeros(shape, jnp.float32)
    for node in range(4):
        column = jnp.asarray(table[:, node], jnp.float32)[None, :, None]
        band = band + jnp.where(offset == node, column, 0.0)
    return band.reshape(3 * count + 1, 4 * count)


def mat(left, right, precision=lax.Precision.HIGHEST):
    return jnp.matmul(left, right, precision=precision)


def point_layout(pointwise):
    count_x, count_y, count_z = pointwise.shape[4:]
    coeffs = pointwise.astype(jnp.float32).transpose(0, 1, 4, 2, 5, 3, 6)
    return coeffs.reshape(7, 16 * count_x * count_y, 4 * count_z)


def band_operator(field, coeffs, counts, anchor):
    count_x, count_y, count_z = counts
    values, slopes = gauss_tables()
    plain = planar(values, values, count_x, count_y)
    along_x = planar(slopes, values, count_x, count_y)
    along_y = planar(values, slopes, count_x, count_y)
    z_tables = jnp.concatenate([long_axis(values, count_z, anchor), long_axis(slopes, count_z, anchor)], 1)
    rows = field.shape[0] * field.shape[1]
    width = 4 * count_z
    through_z = mat(field.reshape(rows, field.shape[2]), z_tables)
    z_value = through_z[:, :width]
    point_value = mat(plain, z_value)
    grad_x = mat(along_x, z_value)
    grad_y = mat(along_y, z_value)
    grad_z = mat(plain, through_z[:, width:])
    flux_x = coeffs[1] * grad_x + coeffs[4] * grad_y + coeffs[5] * grad_z
    flux_y = coeffs[4] * grad_x + coeffs[2] * grad_y + coeffs[6] * grad_z
    flux_z = coeffs[5] * grad_x + coeffs[6] * grad_y + coeffs[3] * grad_z
    mass_term = coeffs[0] * point_value
    backward = jnp.concatenate([plain, along_x, along_y], 0).T
    near = mat(backward, jnp.concatenate([mass_term, flux_x, flux_y], 0))
    far = mat(plain.T, flux_z)
    merged = mat(jnp.concatenate([near, far], 1), z_tables.T)
    return merged.reshape(field.shape)


def band_diagonal(coeffs, counts, anchor):
    count_x, count_y, count_z = counts
    values, slopes = gauss_tables()
    square_v = values * values
    square_s = slopes * slopes
    mixed = values * slopes
    groups = [
        (square_v, [(square_v, square_v, 0, 1.0), (square_s, square_v, 1, 1.0),
                    (square_v, square_s, 2, 1.0), (mixed, mixed, 4, 2.0)]),
        (square_s, [(square_v, square_v, 3, 1.0)]),
        (mixed, [(mixed, square_v, 5, 2.0), (square_v, mixed, 6, 2.0)]),
    ]
    total = 0.0
    for z_table, members in groups:
        inner = 0.0
        for table_x, table_y, entry, factor in members:
            inner = inner + mat(
                factor * planar(table_x, table_y, count_x, count_y).T, coeffs[entry], lax.Precision.HIGH
            )
        total = total + mat(inner, long_axis(z_table, count_z, anchor).T, lax.Precision.HIGH)
    return total.reshape(3 * count_x + 1, 3 * count_y + 1, 3 * count_z + 1)


def upper_x(plane):
    return shifted(plane, BX, -1)


def upper_y(plane):
    return shifted(plane, BY, -1)


def lower_x(plane):
    return shifted(plane, BX, 1)


def lower_y(plane):
    return shifted(plane, BY, 1)


def global_sums(terms):
    return (over_axes(terms[0], BX_BY), over_axes(terms[1], BX_BY))


def widen(dof_field):
    widened = jnp.concatenate([dof_field, upper_x(dof_field[0:1])], 0)
    widened = jnp.concatenate([widened, upper_y(widened[:, 0:1])], 1)
    return widened


def pad_top(dof_field):
    return jnp.pad(dof_field, ((0, 0), (0, 0), (0, 1)))


def collect(contributions, rows_x, rows_y, rows_z):
    summed = contributions[:, :, :rows_z]
    arrived = lower_y(summed[:, rows_y:])
    summed = jnp.concatenate([summed[:, 0:1] + arrived, summed[:, 1:rows_y]], 1)
    arrived = lower_x(summed[rows_x:])
    summed = jnp.concatenate([summed[0:1] + arrived, summed[1:rows_x]], 0)
    return summed


def shards(cotangent, pointwise):
    rows_x, rows_y, rows_z = cotangent.shape
    total_x = rows_x * lax.axis_size(BX)
    total_y = rows_y * lax.axis_size(BY)
    extent = cotangent.shape
    place_x = lax.broadcasted_iota(jnp.int32, extent, 0) + lax.axis_index(BX) * rows_x
    place_y = lax.broadcasted_iota(jnp.int32, extent, 1) + lax.axis_index(BY) * rows_y
    place_z = lax.broadcasted_iota(jnp.int32, extent, 2)
    inside = (
        (place_x > 0) & (place_y > 0) & (place_z > 0) & (place_x < total_x) & (place_y < total_y)
    )
    interior = jnp.where(inside, 1.0, 0.0).astype(jnp.float32)
    counts = pointwise.shape[4:]
    coeffs = point_layout(pointwise)
    anchor = (cotangent[0, 0, 0] * 0.0).astype(jnp.int32)
    diagonal = collect(band_diagonal(coeffs, counts, anchor), rows_x, rows_y, rows_z)

    wide_extent = (rows_x + 1, rows_y + 1, rows_z)
    wide_x = lax.broadcasted_iota(jnp.int32, wide_extent, 0) + lax.axis_index(BX) * rows_x
    wide_y = lax.broadcasted_iota(jnp.int32, wide_extent, 1) + lax.axis_index(BY) * rows_y
    wide_z = lax.broadcasted_iota(jnp.int32, wide_extent, 2)
    wide_inside = (
        (wide_x > 0) & (wide_y > 0) & (wide_z > 0) & (wide_x < total_x) & (wide_y < total_y)
    )
    wide_interior = jnp.where(wide_inside, 1.0, 0.0).astype(jnp.float32)

    def contributions(wide_field):
        return band_operator(pad_top(wide_field), coeffs, counts, anchor)[:, :, :rows_z]

    def local_dot(left, right):
        return jnp.sum(left * right)

    residual = cotangent * interior
    precond = residual / diagonal
    wide_precond = widen(precond)
    image = collect(contributions(wide_precond), rows_x, rows_y, rows_z) * interior
    scaled = image / diagonal
    wide_scaled = widen(scaled)
    raw_second = contributions(wide_scaled)
    masked_second = raw_second * wide_interior
    products = jnp.stack(
        [residual * precond, precond * image, residual * scaled, image * scaled]
    )
    wide_products = jnp.stack([wide_precond * masked_second, wide_scaled * masked_second])
    terms = jnp.concatenate(
        [
            jnp.sum(products.reshape(4, -1, products.shape[-1]), axis=(1, 2)),
            jnp.sum(wide_products.reshape(2, -1, wide_products.shape[-1]), axis=(1, 2)),
        ]
    )
    arrived = lower_x(raw_second[rows_x:])
    partial = jnp.concatenate([raw_second[0:1] + arrived, raw_second[1:rows_x]], 0)
    summed = lax.psum(terms, BX_BY[0])
    summed, partial = lax.optimization_barrier((summed, partial))
    arrived = lower_y(partial[:, rows_y:])
    second = jnp.concatenate([partial[:, 0:1] + arrived, partial[:, 1:rows_y]], 1) * interior
    summed = lax.psum(summed, BX_BY[1])
    summed, second = lax.optimization_barrier((summed, second))
    for axis in BX_BY[2:]:
        summed = lax.psum(summed, axis)
    parts = lax.optimization_barrier(jnp.broadcast_to(summed[:, None, None, None], (6, 1, 1, rows_z)))
    rz_now, curvature, cross_r, cross_q, cross_z, curvature_w = [parts[k] for k in range(6)]
    alpha = rz_now / curvature
    fresh = rz_now - alpha * cross_r - alpha * curvature + alpha * alpha * cross_q
    ratio = fresh / rz_now
    grow = 1.0 + ratio
    next_curvature = (
        grow * grow * curvature - alpha * grow * (cross_z + cross_q) + alpha * alpha * curvature_w
    )
    next_alpha = fresh / next_curvature
    residual = residual - alpha * image
    direction = residual / diagonal + ratio * precond
    direction_image = image - alpha * second + ratio * image
    adjoint = alpha * precond + next_alpha * direction
    residual = residual - next_alpha * direction_image
    return (adjoint, residual)


def solution(mesh):
    split = Mesh(mesh.devices.reshape(4, 3, 4, 8, 2), ("bx_0", "bx_1", "by_0", "by_1", "by_2"))
    in_specs = (P(BX, BY, None), P(None, None, None, None, BX, BY, None))
    out_specs = (P(BX, BY, None), P(BX, BY, None))
    return jax.shard_map(
        shards, mesh=split, in_specs=in_specs, out_specs=out_specs, check_vma=False
    )
```

```python
import math

import jax
import jax.numpy as jnp
import numpy as np
from jax import lax
from jax.sharding import Mesh
from jax.sharding import PartitionSpec as P

ITERS = 2
BX = ("bx_0", "bx_1")
BY = ("by_0", "by_1", "by_2")
BX_BY = ("bx_0", "bx_1", "by_0", "by_1", "by_2")


EINSUM_FORMS = ("pa,abcxyz->pbcxyz", "pb,abcxyz->apcxyz", "pc,abcxyz->abpxyz")


def shifted(value, axis, steps):
    count = lax.axis_size(axis)
    initial, last = (max(0, -steps), min(count, count - steps))
    return lax.ppermute(value, axis, [(source, source + steps) for source in range(initial, last)])


def over_axes(value, axes):
    for axis in axes:
        value = lax.psum(value, axis)
    return value


def gauss_tables():
    inner_point = math.sqrt(3.0 / 7.0 - 2.0 / 7.0 * math.sqrt(6.0 / 5.0))
    outer_point = math.sqrt(3.0 / 7.0 + 2.0 / 7.0 * math.sqrt(6.0 / 5.0))
    points = [-outer_point, -inner_point, inner_point, outer_point]
    lobatto = [-1.0, -1.0 / math.sqrt(5.0), 1.0 / math.sqrt(5.0), 1.0]
    values = np.zeros((4, 4))
    slopes = np.zeros((4, 4))
    for a in range(4):
        others = [lobatto[k] for k in range(4) if k != a]
        scaling = (lobatto[a] - others[0]) * (lobatto[a] - others[1]) * (lobatto[a] - others[2])
        for q in range(4):
            sample = points[q]
            values[q, a] = (
                (sample - others[0]) * (sample - others[1]) * (sample - others[2]) / scaling
            )
            slopes[q, a] = (
                (sample - others[1]) * (sample - others[2])
                + (sample - others[0]) * (sample - others[2])
                + (sample - others[0]) * (sample - others[1])
            ) / scaling
    return (values, slopes)


def apply_table(weights_1d, operand, stack_pos):
    return jnp.einsum(EINSUM_FORMS[stack_pos], weights_1d, operand, precision=lax.Precision.HIGHEST)


def split_axis(dof_field, axis_pos, stack_pos):
    elem_count = (dof_field.shape[axis_pos] - 1) // 3
    widths = [(0, 0)] * dof_field.ndim
    widths[axis_pos] = (0, 2)
    padded = jnp.pad(dof_field, widths)
    shaped = padded.reshape(
        dof_field.shape[:axis_pos] + (elem_count + 1, 3) + dof_field.shape[axis_pos + 1 :]
    )
    lower_rows = lax.slice_in_dim(shaped, 0, elem_count, axis=axis_pos)
    upper_rows = lax.slice_in_dim(shaped, 1, elem_count + 1, axis=axis_pos)
    pieces = [lax.index_in_dim(lower_rows, k, axis_pos + 1, keepdims=False) for k in range(3)]
    pieces.append(lax.index_in_dim(upper_rows, 0, axis_pos + 1, keepdims=False))
    return jnp.stack(pieces, stack_pos)


def merge_axis(parts, axis_pos, stack_pos):
    pieces = [lax.index_in_dim(parts, k, stack_pos, keepdims=False) for k in range(4)]
    target = axis_pos - 1
    extent = pieces[0].shape
    elem_count = extent[target]
    ending = [(0, 0)] * len(extent)
    ending[target] = (0, 1)
    leading = [(0, 0)] * len(extent)
    leading[target] = (1, 0)
    head_piece = jnp.pad(pieces[0], ending) + jnp.pad(pieces[3], leading)
    stacked = jnp.stack(
        [head_piece, jnp.pad(pieces[1], ending), jnp.pad(pieces[2], ending)], target + 1
    )
    merged = stacked.reshape(extent[:target] + (3 * (elem_count + 1),) + extent[target + 1 :])
    return lax.slice_in_dim(merged, 0, 3 * elem_count + 1, axis=target)


def element_action(elements, pointwise):
    table_pair = gauss_tables()
    values = jnp.asarray(table_pair[0], jnp.float32)
    slopes = jnp.asarray(table_pair[1], jnp.float32)
    coeffs = pointwise.astype(jnp.float32)
    x_value = apply_table(values, elements, 0)
    x_slope = apply_table(slopes, elements, 0)
    value_value = apply_table(values, x_value, 1)
    value_slope = apply_table(slopes, x_value, 1)
    slope_value = apply_table(values, x_slope, 1)
    point_value = apply_table(values, value_value, 2)
    grad_z = apply_table(slopes, value_value, 2)
    grad_y = apply_table(values, value_slope, 2)
    grad_x = apply_table(values, slope_value, 2)
    flux_x = coeffs[1] * grad_x + coeffs[4] * grad_y + coeffs[5] * grad_z
    flux_y = coeffs[4] * grad_x + coeffs[2] * grad_y + coeffs[6] * grad_z
    flux_z = coeffs[5] * grad_x + coeffs[6] * grad_y + coeffs[3] * grad_z
    mass_term = coeffs[0] * point_value
    back_plain = apply_table(values.T, mass_term, 2) + apply_table(slopes.T, flux_z, 2)
    back_fluxx = apply_table(values.T, flux_x, 2)
    back_fluxy = apply_table(values.T, flux_y, 2)
    near_sum = apply_table(values.T, back_plain, 1) + apply_table(slopes.T, back_fluxy, 1)
    far_sum = apply_table(values.T, back_fluxx, 1)
    return apply_table(values.T, near_sum, 0) + apply_table(slopes.T, far_sum, 0)


def diagonal_action(pointwise):
    table_pair = gauss_tables()
    values = jnp.asarray(table_pair[0], jnp.float32)
    slopes = jnp.asarray(table_pair[1], jnp.float32)
    coeffs = pointwise.astype(jnp.float32)
    square_v = values * values
    square_s = slopes * slopes
    mixed_vs = values * slopes

    def triple(table_x, table_y, table_z, term):
        return apply_table(table_x.T, apply_table(table_y.T, apply_table(table_z.T, term, 2), 1), 0)

    running_total = triple(square_v, square_v, square_v, coeffs[0])
    running_total = running_total + triple(square_s, square_v, square_v, coeffs[1])
    running_total = running_total + triple(square_v, square_s, square_v, coeffs[2])
    running_total = running_total + triple(square_v, square_v, square_s, coeffs[3])
    running_total = running_total + 2.0 * triple(mixed_vs, mixed_vs, square_v, coeffs[4])
    running_total = running_total + 2.0 * triple(mixed_vs, square_v, mixed_vs, coeffs[5])
    running_total = running_total + 2.0 * triple(square_v, mixed_vs, mixed_vs, coeffs[6])
    return running_total


def to_dofs(parts):
    return merge_axis(merge_axis(merge_axis(parts, 5, 2), 3, 1), 1, 0)


def element_block(dof_block, pointwise):
    elements = split_axis(split_axis(split_axis(dof_block, 0, 0), 2, 1), 4, 2)
    return to_dofs(element_action(elements, pointwise))


def banded(table, count):
    band = np.zeros((3 * count + 1, 4, count))
    for index in range(count):
        band[3 * index : 3 * index + 4, :, index] = table.T
    return band


def planar(table_x, table_y, count_x, count_y):
    kron = np.einsum("xpi,yqj->piqjxy", banded(table_x, count_x), banded(table_y, count_y))
    return jnp.asarray(kron.reshape(16 * count_x * count_y, -1), jnp.float32)


def long_axis(table, count, anchor):
    shape = (3 * count + 1, 4, count)
    offset = lax.broadcasted_iota(jnp.int32, shape, 0) - 3 * lax.broadcasted_iota(jnp.int32, shape, 2)
    offset = offset + anchor
    band = jnp.zeros(shape, jnp.float32)
    for node in range(4):
        column = jnp.asarray(table[:, node], jnp.float32)[None, :, None]
        band = band + jnp.where(offset == node, column, 0.0)
    return band.reshape(3 * count + 1, 4 * count)


def mat(left, right):
    return jnp.matmul(left, right, precision=lax.Precision.HIGHEST)


def point_layout(pointwise):
    count_x, count_y, count_z = pointwise.shape[4:]
    coeffs = pointwise.astype(jnp.float32).transpose(0, 1, 4, 2, 5, 3, 6)
    return coeffs.reshape(7, 16 * count_x * count_y, 4 * count_z)


def band_operator(field, coeffs, counts, anchor):
    count_x, count_y, count_z = counts
    values, slopes = gauss_tables()
    plain = planar(values, values, count_x, count_y)
    along_x = planar(slopes, values, count_x, count_y)
    along_y = planar(values, slopes, count_x, count_y)
    z_tables = jnp.concatenate([long_axis(values, count_z, anchor), long_axis(slopes, count_z, anchor)], 1)
    rows = field.shape[0] * field.shape[1]
    width = 4 * count_z
    through_z = mat(field.reshape(rows, field.shape[2]), z_tables)
    z_value = through_z[:, :width]
    planes = plain.shape[0]
    stacked = mat(jnp.concatenate([plain, along_x, along_y], 0), z_value)
    point_value = stacked[:planes]
    grad_x = stacked[planes : 2 * planes]
    grad_y = stacked[2 * planes :]
    grad_z = mat(plain, through_z[:, width:])
    flux_x = coeffs[1] * grad_x + coeffs[4] * grad_y + coeffs[5] * grad_z
    flux_y = coeffs[4] * grad_x + coeffs[2] * grad_y + coeffs[6] * grad_z
    flux_z = coeffs[5] * grad_x + coeffs[6] * grad_y + coeffs[3] * grad_z
    mass_term = coeffs[0] * point_value
    backward = jnp.concatenate([plain, along_x, along_y], 0).T
    near = mat(backward, jnp.concatenate([mass_term, flux_x, flux_y], 0))
    far = mat(plain.T, flux_z)
    merged = mat(jnp.concatenate([near, far], 1), z_tables.T)
    return merged.reshape(field.shape)


def band_diagonal(coeffs, counts, anchor):
    count_x, count_y, count_z = counts
    values, slopes = gauss_tables()
    square_v = values * values
    square_s = slopes * slopes
    mixed = values * slopes
    groups = [
        (square_v, [(square_v, square_v, 0, 1.0), (square_s, square_v, 1, 1.0),
                    (square_v, square_s, 2, 1.0), (mixed, mixed, 4, 2.0)]),
        (square_s, [(square_v, square_v, 3, 1.0)]),
        (mixed, [(mixed, square_v, 5, 2.0), (square_v, mixed, 6, 2.0)]),
    ]
    inners = []
    bands = []
    for z_table, members in groups:
        inner = 0.0
        for table_x, table_y, entry, factor in members:
            inner = inner + mat(factor * planar(table_x, table_y, count_x, count_y).T, coeffs[entry])
        inners.append(inner)
        bands.append(long_axis(z_table, count_z, anchor).T)
    total = mat(jnp.concatenate(inners, 1), jnp.concatenate(bands, 0))
    return total.reshape(3 * count_x + 1, 3 * count_y + 1, 3 * count_z + 1)


def upper_x(plane):
    return shifted(plane, BX, -1)


def upper_y(plane):
    return shifted(plane, BY, -1)


def lower_x(plane):
    return shifted(plane, BX, 1)


def lower_y(plane):
    return shifted(plane, BY, 1)


def global_sums(terms):
    return (over_axes(terms[0], BX_BY), over_axes(terms[1], BX_BY))


def widen(dof_field):
    widened = jnp.concatenate([dof_field, upper_x(dof_field[0:1])], 0)
    widened = jnp.concatenate([widened, upper_y(widened[:, 0:1])], 1)
    return widened


def pad_top(dof_field):
    return jnp.pad(dof_field, ((0, 0), (0, 0), (0, 1)))


def collect(contributions, rows_x, rows_y, rows_z):
    summed = contributions[:, :, :rows_z]
    arrived = lower_y(summed[:, rows_y:])
    summed = jnp.concatenate([summed[:, 0:1] + arrived, summed[:, 1:rows_y]], 1)
    arrived = lower_x(summed[rows_x:])
    summed = jnp.concatenate([summed[0:1] + arrived, summed[1:rows_x]], 0)
    return summed


def shards(cotangent, pointwise):
    rows_x, rows_y, rows_z = cotangent.shape
    total_x = rows_x * lax.axis_size(BX)
    total_y = rows_y * lax.axis_size(BY)
    extent = cotangent.shape
    place_x = lax.broadcasted_iota(jnp.int32, extent, 0) + lax.axis_index(BX) * rows_x
    place_y = lax.broadcasted_iota(jnp.int32, extent, 1) + lax.axis_index(BY) * rows_y
    place_z = lax.broadcasted_iota(jnp.int32, extent, 2)
    inside = (
        (place_x > 0) & (place_y > 0) & (place_z > 0) & (place_x < total_x) & (place_y < total_y)
    )
    interior = jnp.where(inside, 1.0, 0.0).astype(jnp.float32)
    counts = pointwise.shape[4:]
    coeffs = point_layout(pointwise)
    anchor = (cotangent[0, 0, 0] * 0.0).astype(jnp.int32)
    diagonal = collect(band_diagonal(coeffs, counts, anchor), rows_x, rows_y, rows_z)

    wide_extent = (rows_x + 1, rows_y + 1, rows_z)
    wide_x = lax.broadcasted_iota(jnp.int32, wide_extent, 0) + lax.axis_index(BX) * rows_x
    wide_y = lax.broadcasted_iota(jnp.int32, wide_extent, 1) + lax.axis_index(BY) * rows_y
    wide_z = lax.broadcasted_iota(jnp.int32, wide_extent, 2)
    wide_inside = (
        (wide_x > 0) & (wide_y > 0) & (wide_z > 0) & (wide_x < total_x) & (wide_y < total_y)
    )
    wide_interior = jnp.where(wide_inside, 1.0, 0.0).astype(jnp.float32)

    def contributions(wide_field):
        return band_operator(pad_top(wide_field), coeffs, counts, anchor)[:, :, :rows_z]

    def local_dot(left, right):
        return jnp.sum(left * right)

    residual = cotangent * interior
    precond = residual / diagonal
    wide_precond = widen(precond)
    image = collect(contributions(wide_precond), rows_x, rows_y, rows_z) * interior
    scaled = image / diagonal
    wide_scaled = widen(scaled)
    raw_second = contributions(wide_scaled)
    masked_second = raw_second * wide_interior
    products = jnp.stack(
        [residual * precond, precond * image, residual * scaled, image * scaled]
    )
    wide_products = jnp.stack([wide_precond * masked_second, wide_scaled * masked_second])
    terms = jnp.concatenate(
        [
            jnp.sum(products.reshape(4, -1, products.shape[-1]), axis=(1, 2)),
            jnp.sum(wide_products.reshape(2, -1, wide_products.shape[-1]), axis=(1, 2)),
        ]
    )
    arrived = lower_x(raw_second[rows_x:])
    partial = jnp.concatenate([raw_second[0:1] + arrived, raw_second[1:rows_x]], 0)
    summed = lax.psum(terms, BX_BY[0])
    summed, partial = lax.optimization_barrier((summed, partial))
    arrived = lower_y(partial[:, rows_y:])
    second = jnp.concatenate([partial[:, 0:1] + arrived, partial[:, 1:rows_y]], 1) * interior
    summed = lax.psum(summed, BX_BY[1])
    summed, second = lax.optimization_barrier((summed, second))
    for axis in BX_BY[2:]:
        summed = lax.psum(summed, axis)
    parts = lax.optimization_barrier(jnp.broadcast_to(summed[:, None, None, None], (6, 1, 1, rows_z)))
    rz_now, curvature, cross_r, cross_q, cross_z, curvature_w = [parts[k] for k in range(6)]
    alpha = rz_now / curvature
    fresh = rz_now - alpha * cross_r - alpha * curvature + alpha * alpha * cross_q
    ratio = fresh / rz_now
    grow = 1.0 + ratio
    next_curvature = (
        grow * grow * curvature - alpha * grow * (cross_z + cross_q) + alpha * alpha * curvature_w
    )
    next_alpha = fresh / next_curvature
    residual = residual - alpha * image
    direction = residual / diagonal + ratio * precond
    direction_image = image - alpha * second + ratio * image
    adjoint = alpha * precond + next_alpha * direction
    residual = residual - next_alpha * direction_image
    return (adjoint, residual)


def solution(mesh):
    split = Mesh(mesh.devices.reshape(4, 3, 4, 8, 2), ("bx_0", "bx_1", "by_0", "by_1", "by_2"))
    in_specs = (P(BX, BY, None), P(None, None, None, None, BX, BY, None))
    out_specs = (P(BX, BY, None), P(BX, BY, None))
    return jax.shard_map(
        shards, mesh=split, in_specs=in_specs, out_specs=out_specs, check_vma=False
    )
```

```python
import math

import jax
import jax.numpy as jnp
import numpy as np
from jax import lax
from jax.sharding import Mesh
from jax.sharding import PartitionSpec as P

ITERS = 2
BX = ("bx_0", "bx_1")
BY = ("by_0", "by_1", "by_2")
BX_BY = ("bx_0", "bx_1", "by_0", "by_1", "by_2")


EINSUM_FORMS = ("pa,abcxyz->pbcxyz", "pb,abcxyz->apcxyz", "pc,abcxyz->abpxyz")


def shifted(value, axis, steps):
    count = lax.axis_size(axis)
    initial, last = (max(0, -steps), min(count, count - steps))
    return lax.ppermute(value, axis, [(source, source + steps) for source in range(initial, last)])


def over_axes(value, axes):
    for axis in axes:
        value = lax.psum(value, axis)
    return value


def gauss_tables():
    inner_point = math.sqrt(3.0 / 7.0 - 2.0 / 7.0 * math.sqrt(6.0 / 5.0))
    outer_point = math.sqrt(3.0 / 7.0 + 2.0 / 7.0 * math.sqrt(6.0 / 5.0))
    points = [-outer_point, -inner_point, inner_point, outer_point]
    lobatto = [-1.0, -1.0 / math.sqrt(5.0), 1.0 / math.sqrt(5.0), 1.0]
    values = np.zeros((4, 4))
    slopes = np.zeros((4, 4))
    for a in range(4):
        others = [lobatto[k] for k in range(4) if k != a]
        scaling = (lobatto[a] - others[0]) * (lobatto[a] - others[1]) * (lobatto[a] - others[2])
        for q in range(4):
            sample = points[q]
            values[q, a] = (
                (sample - others[0]) * (sample - others[1]) * (sample - others[2]) / scaling
            )
            slopes[q, a] = (
                (sample - others[1]) * (sample - others[2])
                + (sample - others[0]) * (sample - others[2])
                + (sample - others[0]) * (sample - others[1])
            ) / scaling
    return (values, slopes)


def apply_table(weights_1d, operand, stack_pos):
    return jnp.einsum(EINSUM_FORMS[stack_pos], weights_1d, operand, precision=lax.Precision.HIGHEST)


def split_axis(dof_field, axis_pos, stack_pos):
    elem_count = (dof_field.shape[axis_pos] - 1) // 3
    widths = [(0, 0)] * dof_field.ndim
    widths[axis_pos] = (0, 2)
    padded = jnp.pad(dof_field, widths)
    shaped = padded.reshape(
        dof_field.shape[:axis_pos] + (elem_count + 1, 3) + dof_field.shape[axis_pos + 1 :]
    )
    lower_rows = lax.slice_in_dim(shaped, 0, elem_count, axis=axis_pos)
    upper_rows = lax.slice_in_dim(shaped, 1, elem_count + 1, axis=axis_pos)
    pieces = [lax.index_in_dim(lower_rows, k, axis_pos + 1, keepdims=False) for k in range(3)]
    pieces.append(lax.index_in_dim(upper_rows, 0, axis_pos + 1, keepdims=False))
    return jnp.stack(pieces, stack_pos)


def merge_axis(parts, axis_pos, stack_pos):
    pieces = [lax.index_in_dim(parts, k, stack_pos, keepdims=False) for k in range(4)]
    target = axis_pos - 1
    extent = pieces[0].shape
    elem_count = extent[target]
    ending = [(0, 0)] * len(extent)
    ending[target] = (0, 1)
    leading = [(0, 0)] * len(extent)
    leading[target] = (1, 0)
    head_piece = jnp.pad(pieces[0], ending) + jnp.pad(pieces[3], leading)
    stacked = jnp.stack(
        [head_piece, jnp.pad(pieces[1], ending), jnp.pad(pieces[2], ending)], target + 1
    )
    merged = stacked.reshape(extent[:target] + (3 * (elem_count + 1),) + extent[target + 1 :])
    return lax.slice_in_dim(merged, 0, 3 * elem_count + 1, axis=target)


def element_action(elements, pointwise):
    table_pair = gauss_tables()
    values = jnp.asarray(table_pair[0], jnp.float32)
    slopes = jnp.asarray(table_pair[1], jnp.float32)
    coeffs = pointwise.astype(jnp.float32)
    x_value = apply_table(values, elements, 0)
    x_slope = apply_table(slopes, elements, 0)
    value_value = apply_table(values, x_value, 1)
    value_slope = apply_table(slopes, x_value, 1)
    slope_value = apply_table(values, x_slope, 1)
    point_value = apply_table(values, value_value, 2)
    grad_z = apply_table(slopes, value_value, 2)
    grad_y = apply_table(values, value_slope, 2)
    grad_x = apply_table(values, slope_value, 2)
    flux_x = coeffs[1] * grad_x + coeffs[4] * grad_y + coeffs[5] * grad_z
    flux_y = coeffs[4] * grad_x + coeffs[2] * grad_y + coeffs[6] * grad_z
    flux_z = coeffs[5] * grad_x + coeffs[6] * grad_y + coeffs[3] * grad_z
    mass_term = coeffs[0] * point_value
    back_plain = apply_table(values.T, mass_term, 2) + apply_table(slopes.T, flux_z, 2)
    back_fluxx = apply_table(values.T, flux_x, 2)
    back_fluxy = apply_table(values.T, flux_y, 2)
    near_sum = apply_table(values.T, back_plain, 1) + apply_table(slopes.T, back_fluxy, 1)
    far_sum = apply_table(values.T, back_fluxx, 1)
    return apply_table(values.T, near_sum, 0) + apply_table(slopes.T, far_sum, 0)


def diagonal_action(pointwise):
    table_pair = gauss_tables()
    values = jnp.asarray(table_pair[0], jnp.float32)
    slopes = jnp.asarray(table_pair[1], jnp.float32)
    coeffs = pointwise.astype(jnp.float32)
    square_v = values * values
    square_s = slopes * slopes
    mixed_vs = values * slopes

    def triple(table_x, table_y, table_z, term):
        return apply_table(table_x.T, apply_table(table_y.T, apply_table(table_z.T, term, 2), 1), 0)

    running_total = triple(square_v, square_v, square_v, coeffs[0])
    running_total = running_total + triple(square_s, square_v, square_v, coeffs[1])
    running_total = running_total + triple(square_v, square_s, square_v, coeffs[2])
    running_total = running_total + triple(square_v, square_v, square_s, coeffs[3])
    running_total = running_total + 2.0 * triple(mixed_vs, mixed_vs, square_v, coeffs[4])
    running_total = running_total + 2.0 * triple(mixed_vs, square_v, mixed_vs, coeffs[5])
    running_total = running_total + 2.0 * triple(square_v, mixed_vs, mixed_vs, coeffs[6])
    return running_total


def to_dofs(parts):
    return merge_axis(merge_axis(merge_axis(parts, 5, 2), 3, 1), 1, 0)


def element_block(dof_block, pointwise):
    elements = split_axis(split_axis(split_axis(dof_block, 0, 0), 2, 1), 4, 2)
    return to_dofs(element_action(elements, pointwise))


def banded(table, count):
    band = np.zeros((3 * count + 1, 4, count))
    for index in range(count):
        band[3 * index : 3 * index + 4, :, index] = table.T
    return band


def planar(table_x, table_y, count_x, count_y):
    kron = np.einsum("xpi,yqj->piqjxy", banded(table_x, count_x), banded(table_y, count_y))
    return jnp.asarray(kron.reshape(16 * count_x * count_y, -1), jnp.float32)


def long_axis(table, count, anchor):
    shape = (3 * count + 1, 4, count)
    offset = lax.broadcasted_iota(jnp.int32, shape, 0) - 3 * lax.broadcasted_iota(jnp.int32, shape, 2)
    offset = offset + anchor
    band = jnp.zeros(shape, jnp.float32)
    for node in range(4):
        column = jnp.asarray(table[:, node], jnp.float32)[None, :, None]
        band = band + jnp.where(offset == node, column, 0.0)
    return band.reshape(3 * count + 1, 4 * count)


def mat(left, right):
    return jnp.matmul(left, right, precision=lax.Precision.HIGHEST)


def point_layout(pointwise):
    count_x, count_y, count_z = pointwise.shape[4:]
    coeffs = pointwise.astype(jnp.float32).transpose(0, 1, 4, 2, 5, 3, 6)
    return coeffs.reshape(7, 16 * count_x * count_y, 4 * count_z)


def band_operator(field, coeffs, counts, anchor):
    count_x, count_y, count_z = counts
    values, slopes = gauss_tables()
    plain = planar(values, values, count_x, count_y)
    along_x = planar(slopes, values, count_x, count_y)
    along_y = planar(values, slopes, count_x, count_y)
    z_tables = jnp.concatenate([long_axis(values, count_z, anchor), long_axis(slopes, count_z, anchor)], 1)
    rows = field.shape[0] * field.shape[1]
    width = 4 * count_z
    through_z = mat(field.reshape(rows, field.shape[2]), z_tables)
    z_value = through_z[:, :width]
    planes = plain.shape[0]
    stacked = mat(jnp.concatenate([plain, along_x, along_y], 0), z_value)
    point_value = stacked[:planes]
    grad_x = stacked[planes : 2 * planes]
    grad_y = stacked[2 * planes :]
    grad_z = mat(plain, through_z[:, width:])
    flux_x = coeffs[1] * grad_x + coeffs[4] * grad_y + coeffs[5] * grad_z
    flux_y = coeffs[4] * grad_x + coeffs[2] * grad_y + coeffs[6] * grad_z
    flux_z = coeffs[5] * grad_x + coeffs[6] * grad_y + coeffs[3] * grad_z
    mass_term = coeffs[0] * point_value
    backward = jnp.concatenate([plain, along_x, along_y], 0).T
    near = mat(backward, jnp.concatenate([mass_term, flux_x, flux_y], 0))
    far = mat(plain.T, flux_z)
    merged = mat(jnp.concatenate([near, far], 1), z_tables.T)
    return merged.reshape(field.shape)


def band_diagonal(coeffs, counts, anchor):
    count_x, count_y, count_z = counts
    values, slopes = gauss_tables()
    square_v = values * values
    square_s = slopes * slopes
    mixed = values * slopes
    groups = [
        (square_v, [(square_v, square_v, 0, 1.0), (square_s, square_v, 1, 1.0),
                    (square_v, square_s, 2, 1.0), (mixed, mixed, 4, 2.0)]),
        (square_s, [(square_v, square_v, 3, 1.0)]),
        (mixed, [(mixed, square_v, 5, 2.0), (square_v, mixed, 6, 2.0)]),
    ]
    inners = []
    bands = []
    for z_table, members in groups:
        inner = 0.0
        for table_x, table_y, entry, factor in members:
            inner = inner + mat(factor * planar(table_x, table_y, count_x, count_y).T, coeffs[entry])
        inners.append(inner)
        bands.append(long_axis(z_table, count_z, anchor).T)
    total = mat(jnp.concatenate(inners, 1), jnp.concatenate(bands, 0))
    return total.reshape(3 * count_x + 1, 3 * count_y + 1, 3 * count_z + 1)


def upper_x(plane):
    return shifted(plane, BX, -1)


def upper_y(plane):
    return shifted(plane, BY, -1)


def lower_x(plane):
    return shifted(plane, BX, 1)


def lower_y(plane):
    return shifted(plane, BY, 1)


def global_sums(terms):
    return (over_axes(terms[0], BX_BY), over_axes(terms[1], BX_BY))


def widen(dof_field):
    widened = jnp.concatenate([dof_field, upper_x(dof_field[0:1])], 0)
    widened = jnp.concatenate([widened, upper_y(widened[:, 0:1])], 1)
    return widened


def pad_top(dof_field):
    return jnp.pad(dof_field, ((0, 0), (0, 0), (0, 1)))


def collect(contributions, rows_x, rows_y, rows_z):
    summed = contributions[:, :, :rows_z]
    arrived = lower_y(summed[:, rows_y:])
    summed = jnp.concatenate([summed[:, 0:1] + arrived, summed[:, 1:rows_y]], 1)
    arrived = lower_x(summed[rows_x:])
    summed = jnp.concatenate([summed[0:1] + arrived, summed[1:rows_x]], 0)
    return summed


def shards(cotangent, pointwise):
    rows_x, rows_y, rows_z = cotangent.shape
    total_x = rows_x * lax.axis_size(BX)
    total_y = rows_y * lax.axis_size(BY)
    extent = cotangent.shape
    place_x = lax.broadcasted_iota(jnp.int32, extent, 0) + lax.axis_index(BX) * rows_x
    place_y = lax.broadcasted_iota(jnp.int32, extent, 1) + lax.axis_index(BY) * rows_y
    place_z = lax.broadcasted_iota(jnp.int32, extent, 2)
    inside = (
        (place_x > 0) & (place_y > 0) & (place_z > 0) & (place_x < total_x) & (place_y < total_y)
    )
    interior = jnp.where(inside, 1.0, 0.0).astype(jnp.float32)
    counts = pointwise.shape[4:]
    coeffs = point_layout(pointwise)
    anchor = (cotangent[0, 0, 0] * 0.0).astype(jnp.int32)
    diagonal = collect(band_diagonal(coeffs, counts, anchor), rows_x, rows_y, rows_z)

    wide_extent = (rows_x + 1, rows_y + 1, rows_z)
    wide_x = lax.broadcasted_iota(jnp.int32, wide_extent, 0) + lax.axis_index(BX) * rows_x
    wide_y = lax.broadcasted_iota(jnp.int32, wide_extent, 1) + lax.axis_index(BY) * rows_y
    wide_z = lax.broadcasted_iota(jnp.int32, wide_extent, 2)
    wide_inside = (
        (wide_x > 0) & (wide_y > 0) & (wide_z > 0) & (wide_x < total_x) & (wide_y < total_y)
    )
    wide_interior = jnp.where(wide_inside, 1.0, 0.0).astype(jnp.float32)

    def contributions(wide_field):
        return band_operator(pad_top(wide_field), coeffs, counts, anchor)[:, :, :rows_z]

    def local_dot(left, right):
        return jnp.sum(left * right)

    residual = cotangent * interior
    precond = residual / diagonal
    wide_precond = widen(precond)
    image = collect(contributions(wide_precond), rows_x, rows_y, rows_z) * interior
    scaled = image / diagonal
    wide_scaled = widen(scaled)
    raw_second = contributions(wide_scaled)
    masked_second = raw_second * wide_interior
    products = jnp.stack(
        [residual * precond, precond * image, residual * scaled, image * scaled]
    )
    wide_products = jnp.stack([wide_precond * masked_second, wide_scaled * masked_second])
    terms = jnp.concatenate(
        [
            jnp.sum(products.reshape(4, -1, products.shape[-1]), axis=(1, 2)),
            jnp.sum(wide_products.reshape(2, -1, wide_products.shape[-1]), axis=(1, 2)),
        ]
    )
    arrived = lower_x(raw_second[rows_x:])
    partial = jnp.concatenate([raw_second[0:1] + arrived, raw_second[1:rows_x]], 0)
    chain = ("bx_1", "by_1", "bx_0", "by_0", "by_2")
    summed = lax.psum(terms, chain[0])
    summed, partial = lax.optimization_barrier((summed, partial))
    arrived = lower_y(partial[:, rows_y:])
    second = jnp.concatenate([partial[:, 0:1] + arrived, partial[:, 1:rows_y]], 1) * interior
    summed = lax.psum(summed, chain[1])
    summed, second = lax.optimization_barrier((summed, second))
    for axis in chain[2:]:
        summed = lax.psum(summed, axis)
    parts = lax.optimization_barrier(jnp.broadcast_to(summed[:, None, None, None], (6, 1, 1, rows_z)))
    rz_now, curvature, cross_r, cross_q, cross_z, curvature_w = [parts[k] for k in range(6)]
    alpha = rz_now / curvature
    fresh = rz_now - alpha * cross_r - alpha * curvature + alpha * alpha * cross_q
    ratio = fresh / rz_now
    grow = 1.0 + ratio
    next_curvature = (
        grow * grow * curvature - alpha * grow * (cross_z + cross_q) + alpha * alpha * curvature_w
    )
    next_alpha = fresh / next_curvature
    residual = residual - alpha * image
    direction = residual / diagonal + ratio * precond
    direction_image = image - alpha * second + ratio * image
    adjoint = alpha * precond + next_alpha * direction
    residual = residual - next_alpha * direction_image
    return (adjoint, residual)


def solution(mesh):
    split = Mesh(mesh.devices.reshape(4, 3, 4, 8, 2), ("bx_0", "bx_1", "by_0", "by_1", "by_2"))
    in_specs = (P(BX, BY, None), P(None, None, None, None, BX, BY, None))
    out_specs = (P(BX, BY, None), P(BX, BY, None))
    return jax.shard_map(
        shards, mesh=split, in_specs=in_specs, out_specs=out_specs, check_vma=False
    )
```
